256 devices in a mesh: gx: 16 (over z, y_lo), gy: 16 (over x, y_hi, core).
Axes of the slice: x: 4, y: 4 (y_hi: 2, y_lo: 2; y = y_hi * 2 + y_lo), z: 8, core: 2. Of those that a mesh axis runs over, the one named last changes fastest.
Arguments:
- stored_slab: bfloat16 [2, 32, 128, 2048], P(None, None, 'gx', 'gy'), may hold values from -6 to 6
- block_scales: bfloat16 [2, 32, 16, 16], P(None, None, 'gx', 'gy'), may hold values from 0.5 to 2
- holder: int32 [16], replicated, may hold values from 0 to 15, each once
- soil_class: int32 [128, 2048], P('gx', 'gy'), may hold values from 0 to 11
- soil_table: float32 [12, 4], replicated, may hold values from 0.01 to 0.05
- cotangent: float32 [2, 32, 128, 2048], P(None, None, 'gx', 'gy'), may hold values from -6 to 6
Outputs:
- recomputed: float32 [2, 32, 128, 2048], P(None, None, 'gx', 'gy')
- sensitivity: float32 [2, 32, 128, 2048], P(None, None, 'gx', 'gy')
The draws below stay inside these ranges and needn't reach their ends.
Inputs may be any that keep to these rules, and one draw needn't show every extreme that they name: holder is a permutation: every gy index holds exactly one checkpoint block.
All inputs are finite; a program needn't handle non-finite values.
Results may differ from the reference program's by a relative error of at most 0.0003.
Values may be sent and summed in bfloat16 or wider, within the bound.
No kernel may reach another device: no remote copies, remote signals or barrier semaphores. Data moves between devices by JAX's collectives and lax.ppermute only.
A program may use at most 128 MiB of HBM per device.

```python
import math
import jax
import jax.numpy as jnp
from jax import lax

CX = 8
CY = 128
NZ = 32
NCLASS = 12
NX = 128
NY = 2048
N_GX = 16
N_GY = 16


def set_ends(entries, rng, smallest, high):
    spot = [jax.random.randint(jax.random.fold_in(rng, axis), (), 0, length) for axis, length in enumerate(entries.shape)]
    longest = entries.shape.index(max(entries.shape))
    beside = spot[:longest] + [(spot[longest] + 1) % entries.shape[longest]] + spot[longest + 1:]
    return entries.at[tuple(spot)].set(smallest).at[tuple(beside)].set(high)


def level_of(own_key, shape, shards, least, high):
    def one(position, blocks):
        heights = jax.random.uniform(jax.random.fold_in(jax.random.fold_in(own_key, 6), position), (blocks,), jnp.float32, least / len(shards), high / len(shards))
        return jnp.repeat(jnp.exp(heights), shape[position] // blocks).reshape((-1,) + (1,) * (len(shape) - position - 1))

    loudness = one(*shards[0])
    for cut in shards[1:]:
        loudness = loudness * one(*cut)
    return loudness


def scatter_about(own_key, shape, width, reach, pieces=(), kind=jnp.bfloat16):
    entries = jax.random.normal(own_key, shape, jnp.float32) * width
    if len(pieces) > 0:
        entries = level_of(own_key, shape, pieces, -0.22, 0.18) * entries
    return jnp.clip(entries, min=-reach, max=reach).astype(kind)


def setup_inputs(seed: int = 0) -> dict:
    keys = jax.random.split(jax.random.key(seed), 7)
    return {
        "stored_slab": scatter_about(keys[0], (2, NZ, NX, NY), 1.0, 6.0, ((2, 16), (3, 16))),
        "block_scales": jnp.clip(jnp.exp(math.log(2.0) - 1.3862944 * jax.random.uniform(keys[1], (2, NZ, N_GX, N_GY), jnp.float32) ** level_of(keys[1], (2, NZ, N_GX, N_GY), ((2, 16), (3, 16)), -0.2, 0.2)), 0.5, 2.0).astype(jnp.bfloat16),
        "holder": jax.random.permutation(keys[2], N_GY).astype(jnp.int32),
        "soil_class": set_ends(jax.random.randint(keys[3], (NX, NY), 0, NCLASS), jax.random.fold_in(keys[3], 1), 0, NCLASS - 1).astype(jnp.int32),
        "soil_table": jnp.clip(jnp.exp(jax.random.uniform(keys[4], (NCLASS, 4), jnp.float32, math.log(0.01), math.log(0.05))), 0.01, 0.05),
        "cotangent": scatter_about(keys[5], (2, NZ, NX, NY), 1.0, 6.0, ((2, 16), (3, 16)), jnp.float32),
    }


OFFSETS = ((1, 0, 0), (-1, 0, 0), (0, 1, 0), (0, -1, 0), (0, 0, 1), (0, 0, -1))

def shifted(block, offset):
    sz, sx, sy = block.shape
    return block[1 + offset[0]:sz - 1 + offset[0], 1 + offset[1]:sx - 1 + offset[1], 1 + offset[2]:sy - 1 + offset[2]]

def spread(field, conduct):
    padded = jnp.pad(field, ((1, 1), (0, 0), (0, 0)))
    cond_pad = jnp.pad(conduct, ((1, 1), (0, 0), (0, 0)))
    middle = shifted(padded, (0, 0, 0))
    mid_cond = shifted(cond_pad, (0, 0, 0))
    summed = jnp.zeros_like(middle)
    for offset in OFFSETS:
        beside = shifted(padded, offset)
        near_cond = shifted(cond_pad, offset)
        summed = summed + 0.5 * (mid_cond + near_cond) * (beside - middle)
    return summed

def tendency(state, coefs):
    suction = state[0]
    warmth = state[1]
    bending = jnp.tanh(suction)
    strong = 1.5 + bending
    gentle = 1.5 + 0.5 * bending
    water_flow = spread(suction, coefs[0] * strong) + spread(warmth, coefs[1] * gentle)
    energy = spread(warmth, coefs[2] * gentle) + spread(suction, coefs[3] * strong)
    return jnp.stack([water_flow, energy])

def forward_all(state, coefs):
    padded = jnp.pad(state, ((0, 0), (0, 0), (1, 1), (1, 1)))
    cond_pad = jnp.pad(coefs, ((0, 0), (0, 0), (1, 1), (1, 1)))

    def block_step(index):
        start = index * CX
        piece = lax.dynamic_slice_in_dim(padded, start, CX + 2, 2)
        cond_piece = lax.dynamic_slice_in_dim(cond_pad, start, CX + 2, 2)
        return tendency(piece, cond_piece)
    blocks = lax.map(block_step, jnp.arange(N_GX, dtype=jnp.int32))
    return jnp.moveaxis(blocks, 0, 2).reshape(2, NZ, NX, NY)

def adjoint_all(state, coefs, adjoint):
    padded = jnp.pad(state, ((0, 0), (0, 0), (2, 2), (2, 2)))
    cond_pad = jnp.pad(coefs, ((0, 0), (0, 0), (2, 2), (2, 2)))
    adj_pad = jnp.pad(adjoint, ((0, 0), (0, 0), (1, 1), (1, 1)))

    def block_step(index):
        start = index * CX
        piece = lax.dynamic_slice_in_dim(padded, start, CX + 4, 2)
        cond_piece = lax.dynamic_slice_in_dim(cond_pad, start, CX + 4, 2)
        adj_piece = lax.dynamic_slice_in_dim(adj_pad, start, CX + 2, 2)

        def tendency_at(field):
            return tendency(field, cond_piece)
        _, pullback = jax.vjp(tendency_at, piece)
        pulled = pullback(adj_piece)[0]
        return pulled[:, :, 2:-2, 2:-2]
    blocks = lax.map(block_step, jnp.arange(N_GX, dtype=jnp.int32))
    return jnp.moveaxis(blocks, 0, 2).reshape(2, NZ, NX, NY)

def reference(stored_slab, block_scales, holder, soil_class, soil_table, cotangent):
    slab = stored_slab.astype(jnp.float32).reshape(2, NZ, NX, N_GY, CY)
    slab = jnp.take(slab, holder, axis=3)
    scales = jnp.take(block_scales.astype(jnp.float32), holder, axis=3)
    state0 = (slab.reshape(2, NZ, N_GX, CX, N_GY, CY) * scales[:, :, :, None, :, None]).reshape(2, NZ, NX, NY)
    coefs = jnp.transpose(soil_table[soil_class], (2, 0, 1))[:, None]
    state1 = state0 + forward_all(state0, coefs)
    state2 = state1 + forward_all(state1, coefs)
    adjoint1 = cotangent + adjoint_all(state1, coefs, cotangent)
    adjoint0 = adjoint1 + adjoint_all(state0, coefs, adjoint1)
    return (state2, adjoint0)
```

```python
import jax
import jax.numpy as jnp
from jax import lax
from jax.experimental import pallas as pl
from jax.experimental.pallas import tpu as pltpu
from jax.sharding import PartitionSpec as P

F32 = jnp.float32
NCOEF = 4
VMEM = pltpu.MemorySpace.VMEM
SMEM = pltpu.MemorySpace.SMEM


def _roll(v, shift, axis):
    shift = shift % v.shape[axis]
    if shift == 0:
        return v
    return pltpu.roll(v, shift, axis)


def _iotas(shape):
    return lax.broadcasted_iota(jnp.int32, shape, 0), lax.broadcasted_iota(jnp.int32, shape, 1)


def _pack_edges(vals, xf_ref, xl_ref, yf_ref, yl_ref):
    x, y = vals[0].shape
    _, lane = _iotas((x, y))
    xf_ref[...] = jnp.zeros(xf_ref.shape, F32)
    xl_ref[...] = jnp.zeros(xl_ref.shape, F32)
    yf = jnp.zeros((x, y), F32)
    yl = jnp.zeros((x, y), F32)
    for k, v in enumerate(vals):
        xf_ref[k : k + 1, :] = v[0:1, :]
        xl_ref[k : k + 1, :] = v[x - 1 : x, :]
        yf = jnp.where(lane == k, _roll(v, k, 1), yf)
        yl = jnp.where(lane == k, _roll(v, k - (y - 1), 1), yl)
    yf_ref[...] = yf
    yl_ref[...] = yl


def _expand_halo(xm_ref, xp_ref, ym_ref, yp_ref, first, nf, nz, dst):
    hxm, hxp, hym, hyp = dst
    x, y = hxm.shape[2], hxm.shape[3]
    ymv = ym_ref[...]
    ypv = yp_ref[...]
    for f in range(nf):
        for z in range(nz):
            k = first + f * nz + z
            hxm[f, z] = jnp.broadcast_to(xm_ref[k : k + 1, :], (x, y))
            hxp[f, z] = jnp.broadcast_to(xp_ref[k : k + 1, :], (x, y))
            hym[f, z] = _roll(ymv, -k, 1)
            hyp[f, z] = _roll(ypv, (y - 1) - k, 1)


def _coef_table(c_ref, cxm_ref, cxp_ref, cym_ref, cyp_ref, first, cs):
    x, y = c_ref.shape[1], c_ref.shape[2]
    ymv = cym_ref[...]
    ypv = cyp_ref[...]
    masks = _iotas((x, y))
    for k in range(NCOEF):
        r = first + k
        cv = c_ref[k]
        cs[k] = cv
        halo = (
            jnp.broadcast_to(cxm_ref[r : r + 1, :], (x, y)),
            jnp.broadcast_to(cxp_ref[r : r + 1, :], (x, y)),
            _roll(ymv, -r, 1),
            _roll(ypv, (y - 1) - r, 1),
        )
        for d, v in enumerate(_neighbours(cv, 0, [h[None] for h in halo], masks)):
            cs[4 + 4 * d + k] = v


def _neighbours(v, z, h, masks):
    row, lane = masks
    x, y = v.shape
    hxm, hxp, hym, hyp = h
    return (
        jnp.where(row == 0, hxm[z], _roll(v, 1, 0)),
        jnp.where(row == x - 1, hxp[z], _roll(v, x - 1, 0)),
        jnp.where(lane == 0, hym[z], _roll(v, 1, 1)),
        jnp.where(lane == y - 1, hyp[z], _roll(v, y - 1, 1)),
    )


def _field_at(ref, f, z, nz):
    zm = jnp.maximum(z - 1, 0)
    zp = jnp.minimum(z + 1, nz - 1)
    vm = jnp.where(z > 0, 1.0, 0.0).astype(F32)
    vp = jnp.where(z < nz - 1, 1.0, 0.0).astype(F32)
    return ref[f, z], ref[f, zm] * vm, ref[f, zp] * vp, vm, vp


def _gains(b):
    return 1.5 + b, 1.5 + 0.5 * b


def _step_body(s_ref, sh, cs, o_ref, nz, masks):
    def body(z, carry):
        u, u_m, u_p, vm, vp = _field_at(s_ref, 0, z, nz)
        t, t_m, t_p, _, _ = _field_at(s_ref, 1, z, nz)
        c = [cs[k] for k in range(NCOEF)]
        g1, g2 = _gains(jnp.tanh(u))
        kw, dtv, lamb, kv = c[0] * g1, c[1] * g2, c[2] * g2, c[3] * g1
        a1 = jnp.zeros_like(u)
        a2 = jnp.zeros_like(u)
        for un, tn, valid in ((u_m, t_m, vm), (u_p, t_p, vp)):
            g1n, g2n = _gains(jnp.tanh(un))
            a1 = a1 + (g1 + valid * g1n) * (un - u)
            a2 = a2 + (g2 + valid * g2n) * (tn - t)
        f0 = c[0] * a1 + c[1] * a2
        f1 = c[2] * a2 + c[3] * a1
        uns = _neighbours(u, z, sh[0], masks)
        tns = _neighbours(t, z, sh[1], masks)
        for d in range(4):
            un, tn = uns[d], tns[d]
            g1n, g2n = _gains(jnp.tanh(un))
            cn = [cs[4 + 4 * d + k] for k in range(NCOEF)]
            du = un - u
            dt = tn - t
            f0 = f0 + (kw + cn[0] * g1n) * du + (dtv + cn[1] * g2n) * dt
            f1 = f1 + (lamb + cn[2] * g2n) * dt + (kv + cn[3] * g1n) * du
        o_ref[0, z] = u + 0.5 * f0
        o_ref[1, z] = t + 0.5 * f1
        return carry

    lax.fori_loop(0, nz, body, 0)


def _adjoint_body(s_ref, sh, a_ref, ah, cs, o_ref, nz, masks):
    def body(z, carry):
        u, u_m, u_p, vm, vp = _field_at(s_ref, 0, z, nz)
        t, t_m, t_p, _, _ = _field_at(s_ref, 1, z, nz)
        a0, a0_m, a0_p, _, _ = _field_at(a_ref, 0, z, nz)
        a1, a1_m, a1_p, _, _ = _field_at(a_ref, 1, z, nz)
        c = [cs[k] for k in range(NCOEF)]
        b = jnp.tanh(u)
        g1, g2 = _gains(b)
        kw, dtv, lamb, kv = c[0] * g1, c[1] * g2, c[2] * g2, c[3] * g1
        zero = jnp.zeros_like(u)
        p10, p11, p20, p21 = zero, zero, zero, zero
        gu0, gu1, gt0, gt1 = zero, zero, zero, zero
        for un, tn, a0n, a1n, valid in ((u_m, t_m, a0_m, a1_m, vm), (u_p, t_p, a0_p, a1_p, vp)):
            g1n, g2n = _gains(jnp.tanh(un))
            s1 = g1 + valid * g1n
            s2 = g2 + valid * g2n
            du, dt, da0, da1 = un - u, tn - t, a0n - a0, a1n - a1
            p10 = p10 + s1 * da0
            p11 = p11 + s1 * da1
            p20 = p20 + s2 * da0
            p21 = p21 + s2 * da1
            gu0 = gu0 + du * da0
            gu1 = gu1 + du * da1
            gt0 = gt0 + dt * da0
            gt1 = gt1 + dt * da1
        ju = c[0] * p10 + c[3] * p11
        jt = c[1] * p20 + c[2] * p21
        uns = _neighbours(u, z, sh[0], masks)
        tns = _neighbours(t, z, sh[1], masks)
        a0ns = _neighbours(a0, z, ah[0], masks)
        a1ns = _neighbours(a1, z, ah[1], masks)
        for d in range(4):
            un, tn, a0n, a1n = uns[d], tns[d], a0ns[d], a1ns[d]
            g1n, g2n = _gains(jnp.tanh(un))
            cn = [cs[4 + 4 * d + k] for k in range(NCOEF)]
            du, dt, da0, da1 = un - u, tn - t, a0n - a0, a1n - a1
            ju = ju + (kw + cn[0] * g1n) * da0 + (kv + cn[3] * g1n) * da1
            jt = jt + (dtv + cn[1] * g2n) * da0 + (lamb + cn[2] * g2n) * da1
            gu0 = gu0 + du * da0
            gu1 = gu1 + du * da1
            gt0 = gt0 + dt * da0
            gt1 = gt1 + dt * da1
        gsum = c[0] * gu0 + c[3] * gu1 + 0.5 * (c[1] * gt0 + c[2] * gt1)
        o_ref[0, z] = a0 + 0.5 * ju - 0.5 * (1.0 - b * b) * gsum
        o_ref[1, z] = a1 + 0.5 * jt
        return carry

    lax.fori_loop(0, nz, body, 0)


def _halo_scratch(nf, nz, x, y):
    return [pltpu.VMEM((nf, nz, x, y), F32) for _ in range(4)]


def _edge_shapes(rows, x, y):
    return (
        jax.ShapeDtypeStruct((rows, y), F32),
        jax.ShapeDtypeStruct((rows, y), F32),
        jax.ShapeDtypeStruct((x, y), F32),
        jax.ShapeDtypeStruct((x, y), F32),
    )


def _rows(n):
    return -(-n // 8) * 8


def prep_call(soil_class, soil_table, cot):
    nf, nz, x, y = cot.shape
    nclass = soil_table.shape[0]

    def kernel(cls_ref, tab_ref, cot_ref, coef_ref, xf_ref, xl_ref, yf_ref, yl_ref):
        cls = cls_ref[...]
        coefs = []
        for k in range(NCOEF):
            cv = jnp.zeros(cls.shape, F32)
            for j in range(nclass):
                cv = jnp.where(cls == j, tab_ref[j, k], cv)
            coef_ref[k] = cv
            coefs.append(cv)
        vals = [cot_ref[f, z] for f in range(nf) for z in range(nz)] + coefs
        _pack_edges(vals, xf_ref, xl_ref, yf_ref, yl_ref)

    rows = _rows(nf * nz + NCOEF)
    return pl.pallas_call(
        kernel,
        out_shape=(jax.ShapeDtypeStruct((NCOEF, x, y), F32),) + _edge_shapes(rows, x, y),
        in_specs=[
            pl.BlockSpec(memory_space=VMEM),
            pl.BlockSpec(memory_space=SMEM),
            pl.BlockSpec(memory_space=VMEM),
        ],
    )(soil_class, soil_table, cot)


def state0_call(gathered, scales, index):
    _, nf, planes, x, y = gathered.shape
    nz = planes - 1

    def kernel(idx_ref, sc_ref, own_ref, left_ref, right_ref, s_ref, xf_ref, xl_ref, ym_ref, yp_ref):
        hown, hl, hr = idx_ref[0], idx_ref[1], idx_ref[2]
        has_l = jnp.where(idx_ref[3] > 0, 1.0, 0.0).astype(F32)
        has_r = jnp.where(idx_ref[4] > 0, 1.0, 0.0).astype(F32)
        _, lane = _iotas((x, y))
        vals = []
        ym = jnp.zeros((x, y), F32)
        yp = jnp.zeros((x, y), F32)
        for f in range(nf):
            for z in range(nz):
                k = f * nz + z
                v = own_ref[f, z].astype(F32) * sc_ref[hown * (nf * nz) + k]
                s_ref[f, z] = v
                vals.append(v)
                lv = left_ref[f, z].astype(F32) * (sc_ref[hl * (nf * nz) + k] * has_l)
                rv = right_ref[f, z].astype(F32) * (sc_ref[hr * (nf * nz) + k] * has_r)
                ym = jnp.where(lane == k, _roll(lv, k - (y - 1), 1), ym)
                yp = jnp.where(lane == k, _roll(rv, k, 1), yp)
        ym_ref[...] = ym
        yp_ref[...] = yp
        xf_ref[...] = jnp.zeros(xf_ref.shape, F32)
        xl_ref[...] = jnp.zeros(xl_ref.shape, F32)
        for k, v in enumerate(vals):
            xf_ref[k : k + 1, :] = v[0:1, :]
            xl_ref[k : k + 1, :] = v[x - 1 : x, :]

    block = (None, nf, planes, x, y)
    rows = _rows(nf * nz)
    grid_spec = pltpu.PrefetchScalarGridSpec(
        num_scalar_prefetch=2,
        grid=(1,),
        in_specs=[
            pl.BlockSpec(block, lambda i, idx, sc: (idx[0], 0, 0, 0, 0)),
            pl.BlockSpec(block, lambda i, idx, sc: (idx[1], 0, 0, 0, 0)),
            pl.BlockSpec(block, lambda i, idx, sc: (idx[2], 0, 0, 0, 0)),
        ],
        out_specs=[
            pl.BlockSpec((nf, nz, x, y), lambda i, idx, sc: (0, 0, 0, 0)),
            pl.BlockSpec((rows, y), lambda i, idx, sc: (0, 0)),
            pl.BlockSpec((rows, y), lambda i, idx, sc: (0, 0)),
            pl.BlockSpec((x, y), lambda i, idx, sc: (0, 0)),
            pl.BlockSpec((x, y), lambda i, idx, sc: (0, 0)),
        ],
    )
    return pl.pallas_call(
        kernel,
        grid_spec=grid_spec,
        out_shape=(jax.ShapeDtypeStruct((nf, nz, x, y), F32),) + _edge_shapes(rows, x, y),
    )(index, scales, gathered, gathered, gathered)


def step_call(s, s_halo, coef, c_halo, c_first, with_edges):
    nf, nz, x, y = s.shape

    def kernel(*refs):
        s_ref, sxm, sxp, sym, syp, c_ref, cxm, cxp, cym, cyp = refs[:10]
        rest = refs[10:]
        if with_edges:
            o_ref, xf_ref, xl_ref, yf_ref, yl_ref = rest[:5]
            scratch = rest[5:]
        else:
            o_ref = rest[0]
            scratch = rest[1:]
        sh_all = scratch[0:4]
        cs = scratch[4]
        _expand_halo(sxm, sxp, sym, syp, 0, nf, nz, sh_all)
        _coef_table(c_ref, cxm, cxp, cym, cyp, c_first, cs)
        masks = _iotas((x, y))
        sh = [tuple(h.at[f] for h in sh_all) for f in range(nf)]
        _step_body(s_ref, sh, cs, o_ref, nz, masks)
        if with_edges:
            vals = [o_ref[f, z] for f in range(nf) for z in range(nz)]
            _pack_edges(vals, xf_ref, xl_ref, yf_ref, yl_ref)

    out_shape = (jax.ShapeDtypeStruct(s.shape, F32),)
    if with_edges:
        out_shape = out_shape + _edge_shapes(_rows(nf * nz), x, y)
    res = pl.pallas_call(
        kernel,
        out_shape=out_shape,
        scratch_shapes=_halo_scratch(nf, nz, x, y) + [pltpu.VMEM((5 * NCOEF, x, y), F32)],
    )(s, *s_halo, coef, *c_halo)
    return res if with_edges else res[0]


def adjoint_call(s, s_halo, a, a_halo, a_first, coef, c_halo, c_first, with_edges):
    nf, nz, x, y = s.shape

    def kernel(*refs):
        s_ref, sxm, sxp, sym, syp, a_ref, axm, axp, aym, ayp, c_ref, cxm, cxp, cym, cyp = refs[:15]
        rest = refs[15:]
        if with_edges:
            o_ref, xf_ref, xl_ref, yf_ref, yl_ref = rest[:5]
            scratch = rest[5:]
        else:
            o_ref = rest[0]
            scratch = rest[1:]
        sh_all = scratch[0:4]
        ah_all = scratch[4:8]
        cs = scratch[8]
        _expand_halo(sxm, sxp, sym, syp, 0, nf, nz, sh_all)
        _expand_halo(axm, axp, aym, ayp, a_first, nf, nz, ah_all)
        _coef_table(c_ref, cxm, cxp, cym, cyp, c_first, cs)
        masks = _iotas((x, y))
        sh = [tuple(h.at[f] for h in sh_all) for f in range(nf)]
        ah = [tuple(h.at[f] for h in ah_all) for f in range(nf)]
        _adjoint_body(s_ref, sh, a_ref, ah, cs, o_ref, nz, masks)
        if with_edges:
            vals = [o_ref[f, z] for f in range(nf) for z in range(nz)]
            _pack_edges(vals, xf_ref, xl_ref, yf_ref, yl_ref)

    out_shape = (jax.ShapeDtypeStruct(s.shape, F32),)
    if with_edges:
        out_shape = out_shape + _edge_shapes(_rows(nf * nz), x, y)
    res = pl.pallas_call(
        kernel,
        out_shape=out_shape,
        scratch_shapes=_halo_scratch(nf, nz, x, y)
        + _halo_scratch(nf, nz, x, y)
        + [pltpu.VMEM((5 * NCOEF, x, y), F32)],
    )(s, *s_halo, a, *a_halo, coef, *c_halo)
    return res if with_edges else res[0]


def _shift(v, axis, step):
    n = lax.axis_size(axis)
    if step > 0:
        pairs = [(i, i + 1) for i in range(n - 1)]
    else:
        pairs = [(i + 1, i) for i in range(n - 1)]
    return lax.ppermute(v, axis, pairs)


def exchange(xf, xl, yf, yl):
    return (
        _shift(xl, "gx", 1),
        _shift(xf, "gx", -1),
        _shift(yl, "gy", 1),
        _shift(yf, "gy", -1),
    )


def on_device(stored_slab, block_scales, holder, soil_class, soil_table, cotangent):
    nf, nz, x, y = stored_slab.shape
    ngy = lax.axis_size("gy")
    gy = lax.axis_index("gy")

    planes = jnp.pad(
        block_scales.reshape(nf, 1, 1, nz), ((0, 0), (0, 0), (0, x - 1), (0, y - nz))
    )
    packed = jnp.concatenate([stored_slab, planes], axis=1)
    gathered = lax.all_gather(packed, "gy", axis=0)

    coef, cxf, cxl, cyf, cyl = prep_call(soil_class, soil_table, cotangent)
    c_halo = exchange(cxf, cxl, cyf, cyl)
    c_first = nf * nz

    index = jnp.stack(
        [
            holder[gy],
            holder[jnp.maximum(gy - 1, 0)],
            holder[jnp.minimum(gy + 1, ngy - 1)],
            (gy > 0).astype(jnp.int32),
            (gy < ngy - 1).astype(jnp.int32),
        ]
    )
    scales = gathered[:, :, nz, 0, :nz].astype(F32).reshape(-1)
    s0, s0xf, s0xl, s0ym, s0yp = state0_call(gathered, scales, index)
    s0_halo = (_shift(s0xl, "gx", 1), _shift(s0xf, "gx", -1), s0ym, s0yp)

    s1, *s1_edges = step_call(s0, s0_halo, coef, c_halo, c_first, True)
    s1_halo = exchange(*s1_edges)

    a1, *a1_edges = adjoint_call(
        s1, s1_halo, cotangent, c_halo, 0, coef, c_halo, c_first, True
    )
    a1_halo = exchange(*a1_edges)
    s2 = step_call(s1, s1_halo, coef, c_halo, c_first, False)

    sens = adjoint_call(s0, s0_halo, a1, a1_halo, 0, coef, c_halo, c_first, False)
    return (s2, sens)


def solution(mesh):
    placed = (
        P(None, None, "gx", "gy"),
        P(None, None, "gx", "gy"),
        P(),
        P("gx", "gy"),
        P(),
        P(None, None, "gx", "gy"),
    )
    return jax.shard_map(
        on_device,
        mesh=mesh,
        in_specs=placed,
        out_specs=(P(None, None, "gx", "gy"), P(None, None, "gx", "gy")),
        check_vma=False,
    )
```

```python
import jax
import jax.numpy as jnp
from jax import lax
from jax.experimental import pallas as pl
from jax.experimental.pallas import tpu as pltpu
from jax.sharding import PartitionSpec as P

F32 = jnp.float32
NCOEF = 4
VMEM = pltpu.MemorySpace.VMEM
SMEM = pltpu.MemorySpace.SMEM


def _roll(v, shift, axis):
    shift = shift % v.shape[axis]
    if shift == 0:
        return v
    return pltpu.roll(v, shift, axis)


def _iotas(shape):
    return lax.broadcasted_iota(jnp.int32, shape, 0), lax.broadcasted_iota(jnp.int32, shape, 1)


def _pack_edges(vals, xf_ref, xl_ref, yf_ref, yl_ref):
    x, y = vals[0].shape
    _, lane = _iotas((x, y))
    xf_ref[...] = jnp.zeros(xf_ref.shape, F32)
    xl_ref[...] = jnp.zeros(xl_ref.shape, F32)
    yf = jnp.zeros((x, y), F32)
    yl = jnp.zeros((x, y), F32)
    for k, v in enumerate(vals):
        xf_ref[k : k + 1, :] = v[0:1, :]
        xl_ref[k : k + 1, :] = v[x - 1 : x, :]
        yf = jnp.where(lane == k, _roll(v, k, 1), yf)
        yl = jnp.where(lane == k, _roll(v, k - (y - 1), 1), yl)
    yf_ref[...] = yf
    yl_ref[...] = yl


def _expand_halo(xm_ref, xp_ref, ym_ref, yp_ref, first, nf, nz, dst):
    hxm, hxp, hym, hyp = dst
    x, y = hxm.shape[2], hxm.shape[3]
    ymv = ym_ref[...]
    ypv = yp_ref[...]
    for f in range(nf):
        for z in range(nz):
            k = first + f * nz + z
            hxm[f, z] = jnp.broadcast_to(xm_ref[k : k + 1, :], (x, y))
            hxp[f, z] = jnp.broadcast_to(xp_ref[k : k + 1, :], (x, y))
            hym[f, z] = _roll(ymv, -k, 1)
            hyp[f, z] = _roll(ypv, (y - 1) - k, 1)


def _coef_table(c_ref, cxm_ref, cxp_ref, cym_ref, cyp_ref, first, cs):
    x, y = c_ref.shape[1], c_ref.shape[2]
    ymv = cym_ref[...]
    ypv = cyp_ref[...]
    masks = _iotas((x, y))
    for k in range(NCOEF):
        r = first + k
        cv = c_ref[k]
        cs[k] = cv
        halo = (
            jnp.broadcast_to(cxm_ref[r : r + 1, :], (x, y)),
            jnp.broadcast_to(cxp_ref[r : r + 1, :], (x, y)),
            _roll(ymv, -r, 1),
            _roll(ypv, (y - 1) - r, 1),
        )
        for d, v in enumerate(_neighbours(cv, 0, [h[None] for h in halo], masks)):
            cs[4 + 4 * d + k] = v


def _neighbours(v, z, h, masks):
    row, lane = masks
    x, y = v.shape
    hxm, hxp, hym, hyp = h
    return (
        jnp.where(row == 0, hxm[z], _roll(v, 1, 0)),
        jnp.where(row == x - 1, hxp[z], _roll(v, x - 1, 0)),
        jnp.where(lane == 0, hym[z], _roll(v, 1, 1)),
        jnp.where(lane == y - 1, hyp[z], _roll(v, y - 1, 1)),
    )


def _field_at(ref, f, z, nz):
    zm = jnp.maximum(z - 1, 0)
    zp = jnp.minimum(z + 1, nz - 1)
    vm = jnp.where(z > 0, 1.0, 0.0).astype(F32)
    vp = jnp.where(z < nz - 1, 1.0, 0.0).astype(F32)
    return ref[f, z], ref[f, zm] * vm, ref[f, zp] * vp, vm, vp


def _gains(b):
    return 1.5 + b, 1.5 + 0.5 * b


def _step_body(s_ref, sh, cs, o_ref, nz, masks):
    def body(z, carry):
        u, u_m, u_p, vm, vp = _field_at(s_ref, 0, z, nz)
        t, t_m, t_p, _, _ = _field_at(s_ref, 1, z, nz)
        c = [cs[k] for k in range(NCOEF)]
        g1, g2 = _gains(jnp.tanh(u))
        kw, dtv, lamb, kv = c[0] * g1, c[1] * g2, c[2] * g2, c[3] * g1
        a1 = jnp.zeros_like(u)
        a2 = jnp.zeros_like(u)
        for un, tn, valid in ((u_m, t_m, vm), (u_p, t_p, vp)):
            g1n, g2n = _gains(jnp.tanh(un))
            a1 = a1 + (g1 + valid * g1n) * (un - u)
            a2 = a2 + (g2 + valid * g2n) * (tn - t)
        f0 = c[0] * a1 + c[1] * a2
        f1 = c[2] * a2 + c[3] * a1
        uns = _neighbours(u, z, sh[0], masks)
        tns = _neighbours(t, z, sh[1], masks)
        for d in range(4):
            un, tn = uns[d], tns[d]
            g1n, g2n = _gains(jnp.tanh(un))
            cn = [cs[4 + 4 * d + k] for k in range(NCOEF)]
            du = un - u
            dt = tn - t
            f0 = f0 + (kw + cn[0] * g1n) * du + (dtv + cn[1] * g2n) * dt
            f1 = f1 + (lamb + cn[2] * g2n) * dt + (kv + cn[3] * g1n) * du
        o_ref[0, z] = u + 0.5 * f0
        o_ref[1, z] = t + 0.5 * f1
        return carry

    lax.fori_loop(0, nz, body, 0)


def _adjoint_body(s_ref, sh, a_ref, ah, cs, o_ref, nz, masks):
    def body(z, carry):
        u, u_m, u_p, vm, vp = _field_at(s_ref, 0, z, nz)
        t, t_m, t_p, _, _ = _field_at(s_ref, 1, z, nz)
        a0, a0_m, a0_p, _, _ = _field_at(a_ref, 0, z, nz)
        a1, a1_m, a1_p, _, _ = _field_at(a_ref, 1, z, nz)
        c = [cs[k] for k in range(NCOEF)]
        b = jnp.tanh(u)
        g1, g2 = _gains(b)
        kw, dtv, lamb, kv = c[0] * g1, c[1] * g2, c[2] * g2, c[3] * g1
        zero = jnp.zeros_like(u)
        p10, p11, p20, p21 = zero, zero, zero, zero
        gu0, gu1, gt0, gt1 = zero, zero, zero, zero
        for un, tn, a0n, a1n, valid in ((u_m, t_m, a0_m, a1_m, vm), (u_p, t_p, a0_p, a1_p, vp)):
            g1n, g2n = _gains(jnp.tanh(un))
            s1 = g1 + valid * g1n
            s2 = g2 + valid * g2n
            du, dt, da0, da1 = un - u, tn - t, a0n - a0, a1n - a1
            p10 = p10 + s1 * da0
            p11 = p11 + s1 * da1
            p20 = p20 + s2 * da0
            p21 = p21 + s2 * da1
            gu0 = gu0 + du * da0
            gu1 = gu1 + du * da1
            gt0 = gt0 + dt * da0
            gt1 = gt1 + dt * da1
        ju = c[0] * p10 + c[3] * p11
        jt = c[1] * p20 + c[2] * p21
        uns = _neighbours(u, z, sh[0], masks)
        tns = _neighbours(t, z, sh[1], masks)
        a0ns = _neighbours(a0, z, ah[0], masks)
        a1ns = _neighbours(a1, z, ah[1], masks)
        for d in range(4):
            un, tn, a0n, a1n = uns[d], tns[d], a0ns[d], a1ns[d]
            g1n, g2n = _gains(jnp.tanh(un))
            cn = [cs[4 + 4 * d + k] for k in range(NCOEF)]
            du, dt, da0, da1 = un - u, tn - t, a0n - a0, a1n - a1
            ju = ju + (kw + cn[0] * g1n) * da0 + (kv + cn[3] * g1n) * da1
            jt = jt + (dtv + cn[1] * g2n) * da0 + (lamb + cn[2] * g2n) * da1
            gu0 = gu0 + du * da0
            gu1 = gu1 + du * da1
            gt0 = gt0 + dt * da0
            gt1 = gt1 + dt * da1
        gsum = c[0] * gu0 + c[3] * gu1 + 0.5 * (c[1] * gt0 + c[2] * gt1)
        o_ref[0, z] = a0 + 0.5 * ju - 0.5 * (1.0 - b * b) * gsum
        o_ref[1, z] = a1 + 0.5 * jt
        return carry

    lax.fori_loop(0, nz, body, 0)


def _halo_scratch(nf, nz, x, y):
    return [pltpu.VMEM((nf, nz, x, y), F32) for _ in range(4)]


def _edge_shapes(rows, x, y):
    return (
        jax.ShapeDtypeStruct((rows, y), F32),
        jax.ShapeDtypeStruct((rows, y), F32),
        jax.ShapeDtypeStruct((x, y), F32),
        jax.ShapeDtypeStruct((x, y), F32),
    )


def _rows(n):
    return -(-n // 8) * 8


def prep_call(soil_class, soil_table, cot):
    nf, nz, x, y = cot.shape
    nclass = soil_table.shape[0]

    def kernel(cls_ref, tab_ref, cot_ref, coef_ref, xf_ref, xl_ref, yf_ref, yl_ref):
        cls = cls_ref[...]
        coefs = []
        for k in range(NCOEF):
            cv = jnp.zeros(cls.shape, F32)
            for j in range(nclass):
                cv = jnp.where(cls == j, tab_ref[j, k], cv)
            coef_ref[k] = cv
            coefs.append(cv)
        vals = [cot_ref[f, z] for f in range(nf) for z in range(nz)] + coefs
        _pack_edges(vals, xf_ref, xl_ref, yf_ref, yl_ref)

    rows = _rows(nf * nz + NCOEF)
    return pl.pallas_call(
        kernel,
        out_shape=(jax.ShapeDtypeStruct((NCOEF, x, y), F32),) + _edge_shapes(rows, x, y),
        in_specs=[
            pl.BlockSpec(memory_space=VMEM),
            pl.BlockSpec(memory_space=SMEM),
            pl.BlockSpec(memory_space=VMEM),
        ],
    )(soil_class, soil_table, cot)


def state0_call(pieces, scales):
    npiece, pp, x, y = pieces.shape
    per = pp - 1
    nplanes = npiece * per

    def kernel(sc_ref, r_ref, s_ref, xf_ref, xl_ref, yf_ref, yl_ref):
        nz = s_ref.shape[1]
        vals = []
        for k in range(nplanes):
            v = r_ref[k // per, k % per].astype(F32) * sc_ref[k]
            s_ref[k // nz, k % nz] = v
            vals.append(v)
        _pack_edges(vals, xf_ref, xl_ref, yf_ref, yl_ref)

    nf = 2
    nz = nplanes // nf
    return pl.pallas_call(
        kernel,
        out_shape=(jax.ShapeDtypeStruct((nf, nz, x, y), F32),) + _edge_shapes(_rows(nplanes), x, y),
        in_specs=[pl.BlockSpec(memory_space=SMEM), pl.BlockSpec(memory_space=VMEM)],
    )(scales, pieces)


def step_call(s, s_halo, coef, c_halo, c_first, with_edges):
    nf, nz, x, y = s.shape

    def kernel(*refs):
        s_ref, sxm, sxp, sym, syp, c_ref, cxm, cxp, cym, cyp = refs[:10]
        rest = refs[10:]
        if with_edges:
            o_ref, xf_ref, xl_ref, yf_ref, yl_ref = rest[:5]
            scratch = rest[5:]
        else:
            o_ref = rest[0]
            scratch = rest[1:]
        sh_all = scratch[0:4]
        cs = scratch[4]
        _expand_halo(sxm, sxp, sym, syp, 0, nf, nz, sh_all)
        _coef_table(c_ref, cxm, cxp, cym, cyp, c_first, cs)
        masks = _iotas((x, y))
        sh = [tuple(h.at[f] for h in sh_all) for f in range(nf)]
        _step_body(s_ref, sh, cs, o_ref, nz, masks)
        if with_edges:
            vals = [o_ref[f, z] for f in range(nf) for z in range(nz)]
            _pack_edges(vals, xf_ref, xl_ref, yf_ref, yl_ref)

    out_shape = (jax.ShapeDtypeStruct(s.shape, F32),)
    if with_edges:
        out_shape = out_shape + _edge_shapes(_rows(nf * nz), x, y)
    res = pl.pallas_call(
        kernel,
        out_shape=out_shape,
        scratch_shapes=_halo_scratch(nf, nz, x, y) + [pltpu.VMEM((5 * NCOEF, x, y), F32)],
    )(s, *s_halo, coef, *c_halo)
    return res if with_edges else res[0]


def adjoint_call(s, s_halo, a, a_halo, a_first, coef, c_halo, c_first, with_edges):
    nf, nz, x, y = s.shape

    def kernel(*refs):
        s_ref, sxm, sxp, sym, syp, a_ref, axm, axp, aym, ayp, c_ref, cxm, cxp, cym, cyp = refs[:15]
        rest = refs[15:]
        if with_edges:
            o_ref, xf_ref, xl_ref, yf_ref, yl_ref = rest[:5]
            scratch = rest[5:]
        else:
            o_ref = rest[0]
            scratch = rest[1:]
        sh_all = scratch[0:4]
        ah_all = scratch[4:8]
        cs = scratch[8]
        _expand_halo(sxm, sxp, sym, syp, 0, nf, nz, sh_all)
        _expand_halo(axm, axp, aym, ayp, a_first, nf, nz, ah_all)
        _coef_table(c_ref, cxm, cxp, cym, cyp, c_first, cs)
        masks = _iotas((x, y))
        sh = [tuple(h.at[f] for h in sh_all) for f in range(nf)]
        ah = [tuple(h.at[f] for h in ah_all) for f in range(nf)]
        _adjoint_body(s_ref, sh, a_ref, ah, cs, o_ref, nz, masks)
        if with_edges:
            vals = [o_ref[f, z] for f in range(nf) for z in range(nz)]
            _pack_edges(vals, xf_ref, xl_ref, yf_ref, yl_ref)

    out_shape = (jax.ShapeDtypeStruct(s.shape, F32),)
    if with_edges:
        out_shape = out_shape + _edge_shapes(_rows(nf * nz), x, y)
    res = pl.pallas_call(
        kernel,
        out_shape=out_shape,
        scratch_shapes=_halo_scratch(nf, nz, x, y)
        + _halo_scratch(nf, nz, x, y)
        + [pltpu.VMEM((5 * NCOEF, x, y), F32)],
    )(s, *s_halo, a, *a_halo, coef, *c_halo)
    return res if with_edges else res[0]


def _shift(v, axis, step):
    n = lax.axis_size(axis)
    if step > 0:
        pairs = [(i, i + 1) for i in range(n - 1)]
    else:
        pairs = [(i + 1, i) for i in range(n - 1)]
    return lax.ppermute(v, axis, pairs)


def exchange(xf, xl, yf, yl):
    return (
        _shift(xl, "gx", 1),
        _shift(xf, "gx", -1),
        _shift(yl, "gy", 1),
        _shift(yf, "gy", -1),
    )


def route_blocks(stored_slab, block_scales, holder):
    nf, nz, x, y = stored_slab.shape
    n = lax.axis_size("gy")
    per = nf * nz // n
    slab = stored_slab.reshape(n, per, x, y)
    sc = jnp.pad(block_scales.reshape(n, 1, 1, per), ((0, 0), (0, 0), (0, x - 1), (0, y - per)))
    send = jnp.concatenate([slab, sc], axis=1)
    held = lax.all_to_all(send, "gy", 0, 0, tiled=True)
    forward = jnp.take(held, holder, axis=0)
    return lax.all_to_all(forward, "gy", 0, 0, tiled=True)


def on_device(stored_slab, block_scales, holder, soil_class, soil_table, cotangent):
    nf, nz, x, y = stored_slab.shape

    coef, cxf, cxl, cyf, cyl = prep_call(soil_class, soil_table, cotangent)
    c_halo = exchange(cxf, cxl, cyf, cyl)
    c_first = nf * nz

    pieces = route_blocks(stored_slab, block_scales, holder)
    per = pieces.shape[1] - 1
    scales = pieces[:, per, 0, :per].astype(F32).reshape(-1)
    s0, *s0_edges = state0_call(pieces, scales)
    s0_halo = exchange(*s0_edges)

    s1, *s1_edges = step_call(s0, s0_halo, coef, c_halo, c_first, True)
    s1_halo = exchange(*s1_edges)

    a1, *a1_edges = adjoint_call(
        s1, s1_halo, cotangent, c_halo, 0, coef, c_halo, c_first, True
    )
    a1_halo = exchange(*a1_edges)
    s2 = step_call(s1, s1_halo, coef, c_halo, c_first, False)

    sens = adjoint_call(s0, s0_halo, a1, a1_halo, 0, coef, c_halo, c_first, False)
    return (s2, sens)


def solution(mesh):
    placed = (
        P(None, None, "gx", "gy"),
        P(None, None, "gx", "gy"),
        P(),
        P("gx", "gy"),
        P(),
        P(None, None, "gx", "gy"),
    )
    return jax.shard_map(
        on_device,
        mesh=mesh,
        in_specs=placed,
        out_specs=(P(None, None, "gx", "gy"), P(None, None, "gx", "gy")),
        check_vma=False,
    )
```

```python
import jax
import jax.numpy as jnp
from jax import lax
from jax.experimental import pallas as pl
from jax.experimental.pallas import tpu as pltpu
from jax.sharding import PartitionSpec as P

F32 = jnp.float32
NCOEF = 4
VMEM = pltpu.MemorySpace.VMEM
SMEM = pltpu.MemorySpace.SMEM


def _roll(v, shift, axis):
    shift = shift % v.shape[axis]
    if shift == 0:
        return v
    return pltpu.roll(v, shift, axis)


def _iotas(shape):
    return lax.broadcasted_iota(jnp.int32, shape, 0), lax.broadcasted_iota(jnp.int32, shape, 1)


def _pack_edges(vals, xf_ref, xl_ref, yf_ref, yl_ref):
    x, y = vals[0].shape
    _, lane = _iotas((x, y))
    xf_ref[...] = jnp.zeros(xf_ref.shape, F32)
    xl_ref[...] = jnp.zeros(xl_ref.shape, F32)
    yf = jnp.zeros((x, y), F32)
    yl = jnp.zeros((x, y), F32)
    for k, v in enumerate(vals):
        xf_ref[k : k + 1, :] = v[0:1, :]
        xl_ref[k : k + 1, :] = v[x - 1 : x, :]
        yf = jnp.where(lane == k, _roll(v, k, 1), yf)
        yl = jnp.where(lane == k, _roll(v, k - (y - 1), 1), yl)
    yf_ref[...] = yf
    yl_ref[...] = yl


def _expand_halo(xm_ref, xp_ref, ym_ref, yp_ref, first, nf, nz, dst):
    hxm, hxp, hym, hyp = dst
    x, y = hxm.shape[2], hxm.shape[3]
    ymv = ym_ref[...]
    ypv = yp_ref[...]
    for f in range(nf):
        for z in range(nz):
            k = first + f * nz + z
            hxm[f, z] = jnp.broadcast_to(xm_ref[k : k + 1, :], (x, y))
            hxp[f, z] = jnp.broadcast_to(xp_ref[k : k + 1, :], (x, y))
            hym[f, z] = _roll(ymv, -k, 1)
            hyp[f, z] = _roll(ypv, (y - 1) - k, 1)


def _coef_table(c_ref, cxm_ref, cxp_ref, cym_ref, cyp_ref, first, cs):
    x, y = c_ref.shape[1], c_ref.shape[2]
    ymv = cym_ref[...]
    ypv = cyp_ref[...]
    masks = _iotas((x, y))
    for k in range(NCOEF):
        r = first + k
        cv = c_ref[k]
        cs[k] = cv
        halo = (
            jnp.broadcast_to(cxm_ref[r : r + 1, :], (x, y)),
            jnp.broadcast_to(cxp_ref[r : r + 1, :], (x, y)),
            _roll(ymv, -r, 1),
            _roll(ypv, (y - 1) - r, 1),
        )
        for d, v in enumerate(_neighbours(cv, 0, [h[None] for h in halo], masks)):
            cs[4 + 4 * d + k] = v


def _neighbours(v, z, h, masks):
    row, lane = masks
    x, y = v.shape
    hxm, hxp, hym, hyp = h
    return (
        jnp.where(row == 0, hxm[z], _roll(v, 1, 0)),
        jnp.where(row == x - 1, hxp[z], _roll(v, x - 1, 0)),
        jnp.where(lane == 0, hym[z], _roll(v, 1, 1)),
        jnp.where(lane == y - 1, hyp[z], _roll(v, y - 1, 1)),
    )


def _field_at(ref, f, z, nz):
    zm = jnp.maximum(z - 1, 0)
    zp = jnp.minimum(z + 1, nz - 1)
    vm = jnp.where(z > 0, 1.0, 0.0).astype(F32)
    vp = jnp.where(z < nz - 1, 1.0, 0.0).astype(F32)
    return ref[f, z], ref[f, zm] * vm, ref[f, zp] * vp, vm, vp


def _gains(b):
    return 1.5 + b, 1.5 + 0.5 * b


def _step_body(s_ref, sh, cs, o_ref, nz, masks):
    def body(z, carry):
        u, u_m, u_p, vm, vp = _field_at(s_ref, 0, z, nz)
        t, t_m, t_p, _, _ = _field_at(s_ref, 1, z, nz)
        c = [cs[k] for k in range(NCOEF)]
        g1, g2 = _gains(jnp.tanh(u))
        kw, dtv, lamb, kv = c[0] * g1, c[1] * g2, c[2] * g2, c[3] * g1
        a1 = jnp.zeros_like(u)
        a2 = jnp.zeros_like(u)
        for un, tn, valid in ((u_m, t_m, vm), (u_p, t_p, vp)):
            g1n, g2n = _gains(jnp.tanh(un))
            a1 = a1 + (g1 + valid * g1n) * (un - u)
            a2 = a2 + (g2 + valid * g2n) * (tn - t)
        f0 = c[0] * a1 + c[1] * a2
        f1 = c[2] * a2 + c[3] * a1
        uns = _neighbours(u, z, sh[0], masks)
        tns = _neighbours(t, z, sh[1], masks)
        for d in range(4):
            un, tn = uns[d], tns[d]
            g1n, g2n = _gains(jnp.tanh(un))
            cn = [cs[4 + 4 * d + k] for k in range(NCOEF)]
            du = un - u
            dt = tn - t
            f0 = f0 + (kw + cn[0] * g1n) * du + (dtv + cn[1] * g2n) * dt
            f1 = f1 + (lamb + cn[2] * g2n) * dt + (kv + cn[3] * g1n) * du
        o_ref[0, z] = u + 0.5 * f0
        o_ref[1, z] = t + 0.5 * f1
        return carry

    lax.fori_loop(0, nz, body, 0)


def _adjoint_body(s_ref, sh, a_ref, ah, cs, o_ref, nz, masks):
    def body(z, carry):
        u, u_m, u_p, vm, vp = _field_at(s_ref, 0, z, nz)
        t, t_m, t_p, _, _ = _field_at(s_ref, 1, z, nz)
        a0, a0_m, a0_p, _, _ = _field_at(a_ref, 0, z, nz)
        a1, a1_m, a1_p, _, _ = _field_at(a_ref, 1, z, nz)
        c = [cs[k] for k in range(NCOEF)]
        b = jnp.tanh(u)
        g1, g2 = _gains(b)
        kw, dtv, lamb, kv = c[0] * g1, c[1] * g2, c[2] * g2, c[3] * g1
        zero = jnp.zeros_like(u)
        p10, p11, p20, p21 = zero, zero, zero, zero
        gu0, gu1, gt0, gt1 = zero, zero, zero, zero
        for un, tn, a0n, a1n, valid in ((u_m, t_m, a0_m, a1_m, vm), (u_p, t_p, a0_p, a1_p, vp)):
            g1n, g2n = _gains(jnp.tanh(un))
            s1 = g1 + valid * g1n
            s2 = g2 + valid * g2n
            du, dt, da0, da1 = un - u, tn - t, a0n - a0, a1n - a1
            p10 = p10 + s1 * da0
            p11 = p11 + s1 * da1
            p20 = p20 + s2 * da0
            p21 = p21 + s2 * da1
            gu0 = gu0 + du * da0
            gu1 = gu1 + du * da1
            gt0 = gt0 + dt * da0
            gt1 = gt1 + dt * da1
        ju = c[0] * p10 + c[3] * p11
        jt = c[1] * p20 + c[2] * p21
        uns = _neighbours(u, z, sh[0], masks)
        tns = _neighbours(t, z, sh[1], masks)
        a0ns = _neighbours(a0, z, ah[0], masks)
        a1ns = _neighbours(a1, z, ah[1], masks)
        for d in range(4):
            un, tn, a0n, a1n = uns[d], tns[d], a0ns[d], a1ns[d]
            g1n, g2n = _gains(jnp.tanh(un))
            cn = [cs[4 + 4 * d + k] for k in range(NCOEF)]
            du, dt, da0, da1 = un - u, tn - t, a0n - a0, a1n - a1
            ju = ju + (kw + cn[0] * g1n) * da0 + (kv + cn[3] * g1n) * da1
            jt = jt + (dtv + cn[1] * g2n) * da0 + (lamb + cn[2] * g2n) * da1
            gu0 = gu0 + du * da0
            gu1 = gu1 + du * da1
            gt0 = gt0 + dt * da0
            gt1 = gt1 + dt * da1
        gsum = c[0] * gu0 + c[3] * gu1 + 0.5 * (c[1] * gt0 + c[2] * gt1)
        o_ref[0, z] = a0 + 0.5 * ju - 0.5 * (1.0 - b * b) * gsum
        o_ref[1, z] = a1 + 0.5 * jt
        return carry

    lax.fori_loop(0, nz, body, 0)


def _halo_scratch(nf, nz, x, y):
    return [pltpu.VMEM((nf, nz, x, y), F32) for _ in range(4)]


def _edge_shapes(rows, x, y):
    return (
        jax.ShapeDtypeStruct((rows, y), F32),
        jax.ShapeDtypeStruct((rows, y), F32),
        jax.ShapeDtypeStruct((x, y), F32),
        jax.ShapeDtypeStruct((x, y), F32),
    )


def _rows(n):
    return -(-n // 8) * 8


def prep_call(soil_class, soil_table, cot, slab, scales):
    nf, nz, x, y = cot.shape
    nclass = soil_table.shape[0]
    nplanes = nf * nz

    def kernel(cls_ref, tab_ref, sc_ref, cot_ref, slab_ref, coef_ref, xf_ref, xl_ref, yf_ref, yl_ref):
        cls = cls_ref[...]
        coefs = []
        for k in range(NCOEF):
            cv = jnp.zeros(cls.shape, F32)
            for j in range(nclass):
                cv = jnp.where(cls == j, tab_ref[j, k], cv)
            coef_ref[k] = cv
            coefs.append(cv)
        vals = [cot_ref[f, z] for f in range(nf) for z in range(nz)] + coefs
        _pack_edges(vals, xf_ref, xl_ref, yf_ref, yl_ref)
        base = len(vals)
        for k in range(nplanes):
            v = slab_ref[k // nz, k % nz].astype(F32)
            xf_ref[base + k : base + k + 1, :] = v[0:1, :]
            xl_ref[base + k : base + k + 1, :] = v[x - 1 : x, :]
        _, lane = _iotas((1, y))
        row = jnp.zeros((1, y), F32)
        for k in range(nplanes):
            row = jnp.where(lane == k, sc_ref[k], row)
        xf_ref[base + nplanes : base + nplanes + 1, :] = row
        xl_ref[base + nplanes : base + nplanes + 1, :] = row

    rows = _rows(2 * nplanes + NCOEF + 1)
    return pl.pallas_call(
        kernel,
        out_shape=(jax.ShapeDtypeStruct((NCOEF, x, y), F32),)
        + _edge_shapes(rows, x, y)[:2]
        + _edge_shapes(8, x, y)[2:],
        in_specs=[
            pl.BlockSpec(memory_space=VMEM),
            pl.BlockSpec(memory_space=SMEM),
            pl.BlockSpec(memory_space=SMEM),
            pl.BlockSpec(memory_space=VMEM),
            pl.BlockSpec(memory_space=VMEM),
        ],
    )(soil_class, soil_table, scales, cot, slab)


def state0_call(pieces, scales, nf, per):
    npiece, _, x, y = pieces.shape
    nplanes = npiece * per
    nz = nplanes // nf

    def kernel(sc_ref, r_ref, s_ref, xm_ref, xp_ref, ym_ref, yp_ref):
        _, lane = _iotas((x, y))
        ym = jnp.zeros((x, y), F32)
        yp = jnp.zeros((x, y), F32)
        for k in range(nplanes):
            p, i = k // per, k % per
            s_ref[k // nz, k % nz] = r_ref[p, i].astype(F32) * sc_ref[k]
            hx = r_ref[p, per].astype(F32)
            xm_ref[k : k + 1, :] = hx[i : i + 1, :] * sc_ref[nplanes + k]
            xp_ref[k : k + 1, :] = hx[per + i : per + i + 1, :] * sc_ref[2 * nplanes + k]
            hy = r_ref[p, per + 2].astype(F32)
            ym = jnp.where(lane == k, _roll(hy, k - i, 1) * sc_ref[3 * nplanes + k], ym)
            yp = jnp.where(lane == k, _roll(hy, k - (per + i), 1) * sc_ref[4 * nplanes + k], yp)
        ym_ref[...] = ym
        yp_ref[...] = yp

    return pl.pallas_call(
        kernel,
        out_shape=(jax.ShapeDtypeStruct((nf, nz, x, y), F32),) + _edge_shapes(nplanes, x, y),
        in_specs=[pl.BlockSpec(memory_space=SMEM), pl.BlockSpec(memory_space=VMEM)],
    )(scales, pieces)


def step_call(s, s_halo, coef, c_halo, c_first, with_edges):
    nf, nz, x, y = s.shape

    def kernel(*refs):
        s_ref, sxm, sxp, sym, syp, c_ref, cxm, cxp, cym, cyp = refs[:10]
        rest = refs[10:]
        if with_edges:
            o_ref, xf_ref, xl_ref, yf_ref, yl_ref = rest[:5]
            scratch = rest[5:]
        else:
            o_ref = rest[0]
            scratch = rest[1:]
        sh_all = scratch[0:4]
        cs = scratch[4]
        _expand_halo(sxm, sxp, sym, syp, 0, nf, nz, sh_all)
        _coef_table(c_ref, cxm, cxp, cym, cyp, c_first, cs)
        masks = _iotas((x, y))
        sh = [tuple(h.at[f] for h in sh_all) for f in range(nf)]
        _step_body(s_ref, sh, cs, o_ref, nz, masks)
        if with_edges:
            vals = [o_ref[f, z] for f in range(nf) for z in range(nz)]
            _pack_edges(vals, xf_ref, xl_ref, yf_ref, yl_ref)

    out_shape = (jax.ShapeDtypeStruct(s.shape, F32),)
    if with_edges:
        out_shape = out_shape + _edge_shapes(_rows(nf * nz), x, y)
    res = pl.pallas_call(
        kernel,
        out_shape=out_shape,
        scratch_shapes=_halo_scratch(nf, nz, x, y) + [pltpu.VMEM((5 * NCOEF, x, y), F32)],
    )(s, *s_halo, coef, *c_halo)
    return res if with_edges else res[0]


def adjoint_call(s, s_halo, a, a_halo, a_first, coef, c_halo, c_first, with_edges):
    nf, nz, x, y = s.shape

    def kernel(*refs):
        s_ref, sxm, sxp, sym, syp, a_ref, axm, axp, aym, ayp, c_ref, cxm, cxp, cym, cyp = refs[:15]
        rest = refs[15:]
        if with_edges:
            o_ref, xf_ref, xl_ref, yf_ref, yl_ref = rest[:5]
            scratch = rest[5:]
        else:
            o_ref = rest[0]
            scratch = rest[1:]
        sh_all = scratch[0:4]
        ah_all = scratch[4:8]
        cs = scratch[8]
        _expand_halo(sxm, sxp, sym, syp, 0, nf, nz, sh_all)
        _expand_halo(axm, axp, aym, ayp, a_first, nf, nz, ah_all)
        _coef_table(c_ref, cxm, cxp, cym, cyp, c_first, cs)
        masks = _iotas((x, y))
        sh = [tuple(h.at[f] for h in sh_all) for f in range(nf)]
        ah = [tuple(h.at[f] for h in ah_all) for f in range(nf)]
        _adjoint_body(s_ref, sh, a_ref, ah, cs, o_ref, nz, masks)
        if with_edges:
            vals = [o_ref[f, z] for f in range(nf) for z in range(nz)]
            _pack_edges(vals, xf_ref, xl_ref, yf_ref, yl_ref)

    out_shape = (jax.ShapeDtypeStruct(s.shape, F32),)
    if with_edges:
        out_shape = out_shape + _edge_shapes(_rows(nf * nz), x, y)
    res = pl.pallas_call(
        kernel,
        out_shape=out_shape,
        scratch_shapes=_halo_scratch(nf, nz, x, y)
        + _halo_scratch(nf, nz, x, y)
        + [pltpu.VMEM((5 * NCOEF, x, y), F32)],
    )(s, *s_halo, a, *a_halo, coef, *c_halo)
    return res if with_edges else res[0]


def _shift(v, axis, step):
    n = lax.axis_size(axis)
    if step > 0:
        pairs = [(i, i + 1) for i in range(n - 1)]
    else:
        pairs = [(i + 1, i) for i in range(n - 1)]
    return lax.ppermute(v, axis, pairs)


def exchange(xf, xl, yf, yl):
    return (
        _shift(xl, "gx", 1),
        _shift(xf, "gx", -1),
        _shift(yl, "gy", 1),
        _shift(yf, "gy", -1),
    )


def route_blocks(stored_slab, block_scales, holder, xm_all, xp_all, first):
    nf, nz, x, y = stored_slab.shape
    n = lax.axis_size("gy")
    nplanes = nf * nz
    per = nplanes // n
    bf = stored_slab.dtype
    slab = stored_slab.reshape(n, per, x, y)
    rows_m = xm_all[first : first + nplanes].astype(bf).reshape(n, per, y)
    rows_p = xp_all[first : first + nplanes].astype(bf).reshape(n, per, y)
    halo = jnp.concatenate([rows_m, rows_p], axis=1)[:, None]
    sc_m = xm_all[first + nplanes, :nplanes].astype(bf).reshape(n, 1, per)
    sc_p = xp_all[first + nplanes, :nplanes].astype(bf).reshape(n, 1, per)
    sc = jnp.concatenate([block_scales.reshape(n, 1, per), sc_m, sc_p], axis=1)
    sc = jnp.pad(sc, ((0, 0), (0, x - 3), (0, y - per)))[:, None]
    held = lax.all_to_all(jnp.concatenate([slab, halo, sc], axis=1), "gy", 0, 0, tiled=True)

    g = jnp.arange(n, dtype=jnp.int32)
    left = jnp.take(holder, jnp.maximum(g - 1, 0))
    right = jnp.take(holder, jnp.minimum(g + 1, n - 1))
    has_l = (g > 0)[:, None, None]
    has_r = (g < n - 1)[:, None, None]
    zero = jnp.zeros((), bf)
    cols_l = jnp.where(has_l, jnp.take(held[:, :per, :, y - 1], left, axis=0), zero)
    cols_r = jnp.where(has_r, jnp.take(held[:, :per, :, 0], right, axis=0), zero)
    scl_l = jnp.where(has_l, jnp.take(held[:, per + 1, 0:1, :per], left, axis=0), zero)
    scl_r = jnp.where(has_r, jnp.take(held[:, per + 1, 0:1, :per], right, axis=0), zero)
    cols = jnp.concatenate([cols_l, cols_r], axis=1).transpose(0, 2, 1)
    scl = jnp.concatenate([scl_l, scl_r], axis=2)
    yplane = jnp.concatenate(
        [
            jnp.pad(cols, ((0, 0), (0, 0), (0, y - 2 * per))),
            jnp.pad(scl, ((0, 0), (0, x - 1), (0, y - 2 * per))),
        ],
        axis=1,
    )
    forward = jnp.concatenate([jnp.take(held, holder, axis=0), yplane.reshape(n, 2, x, y)], axis=1)
    return lax.all_to_all(forward, "gy", 0, 0, tiled=True)


def on_device(stored_slab, block_scales, holder, soil_class, soil_table, cotangent):
    nf, nz, x, y = stored_slab.shape
    nplanes = nf * nz

    coef, cxf, cxl, cyf, cyl = prep_call(
        soil_class, soil_table, cotangent, stored_slab, block_scales.reshape(-1).astype(F32)
    )
    c_halo = exchange(cxf, cxl, cyf, cyl)
    c_first = nplanes

    pieces = route_blocks(stored_slab, block_scales, holder, c_halo[0], c_halo[1], nplanes + NCOEF)
    per = nplanes // pieces.shape[0]
    scales = jnp.concatenate(
        [
            pieces[:, per + 1, 0:3, :per].transpose(1, 0, 2).reshape(3, nplanes),
            pieces[:, per + 3, 0, : 2 * per].reshape(-1, 2, per).transpose(1, 0, 2).reshape(2, nplanes),
        ]
    ).astype(F32).reshape(-1)
    s0, *s0_halo = state0_call(pieces, scales, nf, per)

    s1, *s1_edges = step_call(s0, s0_halo, coef, c_halo, c_first, True)
    s1_halo = exchange(*s1_edges)

    a1, *a1_edges = adjoint_call(
        s1, s1_halo, cotangent, c_halo, 0, coef, c_halo, c_first, True
    )
    a1_halo = exchange(*a1_edges)
    s2 = step_call(s1, s1_halo, coef, c_halo, c_first, False)

    sens = adjoint_call(s0, s0_halo, a1, a1_halo, 0, coef, c_halo, c_first, False)
    return (s2, sens)


def solution(mesh):
    placed = (
        P(None, None, "gx", "gy"),
        P(None, None, "gx", "gy"),
        P(),
        P("gx", "gy"),
        P(),
        P(None, None, "gx", "gy"),
    )
    return jax.shard_map(
        on_device,
        mesh=mesh,
        in_specs=placed,
        out_specs=(P(None, None, "gx", "gy"), P(None, None, "gx", "gy")),
        check_vma=False,
    )
```

```python
import jax
import jax.numpy as jnp
from jax import lax
from jax.experimental import pallas as pl
from jax.experimental.pallas import tpu as pltpu
from jax.sharding import PartitionSpec as P

F32 = jnp.float32
NCOEF = 4
UNROLL = 4
VMEM = pltpu.MemorySpace.VMEM
SMEM = pltpu.MemorySpace.SMEM


def _roll(v, shift, axis):
    shift = shift % v.shape[axis]
    if shift == 0:
        return v
    return pltpu.roll(v, shift, axis)


def _iotas(shape):
    return lax.broadcasted_iota(jnp.int32, shape, 0), lax.broadcasted_iota(jnp.int32, shape, 1)


def _pack_edges(vals, xf_ref, xl_ref, yf_ref, yl_ref):
    x, y = vals[0].shape
    _, lane = _iotas((x, y))
    xf_ref[...] = jnp.zeros(xf_ref.shape, F32)
    xl_ref[...] = jnp.zeros(xl_ref.shape, F32)
    yf = jnp.zeros((x, y), F32)
    yl = jnp.zeros((x, y), F32)
    for k, v in enumerate(vals):
        xf_ref[k : k + 1, :] = v[0:1, :]
        xl_ref[k : k + 1, :] = v[x - 1 : x, :]
        yf = jnp.where(lane == k, _roll(v, k, 1), yf)
        yl = jnp.where(lane == k, _roll(v, k - (y - 1), 1), yl)
    yf_ref[...] = yf
    yl_ref[...] = yl


def _expand_halo(xm_ref, xp_ref, ym_ref, yp_ref, first, nf, nz, dst):
    hxm, hxp, hym, hyp = dst
    x, y = hxm.shape[2], hxm.shape[3]
    ymv = ym_ref[...]
    ypv = yp_ref[...]
    for f in range(nf):
        for z in range(nz):
            k = first + f * nz + z
            hxm[f, z] = jnp.broadcast_to(xm_ref[k : k + 1, :], (x, y))
            hxp[f, z] = jnp.broadcast_to(xp_ref[k : k + 1, :], (x, y))
            hym[f, z] = _roll(ymv, -k, 1)
            hyp[f, z] = _roll(ypv, (y - 1) - k, 1)


def _coef_table(c_ref, cxm_ref, cxp_ref, cym_ref, cyp_ref, first, cs):
    x, y = c_ref.shape[1], c_ref.shape[2]
    ymv = cym_ref[...]
    ypv = cyp_ref[...]
    masks = _iotas((x, y))
    for k in range(NCOEF):
        r = first + k
        cv = c_ref[k]
        cs[k] = cv
        halo = (
            jnp.broadcast_to(cxm_ref[r : r + 1, :], (x, y)),
            jnp.broadcast_to(cxp_ref[r : r + 1, :], (x, y)),
            _roll(ymv, -r, 1),
            _roll(ypv, (y - 1) - r, 1),
        )
        for d, v in enumerate(_neighbours(cv, 0, [h[None] for h in halo], masks)):
            cs[4 + 4 * d + k] = v


def _neighbours(v, z, h, masks):
    row, lane = masks
    x, y = v.shape
    hxm, hxp, hym, hyp = h
    return (
        jnp.where(row == 0, hxm[z], _roll(v, 1, 0)),
        jnp.where(row == x - 1, hxp[z], _roll(v, x - 1, 0)),
        jnp.where(lane == 0, hym[z], _roll(v, 1, 1)),
        jnp.where(lane == y - 1, hyp[z], _roll(v, y - 1, 1)),
    )


def _field_at(ref, f, z, nz):
    zm = jnp.maximum(z - 1, 0)
    zp = jnp.minimum(z + 1, nz - 1)
    vm = jnp.where(z > 0, 1.0, 0.0).astype(F32)
    vp = jnp.where(z < nz - 1, 1.0, 0.0).astype(F32)
    return ref[f, z], ref[f, zm] * vm, ref[f, zp] * vp, vm, vp


def _gains(b):
    return 1.5 + b, 1.5 + 0.5 * b


def _step_body(s_ref, sh, cs, o_ref, nz, masks):
    def body(z, carry):
        u, u_m, u_p, vm, vp = _field_at(s_ref, 0, z, nz)
        t, t_m, t_p, _, _ = _field_at(s_ref, 1, z, nz)
        c = [cs[k] for k in range(NCOEF)]
        g1, g2 = _gains(jnp.tanh(u))
        kw, dtv, lamb, kv = c[0] * g1, c[1] * g2, c[2] * g2, c[3] * g1
        a1 = jnp.zeros_like(u)
        a2 = jnp.zeros_like(u)
        for un, tn, valid in ((u_m, t_m, vm), (u_p, t_p, vp)):
            g1n, g2n = _gains(jnp.tanh(un))
            a1 = a1 + (g1 + valid * g1n) * (un - u)
            a2 = a2 + (g2 + valid * g2n) * (tn - t)
        f0 = c[0] * a1 + c[1] * a2
        f1 = c[2] * a2 + c[3] * a1
        uns = _neighbours(u, z, sh[0], masks)
        tns = _neighbours(t, z, sh[1], masks)
        for d in range(4):
            un, tn = uns[d], tns[d]
            g1n, g2n = _gains(jnp.tanh(un))
            cn = [cs[4 + 4 * d + k] for k in range(NCOEF)]
            du = un - u
            dt = tn - t
            f0 = f0 + (kw + cn[0] * g1n) * du + (dtv + cn[1] * g2n) * dt
            f1 = f1 + (lamb + cn[2] * g2n) * dt + (kv + cn[3] * g1n) * du
        o_ref[0, z] = u + 0.5 * f0
        o_ref[1, z] = t + 0.5 * f1
        return carry

    lax.fori_loop(0, nz, body, 0, unroll=UNROLL)


def _adjoint_body(s_ref, sh, a_ref, ah, cs, o_ref, nz, masks):
    def body(z, carry):
        u, u_m, u_p, vm, vp = _field_at(s_ref, 0, z, nz)
        t, t_m, t_p, _, _ = _field_at(s_ref, 1, z, nz)
        a0, a0_m, a0_p, _, _ = _field_at(a_ref, 0, z, nz)
        a1, a1_m, a1_p, _, _ = _field_at(a_ref, 1, z, nz)
        c = [cs[k] for k in range(NCOEF)]
        b = jnp.tanh(u)
        g1, g2 = _gains(b)
        kw, dtv, lamb, kv = c[0] * g1, c[1] * g2, c[2] * g2, c[3] * g1
        zero = jnp.zeros_like(u)
        p10, p11, p20, p21 = zero, zero, zero, zero
        gu0, gu1, gt0, gt1 = zero, zero, zero, zero
        for un, tn, a0n, a1n, valid in ((u_m, t_m, a0_m, a1_m, vm), (u_p, t_p, a0_p, a1_p, vp)):
            g1n, g2n = _gains(jnp.tanh(un))
            s1 = g1 + valid * g1n
            s2 = g2 + valid * g2n
            du, dt, da0, da1 = un - u, tn - t, a0n - a0, a1n - a1
            p10 = p10 + s1 * da0
            p11 = p11 + s1 * da1
            p20 = p20 + s2 * da0
            p21 = p21 + s2 * da1
            gu0 = gu0 + du * da0
            gu1 = gu1 + du * da1
            gt0 = gt0 + dt * da0
            gt1 = gt1 + dt * da1
        ju = c[0] * p10 + c[3] * p11
        jt = c[1] * p20 + c[2] * p21
        uns = _neighbours(u, z, sh[0], masks)
        tns = _neighbours(t, z, sh[1], masks)
        a0ns = _neighbours(a0, z, ah[0], masks)
        a1ns = _neighbours(a1, z, ah[1], masks)
        for d in range(4):
            un, tn, a0n, a1n = uns[d], tns[d], a0ns[d], a1ns[d]
            g1n, g2n = _gains(jnp.tanh(un))
            cn = [cs[4 + 4 * d + k] for k in range(NCOEF)]
            du, dt, da0, da1 = un - u, tn - t, a0n - a0, a1n - a1
            ju = ju + (kw + cn[0] * g1n) * da0 + (kv + cn[3] * g1n) * da1
            jt = jt + (dtv + cn[1] * g2n) * da0 + (lamb + cn[2] * g2n) * da1
            gu0 = gu0 + du * da0
            gu1 = gu1 + du * da1
            gt0 = gt0 + dt * da0
            gt1 = gt1 + dt * da1
        gsum = c[0] * gu0 + c[3] * gu1 + 0.5 * (c[1] * gt0 + c[2] * gt1)
        o_ref[0, z] = a0 + 0.5 * ju - 0.5 * (1.0 - b * b) * gsum
        o_ref[1, z] = a1 + 0.5 * jt
        return carry

    lax.fori_loop(0, nz, body, 0, unroll=UNROLL)


def _halo_scratch(nf, nz, x, y):
    return [pltpu.VMEM((nf, nz, x, y), F32) for _ in range(4)]


def _edge_shapes(rows, x, y):
    return (
        jax.ShapeDtypeStruct((rows, y), F32),
        jax.ShapeDtypeStruct((rows, y), F32),
        jax.ShapeDtypeStruct((x, y), F32),
        jax.ShapeDtypeStruct((x, y), F32),
    )


def _rows(n):
    return -(-n // 8) * 8


def prep_call(soil_class, soil_table, cot, slab, scales):
    nf, nz, x, y = cot.shape
    nclass = soil_table.shape[0]
    nplanes = nf * nz

    def kernel(cls_ref, tab_ref, sc_ref, cot_ref, slab_ref, coef_ref, xf_ref, xl_ref, yf_ref, yl_ref):
        cls = cls_ref[...]
        coefs = []
        for k in range(NCOEF):
            cv = jnp.zeros(cls.shape, F32)
            for j in range(nclass):
                cv = jnp.where(cls == j, tab_ref[j, k], cv)
            coef_ref[k] = cv
            coefs.append(cv)
        vals = [cot_ref[f, z] for f in range(nf) for z in range(nz)] + coefs
        _pack_edges(vals, xf_ref, xl_ref, yf_ref, yl_ref)
        base = len(vals)
        for k in range(nplanes):
            v = slab_ref[k // nz, k % nz].astype(F32)
            xf_ref[base + k : base + k + 1, :] = v[0:1, :]
            xl_ref[base + k : base + k + 1, :] = v[x - 1 : x, :]
        _, lane = _iotas((1, y))
        row = jnp.zeros((1, y), F32)
        for k in range(nplanes):
            row = jnp.where(lane == k, sc_ref[k], row)
        xf_ref[base + nplanes : base + nplanes + 1, :] = row
        xl_ref[base + nplanes : base + nplanes + 1, :] = row

    rows = _rows(2 * nplanes + NCOEF + 1)
    return pl.pallas_call(
        kernel,
        out_shape=(jax.ShapeDtypeStruct((NCOEF, x, y), F32),)
        + _edge_shapes(rows, x, y)[:2]
        + _edge_shapes(8, x, y)[2:],
        in_specs=[
            pl.BlockSpec(memory_space=VMEM),
            pl.BlockSpec(memory_space=SMEM),
            pl.BlockSpec(memory_space=SMEM),
            pl.BlockSpec(memory_space=VMEM),
            pl.BlockSpec(memory_space=VMEM),
        ],
    )(soil_class, soil_table, scales, cot, slab)


def state0_call(pieces, scales, nf, per):
    npiece, _, x, y = pieces.shape
    nplanes = npiece * per
    nz = nplanes // nf

    def kernel(sc_ref, r_ref, s_ref, xm_ref, xp_ref, ym_ref, yp_ref):
        _, lane = _iotas((x, y))
        ym = jnp.zeros((x, y), F32)
        yp = jnp.zeros((x, y), F32)
        for k in range(nplanes):
            p, i = k // per, k % per
            s_ref[k // nz, k % nz] = r_ref[p, i].astype(F32) * sc_ref[k]
            hx = r_ref[p, per].astype(F32)
            xm_ref[k : k + 1, :] = hx[i : i + 1, :] * sc_ref[nplanes + k]
            xp_ref[k : k + 1, :] = hx[per + i : per + i + 1, :] * sc_ref[2 * nplanes + k]
            hy = r_ref[p, per + 2].astype(F32)
            ym = jnp.where(lane == k, _roll(hy, k - i, 1) * sc_ref[3 * nplanes + k], ym)
            yp = jnp.where(lane == k, _roll(hy, k - (per + i), 1) * sc_ref[4 * nplanes + k], yp)
        ym_ref[...] = ym
        yp_ref[...] = yp

    return pl.pallas_call(
        kernel,
        out_shape=(jax.ShapeDtypeStruct((nf, nz, x, y), F32),) + _edge_shapes(nplanes, x, y),
        in_specs=[pl.BlockSpec(memory_space=SMEM), pl.BlockSpec(memory_space=VMEM)],
    )(scales, pieces)


def step_call(s, s_halo, coef, c_halo, c_first, with_edges):
    nf, nz, x, y = s.shape

    def kernel(*refs):
        s_ref, sxm, sxp, sym, syp, c_ref, cxm, cxp, cym, cyp = refs[:10]
        rest = refs[10:]
        if with_edges:
            o_ref, xf_ref, xl_ref, yf_ref, yl_ref = rest[:5]
            scratch = rest[5:]
        else:
            o_ref = rest[0]
            scratch = rest[1:]
        sh_all = scratch[0:4]
        cs = scratch[4]
        _expand_halo(sxm, sxp, sym, syp, 0, nf, nz, sh_all)
        _coef_table(c_ref, cxm, cxp, cym, cyp, c_first, cs)
        masks = _iotas((x, y))
        sh = [tuple(h.at[f] for h in sh_all) for f in range(nf)]
        _step_body(s_ref, sh, cs, o_ref, nz, masks)
        if with_edges:
            vals = [o_ref[f, z] for f in range(nf) for z in range(nz)]
            _pack_edges(vals, xf_ref, xl_ref, yf_ref, yl_ref)

    out_shape = (jax.ShapeDtypeStruct(s.shape, F32),)
    if with_edges:
        out_shape = out_shape + _edge_shapes(_rows(nf * nz), x, y)
    res = pl.pallas_call(
        kernel,
        out_shape=out_shape,
        scratch_shapes=_halo_scratch(nf, nz, x, y) + [pltpu.VMEM((5 * NCOEF, x, y), F32)],
    )(s, *s_halo, coef, *c_halo)
    return res if with_edges else res[0]


def adjoint_call(s, s_halo, a, a_halo, a_first, coef, c_halo, c_first, with_edges):
    nf, nz, x, y = s.shape

    def kernel(*refs):
        s_ref, sxm, sxp, sym, syp, a_ref, axm, axp, aym, ayp, c_ref, cxm, cxp, cym, cyp = refs[:15]
        rest = refs[15:]
        if with_edges:
            o_ref, xf_ref, xl_ref, yf_ref, yl_ref = rest[:5]
            scratch = rest[5:]
        else:
            o_ref = rest[0]
            scratch = rest[1:]
        sh_all = scratch[0:4]
        ah_all = scratch[4:8]
        cs = scratch[8]
        _expand_halo(sxm, sxp, sym, syp, 0, nf, nz, sh_all)
        _expand_halo(axm, axp, aym, ayp, a_first, nf, nz, ah_all)
        _coef_table(c_ref, cxm, cxp, cym, cyp, c_first, cs)
        masks = _iotas((x, y))
        sh = [tuple(h.at[f] for h in sh_all) for f in range(nf)]
        ah = [tuple(h.at[f] for h in ah_all) for f in range(nf)]
        _adjoint_body(s_ref, sh, a_ref, ah, cs, o_ref, nz, masks)
        if with_edges:
            vals = [o_ref[f, z] for f in range(nf) for z in range(nz)]
            _pack_edges(vals, xf_ref, xl_ref, yf_ref, yl_ref)

    out_shape = (jax.ShapeDtypeStruct(s.shape, F32),)
    if with_edges:
        out_shape = out_shape + _edge_shapes(_rows(nf * nz), x, y)
    res = pl.pallas_call(
        kernel,
        out_shape=out_shape,
        scratch_shapes=_halo_scratch(nf, nz, x, y)
        + _halo_scratch(nf, nz, x, y)
        + [pltpu.VMEM((5 * NCOEF, x, y), F32)],
    )(s, *s_halo, a, *a_halo, coef, *c_halo)
    return res if with_edges else res[0]


def _shift(v, axis, step):
    n = lax.axis_size(axis)
    if step > 0:
        pairs = [(i, i + 1) for i in range(n - 1)]
    else:
        pairs = [(i + 1, i) for i in range(n - 1)]
    return lax.ppermute(v, axis, pairs)


def exchange(xf, xl, yf, yl):
    return (
        _shift(xl, "gx", 1),
        _shift(xf, "gx", -1),
        _shift(yl, "gy", 1),
        _shift(yf, "gy", -1),
    )


def route_blocks(stored_slab, block_scales, holder, xm_all, xp_all, first):
    nf, nz, x, y = stored_slab.shape
    n = lax.axis_size("gy")
    nplanes = nf * nz
    per = nplanes // n
    bf = stored_slab.dtype
    slab = stored_slab.reshape(n, per, x, y)
    rows_m = xm_all[first : first + nplanes].astype(bf).reshape(n, per, y)
    rows_p = xp_all[first : first + nplanes].astype(bf).reshape(n, per, y)
    halo = jnp.concatenate([rows_m, rows_p], axis=1)[:, None]
    sc_m = xm_all[first + nplanes, :nplanes].astype(bf).reshape(n, 1, per)
    sc_p = xp_all[first + nplanes, :nplanes].astype(bf).reshape(n, 1, per)
    sc = jnp.concatenate([block_scales.reshape(n, 1, per), sc_m, sc_p], axis=1)
    sc = jnp.pad(sc, ((0, 0), (0, x - 3), (0, y - per)))[:, None]
    held = lax.all_to_all(jnp.concatenate([slab, halo, sc], axis=1), "gy", 0, 0, tiled=True)

    g = jnp.arange(n, dtype=jnp.int32)
    left = jnp.take(holder, jnp.maximum(g - 1, 0))
    right = jnp.take(holder, jnp.minimum(g + 1, n - 1))
    has_l = (g > 0)[:, None, None]
    has_r = (g < n - 1)[:, None, None]
    zero = jnp.zeros((), bf)
    cols_l = jnp.where(has_l, jnp.take(held[:, :per, :, y - 1], left, axis=0), zero)
    cols_r = jnp.where(has_r, jnp.take(held[:, :per, :, 0], right, axis=0), zero)
    scl_l = jnp.where(has_l, jnp.take(held[:, per + 1, 0:1, :per], left, axis=0), zero)
    scl_r = jnp.where(has_r, jnp.take(held[:, per + 1, 0:1, :per], right, axis=0), zero)
    cols = jnp.concatenate([cols_l, cols_r], axis=1).transpose(0, 2, 1)
    scl = jnp.concatenate([scl_l, scl_r], axis=2)
    yplane = jnp.concatenate(
        [
            jnp.pad(cols, ((0, 0), (0, 0), (0, y - 2 * per))),
            jnp.pad(scl, ((0, 0), (0, x - 1), (0, y - 2 * per))),
        ],
        axis=1,
    )
    forward = jnp.concatenate([jnp.take(held, holder, axis=0), yplane.reshape(n, 2, x, y)], axis=1)
    return lax.all_to_all(forward, "gy", 0, 0, tiled=True)


def on_device(stored_slab, block_scales, holder, soil_class, soil_table, cotangent):
    nf, nz, x, y = stored_slab.shape
    nplanes = nf * nz

    coef, cxf, cxl, cyf, cyl = prep_call(
        soil_class, soil_table, cotangent, stored_slab, block_scales.reshape(-1).astype(F32)
    )
    c_halo = exchange(cxf, cxl, cyf, cyl)
    c_first = nplanes

    pieces = route_blocks(stored_slab, block_scales, holder, c_halo[0], c_halo[1], nplanes + NCOEF)
    per = nplanes // pieces.shape[0]
    scales = jnp.concatenate(
        [
            pieces[:, per + 1, 0:3, :per].transpose(1, 0, 2).reshape(3, nplanes),
            pieces[:, per + 3, 0, : 2 * per].reshape(-1, 2, per).transpose(1, 0, 2).reshape(2, nplanes),
        ]
    ).astype(F32).reshape(-1)
    s0, *s0_halo = state0_call(pieces, scales, nf, per)

    s1, *s1_edges = step_call(s0, s0_halo, coef, c_halo, c_first, True)
    s1_halo = exchange(*s1_edges)

    a1, *a1_edges = adjoint_call(
        s1, s1_halo, cotangent, c_halo, 0, coef, c_halo, c_first, True
    )
    a1_halo = exchange(*a1_edges)
    s2 = step_call(s1, s1_halo, coef, c_halo, c_first, False)

    sens = adjoint_call(s0, s0_halo, a1, a1_halo, 0, coef, c_halo, c_first, False)
    return (s2, sens)


def solution(mesh):
    placed = (
        P(None, None, "gx", "gy"),
        P(None, None, "gx", "gy"),
        P(),
        P("gx", "gy"),
        P(),
        P(None, None, "gx", "gy"),
    )
    return jax.shard_map(
        on_device,
        mesh=mesh,
        in_specs=placed,
        out_specs=(P(None, None, "gx", "gy"), P(None, None, "gx", "gy")),
        check_vma=False,
    )
```

```python
import jax
import jax.numpy as jnp
from jax import lax
from jax.experimental import pallas as pl
from jax.experimental.pallas import tpu as pltpu
from jax.sharding import PartitionSpec as P

F32 = jnp.float32
NCOEF = 4
UNROLL = 4
VMEM = pltpu.MemorySpace.VMEM
SMEM = pltpu.MemorySpace.SMEM


def _roll(v, shift, axis):
    shift = shift % v.shape[axis]
    if shift == 0:
        return v
    return pltpu.roll(v, shift, axis)


def _iotas(shape):
    return lax.broadcasted_iota(jnp.int32, shape, 0), lax.broadcasted_iota(jnp.int32, shape, 1)


def _pack_edges(vals, xf_ref, xl_ref, yf_ref, yl_ref):
    x, y = vals[0].shape
    _, lane = _iotas((x, y))
    xf_ref[...] = jnp.zeros(xf_ref.shape, F32)
    xl_ref[...] = jnp.zeros(xl_ref.shape, F32)
    yf = jnp.zeros((x, y), F32)
    yl = jnp.zeros((x, y), F32)
    for k, v in enumerate(vals):
        xf_ref[k : k + 1, :] = v[0:1, :]
        xl_ref[k : k + 1, :] = v[x - 1 : x, :]
        yf = jnp.where(lane == k, _roll(v, k, 1), yf)
        yl = jnp.where(lane == k, _roll(v, k - (y - 1), 1), yl)
    yf_ref[...] = yf
    yl_ref[...] = yl


def _expand_halo(xm_ref, xp_ref, ym_ref, yp_ref, first, nf, nz, dst):
    hxm, hxp, hym, hyp = dst
    x, y = hxm.shape[2], hxm.shape[3]
    ymv = ym_ref[...]
    ypv = yp_ref[...]
    for f in range(nf):
        for z in range(nz):
            k = first + f * nz + z
            hxm[f, z] = jnp.broadcast_to(xm_ref[k : k + 1, :], (x, y))
            hxp[f, z] = jnp.broadcast_to(xp_ref[k : k + 1, :], (x, y))
            hym[f, z] = _roll(ymv, -k, 1)
            hyp[f, z] = _roll(ypv, (y - 1) - k, 1)


def _coef_table(c_ref, cxm_ref, cxp_ref, cym_ref, cyp_ref, first, cs):
    x, y = c_ref.shape[1], c_ref.shape[2]
    ymv = cym_ref[...]
    ypv = cyp_ref[...]
    masks = _iotas((x, y))
    for k in range(NCOEF):
        r = first + k
        cv = c_ref[k]
        cs[k] = cv
        halo = (
            jnp.broadcast_to(cxm_ref[r : r + 1, :], (x, y)),
            jnp.broadcast_to(cxp_ref[r : r + 1, :], (x, y)),
            _roll(ymv, -r, 1),
            _roll(ypv, (y - 1) - r, 1),
        )
        for d, v in enumerate(_neighbours(cv, 0, [h[None] for h in halo], masks)):
            cs[4 + 4 * d + k] = v


def _neighbours(v, z, h, masks):
    row, lane = masks
    x, y = v.shape
    hxm, hxp, hym, hyp = h
    return (
        jnp.where(row == 0, hxm[z], _roll(v, 1, 0)),
        jnp.where(row == x - 1, hxp[z], _roll(v, x - 1, 0)),
        jnp.where(lane == 0, hym[z], _roll(v, 1, 1)),
        jnp.where(lane == y - 1, hyp[z], _roll(v, y - 1, 1)),
    )


def _field_at(ref, f, z, nz):
    zm = jnp.maximum(z - 1, 0)
    zp = jnp.minimum(z + 1, nz - 1)
    vm = jnp.where(z > 0, 1.0, 0.0).astype(F32)
    vp = jnp.where(z < nz - 1, 1.0, 0.0).astype(F32)
    return ref[f, z], ref[f, zm] * vm, ref[f, zp] * vp, vm, vp


def _gains(b):
    return 1.5 + b, 1.5 + 0.5 * b


def _step_body(s_ref, sh, cs, o_ref, nz, masks):
    def body(z, carry):
        u, u_m, u_p, vm, vp = _field_at(s_ref, 0, z, nz)
        t, t_m, t_p, _, _ = _field_at(s_ref, 1, z, nz)
        c = [cs[k] for k in range(NCOEF)]
        g1, g2 = _gains(jnp.tanh(u))
        kw, dtv, lamb, kv = c[0] * g1, c[1] * g2, c[2] * g2, c[3] * g1
        a1 = jnp.zeros_like(u)
        a2 = jnp.zeros_like(u)
        for un, tn, valid in ((u_m, t_m, vm), (u_p, t_p, vp)):
            g1n, g2n = _gains(jnp.tanh(un))
            a1 = a1 + (g1 + valid * g1n) * (un - u)
            a2 = a2 + (g2 + valid * g2n) * (tn - t)
        f0 = c[0] * a1 + c[1] * a2
        f1 = c[2] * a2 + c[3] * a1
        uns = _neighbours(u, z, sh[0], masks)
        tns = _neighbours(t, z, sh[1], masks)
        for d in range(4):
            un, tn = uns[d], tns[d]
            g1n, g2n = _gains(jnp.tanh(un))
            cn = [cs[4 + 4 * d + k] for k in range(NCOEF)]
            du = un - u
            dt = tn - t
            f0 = f0 + (kw + cn[0] * g1n) * du + (dtv + cn[1] * g2n) * dt
            f1 = f1 + (lamb + cn[2] * g2n) * dt + (kv + cn[3] * g1n) * du
        o_ref[0, z] = u + 0.5 * f0
        o_ref[1, z] = t + 0.5 * f1
        return carry

    lax.fori_loop(0, nz, body, 0, unroll=UNROLL)


def _adjoint_body(s_ref, sh, a_ref, ah, cs, o_ref, nz, masks):
    def body(z, carry):
        u, u_m, u_p, vm, vp = _field_at(s_ref, 0, z, nz)
        t, t_m, t_p, _, _ = _field_at(s_ref, 1, z, nz)
        a0, a0_m, a0_p, _, _ = _field_at(a_ref, 0, z, nz)
        a1, a1_m, a1_p, _, _ = _field_at(a_ref, 1, z, nz)
        c = [cs[k] for k in range(NCOEF)]
        b = jnp.tanh(u)
        g1, g2 = _gains(b)
        kw, dtv, lamb, kv = c[0] * g1, c[1] * g2, c[2] * g2, c[3] * g1
        zero = jnp.zeros_like(u)
        p10, p11, p20, p21 = zero, zero, zero, zero
        gu0, gu1, gt0, gt1 = zero, zero, zero, zero
        for un, tn, a0n, a1n, valid in ((u_m, t_m, a0_m, a1_m, vm), (u_p, t_p, a0_p, a1_p, vp)):
            g1n, g2n = _gains(jnp.tanh(un))
            s1 = g1 + valid * g1n
            s2 = g2 + valid * g2n
            du, dt, da0, da1 = un - u, tn - t, a0n - a0, a1n - a1
            p10 = p10 + s1 * da0
            p11 = p11 + s1 * da1
            p20 = p20 + s2 * da0
            p21 = p21 + s2 * da1
            gu0 = gu0 + du * da0
            gu1 = gu1 + du * da1
            gt0 = gt0 + dt * da0
            gt1 = gt1 + dt * da1
        ju = c[0] * p10 + c[3] * p11
        jt = c[1] * p20 + c[2] * p21
        uns = _neighbours(u, z, sh[0], masks)
        tns = _neighbours(t, z, sh[1], masks)
        a0ns = _neighbours(a0, z, ah[0], masks)
        a1ns = _neighbours(a1, z, ah[1], masks)
        for d in range(4):
            un, tn, a0n, a1n = uns[d], tns[d], a0ns[d], a1ns[d]
            g1n, g2n = _gains(jnp.tanh(un))
            cn = [cs[4 + 4 * d + k] for k in range(NCOEF)]
            du, dt, da0, da1 = un - u, tn - t, a0n - a0, a1n - a1
            ju = ju + (kw + cn[0] * g1n) * da0 + (kv + cn[3] * g1n) * da1
            jt = jt + (dtv + cn[1] * g2n) * da0 + (lamb + cn[2] * g2n) * da1
            gu0 = gu0 + du * da0
            gu1 = gu1 + du * da1
            gt0 = gt0 + dt * da0
            gt1 = gt1 + dt * da1
        gsum = c[0] * gu0 + c[3] * gu1 + 0.5 * (c[1] * gt0 + c[2] * gt1)
        o_ref[0, z] = a0 + 0.5 * ju - 0.5 * (1.0 - b * b) * gsum
        o_ref[1, z] = a1 + 0.5 * jt
        return carry

    lax.fori_loop(0, nz, body, 0, unroll=UNROLL)


def _halo_scratch(nf, nz, x, y):
    return [pltpu.VMEM((nf, nz, x, y), F32) for _ in range(4)]


def _edge_shapes(rows, x, y):
    return (
        jax.ShapeDtypeStruct((rows, y), F32),
        jax.ShapeDtypeStruct((rows, y), F32),
        jax.ShapeDtypeStruct((x, y), F32),
        jax.ShapeDtypeStruct((x, y), F32),
    )


def _rows(n):
    return -(-n // 8) * 8


def prep_call(soil_class, soil_table, cot):
    nf, nz, x, y = cot.shape
    nclass = soil_table.shape[0]

    def kernel(cls_ref, tab_ref, cot_ref, coef_ref, xf_ref, xl_ref, yf_ref, yl_ref):
        cls = cls_ref[...]
        coefs = []
        for k in range(NCOEF):
            cv = jnp.zeros(cls.shape, F32)
            for j in range(nclass):
                cv = jnp.where(cls == j, tab_ref[j, k], cv)
            coef_ref[k] = cv
            coefs.append(cv)
        vals = [cot_ref[f, z] for f in range(nf) for z in range(nz)] + coefs
        _pack_edges(vals, xf_ref, xl_ref, yf_ref, yl_ref)

    rows = _rows(nf * nz + NCOEF)
    return pl.pallas_call(
        kernel,
        out_shape=(jax.ShapeDtypeStruct((NCOEF, x, y), F32),) + _edge_shapes(rows, x, y),
        in_specs=[
            pl.BlockSpec(memory_space=VMEM),
            pl.BlockSpec(memory_space=SMEM),
            pl.BlockSpec(memory_space=VMEM),
        ],
    )(soil_class, soil_table, cot)


def state0_call(pieces, scales, nf, per):
    npiece, _, x, y = pieces.shape
    nplanes = npiece * per
    nz = nplanes // nf

    def kernel(sc_ref, r_ref, s_ref, xm_ref, xp_ref, ym_ref, yp_ref):
        _, lane = _iotas((x, y))
        ym = jnp.zeros((x, y), F32)
        yp = jnp.zeros((x, y), F32)
        for k in range(nplanes):
            p, i = k // per, k % per
            s_ref[k // nz, k % nz] = r_ref[p, i].astype(F32) * sc_ref[k]
            hx = r_ref[p, per].astype(F32)
            xm_ref[k : k + 1, :] = hx[i : i + 1, :] * sc_ref[nplanes + k]
            xp_ref[k : k + 1, :] = hx[per + i : per + i + 1, :] * sc_ref[2 * nplanes + k]
            hy = r_ref[p, per + 2].astype(F32)
            ym = jnp.where(lane == k, _roll(hy, k - i, 1) * sc_ref[3 * nplanes + k], ym)
            yp = jnp.where(lane == k, _roll(hy, k - (per + i), 1) * sc_ref[4 * nplanes + k], yp)
        ym_ref[...] = ym
        yp_ref[...] = yp

    return pl.pallas_call(
        kernel,
        out_shape=(jax.ShapeDtypeStruct((nf, nz, x, y), F32),) + _edge_shapes(nplanes, x, y),
        in_specs=[pl.BlockSpec(memory_space=SMEM), pl.BlockSpec(memory_space=VMEM)],
    )(scales, pieces)


def step_call(s, s_halo, coef, c_halo, c_first, with_edges):
    nf, nz, x, y = s.shape

    def kernel(*refs):
        s_ref, sxm, sxp, sym, syp, c_ref, cxm, cxp, cym, cyp = refs[:10]
        rest = refs[10:]
        if with_edges:
            o_ref, xf_ref, xl_ref, yf_ref, yl_ref = rest[:5]
            scratch = rest[5:]
        else:
            o_ref = rest[0]
            scratch = rest[1:]
        sh_all = scratch[0:4]
        cs = scratch[4]
        _expand_halo(sxm, sxp, sym, syp, 0, nf, nz, sh_all)
        _coef_table(c_ref, cxm, cxp, cym, cyp, c_first, cs)
        masks = _iotas((x, y))
        sh = [tuple(h.at[f] for h in sh_all) for f in range(nf)]
        _step_body(s_ref, sh, cs, o_ref, nz, masks)
        if with_edges:
            vals = [o_ref[f, z] for f in range(nf) for z in range(nz)]
            _pack_edges(vals, xf_ref, xl_ref, yf_ref, yl_ref)

    out_shape = (jax.ShapeDtypeStruct(s.shape, F32),)
    if with_edges:
        out_shape = out_shape + _edge_shapes(_rows(nf * nz), x, y)
    res = pl.pallas_call(
        kernel,
        out_shape=out_shape,
        scratch_shapes=_halo_scratch(nf, nz, x, y) + [pltpu.VMEM((5 * NCOEF, x, y), F32)],
    )(s, *s_halo, coef, *c_halo)
    return res if with_edges else res[0]


def adjoint_call(s, s_halo, a, a_halo, a_first, coef, c_halo, c_first, with_edges):
    nf, nz, x, y = s.shape

    def kernel(*refs):
        s_ref, sxm, sxp, sym, syp, a_ref, axm, axp, aym, ayp, c_ref, cxm, cxp, cym, cyp = refs[:15]
        rest = refs[15:]
        if with_edges:
            o_ref, xf_ref, xl_ref, yf_ref, yl_ref = rest[:5]
            scratch = rest[5:]
        else:
            o_ref = rest[0]
            scratch = rest[1:]
        sh_all = scratch[0:4]
        ah_all = scratch[4:8]
        cs = scratch[8]
        _expand_halo(sxm, sxp, sym, syp, 0, nf, nz, sh_all)
        _expand_halo(axm, axp, aym, ayp, a_first, nf, nz, ah_all)
        _coef_table(c_ref, cxm, cxp, cym, cyp, c_first, cs)
        masks = _iotas((x, y))
        sh = [tuple(h.at[f] for h in sh_all) for f in range(nf)]
        ah = [tuple(h.at[f] for h in ah_all) for f in range(nf)]
        _adjoint_body(s_ref, sh, a_ref, ah, cs, o_ref, nz, masks)
        if with_edges:
            vals = [o_ref[f, z] for f in range(nf) for z in range(nz)]
            _pack_edges(vals, xf_ref, xl_ref, yf_ref, yl_ref)

    out_shape = (jax.ShapeDtypeStruct(s.shape, F32),)
    if with_edges:
        out_shape = out_shape + _edge_shapes(_rows(nf * nz), x, y)
    res = pl.pallas_call(
        kernel,
        out_shape=out_shape,
        scratch_shapes=_halo_scratch(nf, nz, x, y)
        + _halo_scratch(nf, nz, x, y)
        + [pltpu.VMEM((5 * NCOEF, x, y), F32)],
    )(s, *s_halo, a, *a_halo, coef, *c_halo)
    return res if with_edges else res[0]


def _shift(v, axis, step):
    n = lax.axis_size(axis)
    if step > 0:
        pairs = [(i, i + 1) for i in range(n - 1)]
    else:
        pairs = [(i + 1, i) for i in range(n - 1)]
    return lax.ppermute(v, axis, pairs)


def exchange(xf, xl, yf, yl):
    return (
        _shift(xl, "gx", 1),
        _shift(xf, "gx", -1),
        _shift(yl, "gy", 1),
        _shift(yf, "gy", -1),
    )


def route_blocks(stored_slab, block_scales, holder, xm_all, xp_all, first):
    nf, nz, x, y = stored_slab.shape
    n = lax.axis_size("gy")
    nplanes = nf * nz
    per = nplanes // n
    bf = stored_slab.dtype
    slab = stored_slab.reshape(n, per, x, y)
    rows_m = xm_all[first : first + nplanes].astype(bf).reshape(n, per, y)
    rows_p = xp_all[first : first + nplanes].astype(bf).reshape(n, per, y)
    halo = jnp.concatenate([rows_m, rows_p], axis=1)[:, None]
    sc_m = xm_all[first + nplanes, :nplanes].astype(bf).reshape(n, 1, per)
    sc_p = xp_all[first + nplanes, :nplanes].astype(bf).reshape(n, 1, per)
    sc = jnp.concatenate([block_scales.reshape(n, 1, per), sc_m, sc_p], axis=1)
    sc = jnp.pad(sc, ((0, 0), (0, x - 3), (0, y - per)))[:, None]
    held = lax.all_to_all(jnp.concatenate([slab, halo, sc], axis=1), "gy", 0, 0, tiled=True)

    g = jnp.arange(n, dtype=jnp.int32)
    left = jnp.take(holder, jnp.maximum(g - 1, 0))
    right = jnp.take(holder, jnp.minimum(g + 1, n - 1))
    has_l = (g > 0)[:, None, None]
    has_r = (g < n - 1)[:, None, None]
    zero = jnp.zeros((), bf)
    cols_l = jnp.where(has_l, jnp.take(held[:, :per, :, y - 1], left, axis=0), zero)
    cols_r = jnp.where(has_r, jnp.take(held[:, :per, :, 0], right, axis=0), zero)
    scl_l = jnp.where(has_l, jnp.take(held[:, per + 1, 0:1, :per], left, axis=0), zero)
    scl_r = jnp.where(has_r, jnp.take(held[:, per + 1, 0:1, :per], right, axis=0), zero)
    cols = jnp.concatenate([cols_l, cols_r], axis=1).transpose(0, 2, 1)
    scl = jnp.concatenate([scl_l, scl_r], axis=2)
    yplane = jnp.concatenate(
        [
            jnp.pad(cols, ((0, 0), (0, 0), (0, y - 2 * per))),
            jnp.pad(scl, ((0, 0), (0, x - 1), (0, y - 2 * per))),
        ],
        axis=1,
    )
    forward = jnp.concatenate([jnp.take(held, holder, axis=0), yplane.reshape(n, 2, x, y)], axis=1)
    return lax.all_to_all(forward, "gy", 0, 0, tiled=True)


def slab_edges(stored_slab, block_scales):
    nf, nz, x, y = stored_slab.shape
    nplanes = nf * nz
    sc = jnp.pad(block_scales.reshape(1, nplanes), ((0, 7), (0, y - nplanes)))
    first = jnp.concatenate([stored_slab[:, :, 0, :].reshape(nplanes, y), sc], axis=0)
    last = jnp.concatenate([stored_slab[:, :, x - 1, :].reshape(nplanes, y), sc], axis=0)
    return first, last


def on_device(stored_slab, block_scales, holder, soil_class, soil_table, cotangent):
    nf, nz, x, y = stored_slab.shape
    nplanes = nf * nz

    sfirst, slast = slab_edges(stored_slab, block_scales)
    pieces = route_blocks(
        stored_slab, block_scales, holder, _shift(slast, "gx", 1), _shift(sfirst, "gx", -1), 0
    )

    coef, cxf, cxl, cyf, cyl = prep_call(soil_class, soil_table, cotangent)
    c_halo = exchange(cxf, cxl, cyf, cyl)
    c_first = nplanes

    per = nplanes // pieces.shape[0]
    scales = jnp.concatenate(
        [
            pieces[:, per + 1, 0:3, :per].transpose(1, 0, 2).reshape(3, nplanes),
            pieces[:, per + 3, 0, : 2 * per].reshape(-1, 2, per).transpose(1, 0, 2).reshape(2, nplanes),
        ]
    ).astype(F32).reshape(-1)
    s0, *s0_halo = state0_call(pieces, scales, nf, per)

    s1, *s1_edges = step_call(s0, s0_halo, coef, c_halo, c_first, True)
    s1_halo = exchange(*s1_edges)

    a1, *a1_edges = adjoint_call(
        s1, s1_halo, cotangent, c_halo, 0, coef, c_halo, c_first, True
    )
    a1_halo = exchange(*a1_edges)
    s2 = step_call(s1, s1_halo, coef, c_halo, c_first, False)

    sens = adjoint_call(s0, s0_halo, a1, a1_halo, 0, coef, c_halo, c_first, False)
    return (s2, sens)


def solution(mesh):
    placed = (
        P(None, None, "gx", "gy"),
        P(None, None, "gx", "gy"),
        P(),
        P("gx", "gy"),
        P(),
        P(None, None, "gx", "gy"),
    )
    return jax.shard_map(
        on_device,
        mesh=mesh,
        in_specs=placed,
        out_specs=(P(None, None, "gx", "gy"), P(None, None, "gx", "gy")),
        check_vma=False,
    )
```

```python
import jax
import jax.numpy as jnp
from jax import lax
from jax.experimental import pallas as pl
from jax.experimental.pallas import tpu as pltpu
from jax.sharding import PartitionSpec as P

F32 = jnp.float32
NCOEF = 4
UNROLL = 4
VMEM = pltpu.MemorySpace.VMEM
SMEM = pltpu.MemorySpace.SMEM


def _roll(v, shift, axis):
    shift = shift % v.shape[axis]
    if shift == 0:
        return v
    return pltpu.roll(v, shift, axis)


def _iotas(shape):
    return lax.broadcasted_iota(jnp.int32, shape, 0), lax.broadcasted_iota(jnp.int32, shape, 1)


def _pack_edges(vals, xf_ref, xl_ref, yf_ref, yl_ref):
    x, y = vals[0].shape
    _, lane = _iotas((x, y))
    xf_ref[...] = jnp.zeros(xf_ref.shape, F32)
    xl_ref[...] = jnp.zeros(xl_ref.shape, F32)
    yf = jnp.zeros((x, y), F32)
    yl = jnp.zeros((x, y), F32)
    for k, v in enumerate(vals):
        xf_ref[k : k + 1, :] = v[0:1, :]
        xl_ref[k : k + 1, :] = v[x - 1 : x, :]
        yf = jnp.where(lane == k, _roll(v, k, 1), yf)
        yl = jnp.where(lane == k, _roll(v, k - (y - 1), 1), yl)
    yf_ref[...] = yf
    yl_ref[...] = yl


def _expand_halo(xm_ref, xp_ref, ym_ref, yp_ref, first, nf, nz, dst):
    hxm, hxp, hym, hyp = dst
    x, y = hxm.shape[2], hxm.shape[3]
    ymv = ym_ref[...]
    ypv = yp_ref[...]
    for f in range(nf):
        for z in range(nz):
            k = first + f * nz + z
            hxm[f, z] = jnp.broadcast_to(xm_ref[k : k + 1, :], (x, y))
            hxp[f, z] = jnp.broadcast_to(xp_ref[k : k + 1, :], (x, y))
            hym[f, z] = _roll(ymv, -k, 1)
            hyp[f, z] = _roll(ypv, (y - 1) - k, 1)


def _coef_table(c_ref, cxm_ref, cxp_ref, cym_ref, cyp_ref, first, cs):
    x, y = c_ref.shape[1], c_ref.shape[2]
    ymv = cym_ref[...]
    ypv = cyp_ref[...]
    masks = _iotas((x, y))
    for k in range(NCOEF):
        r = first + k
        cv = c_ref[k]
        cs[k] = cv
        halo = (
            jnp.broadcast_to(cxm_ref[r : r + 1, :], (x, y)),
            jnp.broadcast_to(cxp_ref[r : r + 1, :], (x, y)),
            _roll(ymv, -r, 1),
            _roll(ypv, (y - 1) - r, 1),
        )
        for d, v in enumerate(_neighbours(cv, 0, [h[None] for h in halo], masks)):
            cs[4 + 4 * d + k] = v


def _neighbours(v, z, h, masks):
    row, lane = masks
    x, y = v.shape
    hxm, hxp, hym, hyp = h
    return (
        jnp.where(row == 0, hxm[z], _roll(v, 1, 0)),
        jnp.where(row == x - 1, hxp[z], _roll(v, x - 1, 0)),
        jnp.where(lane == 0, hym[z], _roll(v, 1, 1)),
        jnp.where(lane == y - 1, hyp[z], _roll(v, y - 1, 1)),
    )


def _field_at(ref, f, z, nz):
    zm = jnp.maximum(z - 1, 0)
    zp = jnp.minimum(z + 1, nz - 1)
    vm = jnp.where(z > 0, 1.0, 0.0).astype(F32)
    vp = jnp.where(z < nz - 1, 1.0, 0.0).astype(F32)
    return ref[f, z], ref[f, zm] * vm, ref[f, zp] * vp, vm, vp


def _gains(b):
    return 1.5 + b, 1.5 + 0.5 * b


def _step_body(s_ref, sh, cs, o_ref, nz, masks):
    def body(z, carry):
        u, u_m, u_p, vm, vp = _field_at(s_ref, 0, z, nz)
        t, t_m, t_p, _, _ = _field_at(s_ref, 1, z, nz)
        c = [cs[k] for k in range(NCOEF)]
        g1, g2 = _gains(jnp.tanh(u))
        kw, dtv, lamb, kv = c[0] * g1, c[1] * g2, c[2] * g2, c[3] * g1
        a1 = jnp.zeros_like(u)
        a2 = jnp.zeros_like(u)
        for un, tn, valid in ((u_m, t_m, vm), (u_p, t_p, vp)):
            g1n, g2n = _gains(jnp.tanh(un))
            a1 = a1 + (g1 + valid * g1n) * (un - u)
            a2 = a2 + (g2 + valid * g2n) * (tn - t)
        f0 = c[0] * a1 + c[1] * a2
        f1 = c[2] * a2 + c[3] * a1
        uns = _neighbours(u, z, sh[0], masks)
        tns = _neighbours(t, z, sh[1], masks)
        for d in range(4):
            un, tn = uns[d], tns[d]
            g1n, g2n = _gains(jnp.tanh(un))
            cn = [cs[4 + 4 * d + k] for k in range(NCOEF)]
            du = un - u
            dt = tn - t
            f0 = f0 + (kw + cn[0] * g1n) * du + (dtv + cn[1] * g2n) * dt
            f1 = f1 + (lamb + cn[2] * g2n) * dt + (kv + cn[3] * g1n) * du
        o_ref[0, z] = u + 0.5 * f0
        o_ref[1, z] = t + 0.5 * f1
        return carry

    lax.fori_loop(0, nz, body, 0, unroll=UNROLL)


def _adjoint_body(s_ref, sh, a_ref, ah, cs, o_ref, nz, masks):
    def body(z, carry):
        u, u_m, u_p, vm, vp = _field_at(s_ref, 0, z, nz)
        t, t_m, t_p, _, _ = _field_at(s_ref, 1, z, nz)
        a0, a0_m, a0_p, _, _ = _field_at(a_ref, 0, z, nz)
        a1, a1_m, a1_p, _, _ = _field_at(a_ref, 1, z, nz)
        c = [cs[k] for k in range(NCOEF)]
        b = jnp.tanh(u)
        g1, g2 = _gains(b)
        kw, dtv, lamb, kv = c[0] * g1, c[1] * g2, c[2] * g2, c[3] * g1
        zero = jnp.zeros_like(u)
        p10, p11, p20, p21 = zero, zero, zero, zero
        gu0, gu1, gt0, gt1 = zero, zero, zero, zero
        for un, tn, a0n, a1n, valid in ((u_m, t_m, a0_m, a1_m, vm), (u_p, t_p, a0_p, a1_p, vp)):
            g1n, g2n = _gains(jnp.tanh(un))
            s1 = g1 + valid * g1n
            s2 = g2 + valid * g2n
            du, dt, da0, da1 = un - u, tn - t, a0n - a0, a1n - a1
            p10 = p10 + s1 * da0
            p11 = p11 + s1 * da1
            p20 = p20 + s2 * da0
            p21 = p21 + s2 * da1
            gu0 = gu0 + du * da0
            gu1 = gu1 + du * da1
            gt0 = gt0 + dt * da0
            gt1 = gt1 + dt * da1
        ju = c[0] * p10 + c[3] * p11
        jt = c[1] * p20 + c[2] * p21
        uns = _neighbours(u, z, sh[0], masks)
        tns = _neighbours(t, z, sh[1], masks)
        a0ns = _neighbours(a0, z, ah[0], masks)
        a1ns = _neighbours(a1, z, ah[1], masks)
        for d in range(4):
            un, tn, a0n, a1n = uns[d], tns[d], a0ns[d], a1ns[d]
            g1n, g2n = _gains(jnp.tanh(un))
            cn = [cs[4 + 4 * d + k] for k in range(NCOEF)]
            du, dt, da0, da1 = un - u, tn - t, a0n - a0, a1n - a1
            ju = ju + (kw + cn[0] * g1n) * da0 + (kv + cn[3] * g1n) * da1
            jt = jt + (dtv + cn[1] * g2n) * da0 + (lamb + cn[2] * g2n) * da1
            gu0 = gu0 + du * da0
            gu1 = gu1 + du * da1
            gt0 = gt0 + dt * da0
            gt1 = gt1 + dt * da1
        gsum = c[0] * gu0 + c[3] * gu1 + 0.5 * (c[1] * gt0 + c[2] * gt1)
        o_ref[0, z] = a0 + 0.5 * ju - 0.5 * (1.0 - b * b) * gsum
        o_ref[1, z] = a1 + 0.5 * jt
        return carry

    lax.fori_loop(0, nz, body, 0, unroll=UNROLL)


def _halo_scratch(nf, nz, x, y):
    return [pltpu.VMEM((nf, nz, x, y), F32) for _ in range(4)]


def _edge_shapes(rows, x, y):
    return (
        jax.ShapeDtypeStruct((rows, y), F32),
        jax.ShapeDtypeStruct((rows, y), F32),
        jax.ShapeDtypeStruct((x, y), F32),
        jax.ShapeDtypeStruct((x, y), F32),
    )


def _rows(n):
    return -(-n // 8) * 8


def prep_call(soil_class, soil_table, cot, slab, scales):
    nf, nz, x, y = cot.shape
    nclass = soil_table.shape[0]
    nplanes = nf * nz

    def kernel(cls_ref, tab_ref, sc_ref, cot_ref, slab_ref, coef_ref, xf_ref, xl_ref, yf_ref, yl_ref):
        cls = cls_ref[...]
        coefs = []
        for k in range(NCOEF):
            cv = jnp.zeros(cls.shape, F32)
            for j in range(nclass):
                cv = jnp.where(cls == j, tab_ref[j, k], cv)
            coef_ref[k] = cv
            coefs.append(cv)
        vals = [cot_ref[f, z] for f in range(nf) for z in range(nz)] + coefs
        _pack_edges(vals, xf_ref, xl_ref, yf_ref, yl_ref)
        base = len(vals)
        for k in range(nplanes):
            v = slab_ref[k // nz, k % nz].astype(F32)
            xf_ref[base + k : base + k + 1, :] = v[0:1, :]
            xl_ref[base + k : base + k + 1, :] = v[x - 1 : x, :]
        _, lane = _iotas((1, y))
        row = jnp.zeros((1, y), F32)
        for k in range(nplanes):
            row = jnp.where(lane == k, sc_ref[k], row)
        xf_ref[base + nplanes : base + nplanes + 1, :] = row
        xl_ref[base + nplanes : base + nplanes + 1, :] = row

    rows = _rows(2 * nplanes + NCOEF + 1)
    return pl.pallas_call(
        kernel,
        out_shape=(jax.ShapeDtypeStruct((NCOEF, x, y), F32),)
        + _edge_shapes(rows, x, y)[:2]
        + _edge_shapes(8, x, y)[2:],
        in_specs=[
            pl.BlockSpec(memory_space=VMEM),
            pl.BlockSpec(memory_space=SMEM),
            pl.BlockSpec(memory_space=SMEM),
            pl.BlockSpec(memory_space=VMEM),
            pl.BlockSpec(memory_space=VMEM),
        ],
    )(soil_class, soil_table, scales, cot, slab)


def state0_call(pieces, scales, nf, per):
    npiece, _, x, y = pieces.shape
    nplanes = npiece * per
    nz = nplanes // nf

    def kernel(sc_ref, r_ref, s_ref, xm_ref, xp_ref, ym_ref, yp_ref):
        _, lane = _iotas((x, y))
        ym = jnp.zeros((x, y), F32)
        yp = jnp.zeros((x, y), F32)
        for k in range(nplanes):
            p, i = k // per, k % per
            s_ref[k // nz, k % nz] = r_ref[p, i].astype(F32) * sc_ref[k]
            hx = r_ref[p, per].astype(F32)
            xm_ref[k : k + 1, :] = hx[i : i + 1, :] * sc_ref[nplanes + k]
            xp_ref[k : k + 1, :] = hx[per + i : per + i + 1, :] * sc_ref[2 * nplanes + k]
            hy = r_ref[p, per + 2].astype(F32)
            ym = jnp.where(lane == k, _roll(hy, k - i, 1) * sc_ref[3 * nplanes + k], ym)
            yp = jnp.where(lane == k, _roll(hy, k - (per + i), 1) * sc_ref[4 * nplanes + k], yp)
        ym_ref[...] = ym
        yp_ref[...] = yp

    return pl.pallas_call(
        kernel,
        out_shape=(jax.ShapeDtypeStruct((nf, nz, x, y), F32),) + _edge_shapes(nplanes, x, y),
        in_specs=[pl.BlockSpec(memory_space=SMEM), pl.BlockSpec(memory_space=VMEM)],
    )(scales, pieces)


def step_call(s, s_halo, coef, c_halo, c_first, with_edges):
    nf, nz, x, y = s.shape

    def kernel(*refs):
        s_ref, sxm, sxp, sym, syp, c_ref, cxm, cxp, cym, cyp = refs[:10]
        rest = refs[10:]
        if with_edges:
            o_ref, xf_ref, xl_ref, yf_ref, yl_ref = rest[:5]
            scratch = rest[5:]
        else:
            o_ref = rest[0]
            scratch = rest[1:]
        sh_all = scratch[0:4]
        cs = scratch[4]
        _expand_halo(sxm, sxp, sym, syp, 0, nf, nz, sh_all)
        _coef_table(c_ref, cxm, cxp, cym, cyp, c_first, cs)
        masks = _iotas((x, y))
        sh = [tuple(h.at[f] for h in sh_all) for f in range(nf)]
        _step_body(s_ref, sh, cs, o_ref, nz, masks)
        if with_edges:
            vals = [o_ref[f, z] for f in range(nf) for z in range(nz)]
            _pack_edges(vals, xf_ref, xl_ref, yf_ref, yl_ref)

    out_shape = (jax.ShapeDtypeStruct(s.shape, F32),)
    if with_edges:
        out_shape = out_shape + _edge_shapes(_rows(nf * nz), x, y)
    res = pl.pallas_call(
        kernel,
        out_shape=out_shape,
        scratch_shapes=_halo_scratch(nf, nz, x, y) + [pltpu.VMEM((5 * NCOEF, x, y), F32)],
    )(s, *s_halo, coef, *c_halo)
    return res if with_edges else res[0]


def adjoint_call(s, s_halo, a, a_halo, a_first, coef, c_halo, c_first, with_edges):
    nf, nz, x, y = s.shape

    def kernel(*refs):
        s_ref, sxm, sxp, sym, syp, a_ref, axm, axp, aym, ayp, c_ref, cxm, cxp, cym, cyp = refs[:15]
        rest = refs[15:]
        if with_edges:
            o_ref, xf_ref, xl_ref, yf_ref, yl_ref = rest[:5]
            scratch = rest[5:]
        else:
            o_ref = rest[0]
            scratch = rest[1:]
        sh_all = scratch[0:4]
        ah_all = scratch[4:8]
        cs = scratch[8]
        _expand_halo(sxm, sxp, sym, syp, 0, nf, nz, sh_all)
        _expand_halo(axm, axp, aym, ayp, a_first, nf, nz, ah_all)
        _coef_table(c_ref, cxm, cxp, cym, cyp, c_first, cs)
        masks = _iotas((x, y))
        sh = [tuple(h.at[f] for h in sh_all) for f in range(nf)]
        ah = [tuple(h.at[f] for h in ah_all) for f in range(nf)]
        _adjoint_body(s_ref, sh, a_ref, ah, cs, o_ref, nz, masks)
        if with_edges:
            vals = [o_ref[f, z] for f in range(nf) for z in range(nz)]
            _pack_edges(vals, xf_ref, xl_ref, yf_ref, yl_ref)

    out_shape = (jax.ShapeDtypeStruct(s.shape, F32),)
    if with_edges:
        out_shape = out_shape + _edge_shapes(_rows(nf * nz), x, y)
    res = pl.pallas_call(
        kernel,
        out_shape=out_shape,
        scratch_shapes=_halo_scratch(nf, nz, x, y)
        + _halo_scratch(nf, nz, x, y)
        + [pltpu.VMEM((5 * NCOEF, x, y), F32)],
    )(s, *s_halo, a, *a_halo, coef, *c_halo)
    return res if with_edges else res[0]


def _shift(v, axis, step):
    n = lax.axis_size(axis)
    if step > 0:
        pairs = [(i, i + 1) for i in range(n - 1)]
    else:
        pairs = [(i + 1, i) for i in range(n - 1)]
    return lax.ppermute(v, axis, pairs)


def exchange(xf, xl, yf, yl):
    return (
        _shift(xl, "gx", 1),
        _shift(xf, "gx", -1),
        _shift(yl, "gy", 1),
        _shift(yf, "gy", -1),
    )


def forward_call(holder, held, per):
    n, planes, x, y = held.shape

    def kernel(hold_ref, h_ref, o_ref):
        _, lane = _iotas((x, y))
        for g in range(n):
            h = hold_ref[g]
            for i in range(planes):
                o_ref[g, i] = h_ref[h, i]
            cols = jnp.zeros((x, y), F32)
            scl = jnp.zeros((x, y), F32)
            if g > 0:
                hl = hold_ref[g - 1]
                for i in range(per):
                    v = h_ref[hl, i].astype(F32)
                    cols = jnp.where(lane == i, _roll(v, i - (y - 1), 1), cols)
                scl = jnp.where(lane < per, h_ref[hl, per + 1].astype(F32), scl)
            if g < n - 1:
                hr = hold_ref[g + 1]
                for i in range(per):
                    v = h_ref[hr, i].astype(F32)
                    cols = jnp.where(lane == per + i, _roll(v, per + i, 1), cols)
                sv = _roll(h_ref[hr, per + 1].astype(F32), per, 1)
                scl = jnp.where((lane >= per) & (lane < 2 * per), sv, scl)
            o_ref[g, planes] = cols.astype(o_ref.dtype)
            o_ref[g, planes + 1] = scl.astype(o_ref.dtype)

    return pl.pallas_call(
        kernel,
        out_shape=jax.ShapeDtypeStruct((n, planes + 2, x, y), held.dtype),
        in_specs=[pl.BlockSpec(memory_space=SMEM), pl.BlockSpec(memory_space=VMEM)],
    )(holder, held)


def route_blocks(stored_slab, block_scales, holder, xm_all, xp_all, first):
    nf, nz, x, y = stored_slab.shape
    n = lax.axis_size("gy")
    nplanes = nf * nz
    per = nplanes // n
    bf = stored_slab.dtype
    slab = stored_slab.reshape(n, per, x, y)
    rows_m = xm_all[first : first + nplanes].astype(bf).reshape(n, per, y)
    rows_p = xp_all[first : first + nplanes].astype(bf).reshape(n, per, y)
    halo = jnp.concatenate([rows_m, rows_p], axis=1)[:, None]
    sc_m = xm_all[first + nplanes, :nplanes].astype(bf).reshape(n, 1, per)
    sc_p = xp_all[first + nplanes, :nplanes].astype(bf).reshape(n, 1, per)
    sc = jnp.concatenate([block_scales.reshape(n, 1, per), sc_m, sc_p], axis=1)
    sc = jnp.pad(sc, ((0, 0), (0, x - 3), (0, y - per)))[:, None]
    held = lax.all_to_all(jnp.concatenate([slab, halo, sc], axis=1), "gy", 0, 0, tiled=True)

    forward = forward_call(holder, held, per)
    return lax.all_to_all(forward, "gy", 0, 0, tiled=True)


def on_device(stored_slab, block_scales, holder, soil_class, soil_table, cotangent):
    nf, nz, x, y = stored_slab.shape
    nplanes = nf * nz

    coef, cxf, cxl, cyf, cyl = prep_call(
        soil_class, soil_table, cotangent, stored_slab, block_scales.reshape(-1).astype(F32)
    )
    c_halo = exchange(cxf, cxl, cyf, cyl)
    c_first = nplanes

    pieces = route_blocks(stored_slab, block_scales, holder, c_halo[0], c_halo[1], nplanes + NCOEF)
    per = nplanes // pieces.shape[0]
    scales = jnp.concatenate(
        [
            pieces[:, per + 1, 0:3, :per].transpose(1, 0, 2).reshape(3, nplanes),
            pieces[:, per + 3, 0, : 2 * per].reshape(-1, 2, per).transpose(1, 0, 2).reshape(2, nplanes),
        ]
    ).astype(F32).reshape(-1)
    s0, *s0_halo = state0_call(pieces, scales, nf, per)

    s1, *s1_edges = step_call(s0, s0_halo, coef, c_halo, c_first, True)
    s1_halo = exchange(*s1_edges)

    a1, *a1_edges = adjoint_call(
        s1, s1_halo, cotangent, c_halo, 0, coef, c_halo, c_first, True
    )
    a1_halo = exchange(*a1_edges)
    s2 = step_call(s1, s1_halo, coef, c_halo, c_first, False)

    sens = adjoint_call(s0, s0_halo, a1, a1_halo, 0, coef, c_halo, c_first, False)
    return (s2, sens)


def solution(mesh):
    placed = (
        P(None, None, "gx", "gy"),
        P(None, None, "gx", "gy"),
        P(),
        P("gx", "gy"),
        P(),
        P(None, None, "gx", "gy"),
    )
    return jax.shard_map(
        on_device,
        mesh=mesh,
        in_specs=placed,
        out_specs=(P(None, None, "gx", "gy"), P(None, None, "gx", "gy")),
        check_vma=False,
    )
```

```python
import jax
import jax.numpy as jnp
from jax import lax
from jax.experimental import pallas as pl
from jax.experimental.pallas import tpu as pltpu
from jax.sharding import PartitionSpec as P

F32 = jnp.float32
NCOEF = 4
UNROLL = 8
VMEM = pltpu.MemorySpace.VMEM
SMEM = pltpu.MemorySpace.SMEM


def _roll(v, shift, axis):
    shift = shift % v.shape[axis]
    if shift == 0:
        return v
    return pltpu.roll(v, shift, axis)


def _iotas(shape):
    return lax.broadcasted_iota(jnp.int32, shape, 0), lax.broadcasted_iota(jnp.int32, shape, 1)


def _pack_edges(vals, xf_ref, xl_ref, yf_ref, yl_ref):
    x, y = vals[0].shape
    _, lane = _iotas((x, y))
    xf_ref[...] = jnp.zeros(xf_ref.shape, F32)
    xl_ref[...] = jnp.zeros(xl_ref.shape, F32)
    yf = jnp.zeros((x, y), F32)
    yl = jnp.zeros((x, y), F32)
    for k, v in enumerate(vals):
        xf_ref[k : k + 1, :] = v[0:1, :]
        xl_ref[k : k + 1, :] = v[x - 1 : x, :]
        yf = jnp.where(lane == k, _roll(v, k, 1), yf)
        yl = jnp.where(lane == k, _roll(v, k - (y - 1), 1), yl)
    yf_ref[...] = yf
    yl_ref[...] = yl


def _expand_halo(xm_ref, xp_ref, ym_ref, yp_ref, first, nf, nz, dst):
    hxm, hxp, hym, hyp = dst
    x, y = hxm.shape[2], hxm.shape[3]
    ymv = ym_ref[...]
    ypv = yp_ref[...]
    for f in range(nf):
        for z in range(nz):
            k = first + f * nz + z
            hxm[f, z] = jnp.broadcast_to(xm_ref[k : k + 1, :], (x, y))
            hxp[f, z] = jnp.broadcast_to(xp_ref[k : k + 1, :], (x, y))
            hym[f, z] = _roll(ymv, -k, 1)
            hyp[f, z] = _roll(ypv, (y - 1) - k, 1)


def _coef_table(c_ref, cxm_ref, cxp_ref, cym_ref, cyp_ref, first, cs):
    x, y = c_ref.shape[1], c_ref.shape[2]
    ymv = cym_ref[...]
    ypv = cyp_ref[...]
    masks = _iotas((x, y))
    for k in range(NCOEF):
        r = first + k
        cv = c_ref[k]
        cs[k] = cv
        halo = (
            jnp.broadcast_to(cxm_ref[r : r + 1, :], (x, y)),
            jnp.broadcast_to(cxp_ref[r : r + 1, :], (x, y)),
            _roll(ymv, -r, 1),
            _roll(ypv, (y - 1) - r, 1),
        )
        for d, v in enumerate(_neighbours(cv, 0, [h[None] for h in halo], masks)):
            cs[4 + 4 * d + k] = v


def _neighbours(v, z, h, masks):
    row, lane = masks
    x, y = v.shape
    hxm, hxp, hym, hyp = h
    return (
        jnp.where(row == 0, hxm[z], _roll(v, 1, 0)),
        jnp.where(row == x - 1, hxp[z], _roll(v, x - 1, 0)),
        jnp.where(lane == 0, hym[z], _roll(v, 1, 1)),
        jnp.where(lane == y - 1, hyp[z], _roll(v, y - 1, 1)),
    )


def _field_at(ref, f, z, nz):
    zm = jnp.maximum(z - 1, 0)
    zp = jnp.minimum(z + 1, nz - 1)
    vm = jnp.where(z > 0, 1.0, 0.0).astype(F32)
    vp = jnp.where(z < nz - 1, 1.0, 0.0).astype(F32)
    return ref[f, z], ref[f, zm] * vm, ref[f, zp] * vp, vm, vp


def _gains(b):
    return 1.5 + b, 1.5 + 0.5 * b


def _step_body(s_ref, sh, cs, o_ref, nz, masks):
    def body(z, carry):
        u, u_m, u_p, vm, vp = _field_at(s_ref, 0, z, nz)
        t, t_m, t_p, _, _ = _field_at(s_ref, 1, z, nz)
        c = [cs[k] for k in range(NCOEF)]
        g1, g2 = _gains(jnp.tanh(u))
        kw, dtv, lamb, kv = c[0] * g1, c[1] * g2, c[2] * g2, c[3] * g1
        a1 = jnp.zeros_like(u)
        a2 = jnp.zeros_like(u)
        for un, tn, valid in ((u_m, t_m, vm), (u_p, t_p, vp)):
            g1n, g2n = _gains(jnp.tanh(un))
            a1 = a1 + (g1 + valid * g1n) * (un - u)
            a2 = a2 + (g2 + valid * g2n) * (tn - t)
        f0 = c[0] * a1 + c[1] * a2
        f1 = c[2] * a2 + c[3] * a1
        uns = _neighbours(u, z, sh[0], masks)
        tns = _neighbours(t, z, sh[1], masks)
        for d in range(4):
            un, tn = uns[d], tns[d]
            g1n, g2n = _gains(jnp.tanh(un))
            cn = [cs[4 + 4 * d + k] for k in range(NCOEF)]
            du = un - u
            dt = tn - t
            f0 = f0 + (kw + cn[0] * g1n) * du + (dtv + cn[1] * g2n) * dt
            f1 = f1 + (lamb + cn[2] * g2n) * dt + (kv + cn[3] * g1n) * du
        o_ref[0, z] = u + 0.5 * f0
        o_ref[1, z] = t + 0.5 * f1
        return carry

    lax.fori_loop(0, nz, body, 0, unroll=UNROLL)


def _adjoint_body(s_ref, sh, a_ref, ah, cs, o_ref, nz, masks):
    def body(z, carry):
        u, u_m, u_p, vm, vp = _field_at(s_ref, 0, z, nz)
        t, t_m, t_p, _, _ = _field_at(s_ref, 1, z, nz)
        a0, a0_m, a0_p, _, _ = _field_at(a_ref, 0, z, nz)
        a1, a1_m, a1_p, _, _ = _field_at(a_ref, 1, z, nz)
        c = [cs[k] for k in range(NCOEF)]
        b = jnp.tanh(u)
        g1, g2 = _gains(b)
        kw, dtv, lamb, kv = c[0] * g1, c[1] * g2, c[2] * g2, c[3] * g1
        zero = jnp.zeros_like(u)
        p10, p11, p20, p21 = zero, zero, zero, zero
        gu0, gu1, gt0, gt1 = zero, zero, zero, zero
        for un, tn, a0n, a1n, valid in ((u_m, t_m, a0_m, a1_m, vm), (u_p, t_p, a0_p, a1_p, vp)):
            g1n, g2n = _gains(jnp.tanh(un))
            s1 = g1 + valid * g1n
            s2 = g2 + valid * g2n
            du, dt, da0, da1 = un - u, tn - t, a0n - a0, a1n - a1
            p10 = p10 + s1 * da0
            p11 = p11 + s1 * da1
            p20 = p20 + s2 * da0
            p21 = p21 + s2 * da1
            gu0 = gu0 + du * da0
            gu1 = gu1 + du * da1
            gt0 = gt0 + dt * da0
            gt1 = gt1 + dt * da1
        ju = c[0] * p10 + c[3] * p11
        jt = c[1] * p20 + c[2] * p21
        uns = _neighbours(u, z, sh[0], masks)
        tns = _neighbours(t, z, sh[1], masks)
        a0ns = _neighbours(a0, z, ah[0], masks)
        a1ns = _neighbours(a1, z, ah[1], masks)
        for d in range(4):
            un, tn, a0n, a1n = uns[d], tns[d], a0ns[d], a1ns[d]
            g1n, g2n = _gains(jnp.tanh(un))
            cn = [cs[4 + 4 * d + k] for k in range(NCOEF)]
            du, dt, da0, da1 = un - u, tn - t, a0n - a0, a1n - a1
            ju = ju + (kw + cn[0] * g1n) * da0 + (kv + cn[3] * g1n) * da1
            jt = jt + (dtv + cn[1] * g2n) * da0 + (lamb + cn[2] * g2n) * da1
            gu0 = gu0 + du * da0
            gu1 = gu1 + du * da1
            gt0 = gt0 + dt * da0
            gt1 = gt1 + dt * da1
        gsum = c[0] * gu0 + c[3] * gu1 + 0.5 * (c[1] * gt0 + c[2] * gt1)
        o_ref[0, z] = a0 + 0.5 * ju - 0.5 * (1.0 - b * b) * gsum
        o_ref[1, z] = a1 + 0.5 * jt
        return carry

    lax.fori_loop(0, nz, body, 0, unroll=UNROLL)


def _halo_scratch(nf, nz, x, y):
    return [pltpu.VMEM((nf, nz, x, y), F32) for _ in range(4)]


def _edge_shapes(rows, x, y):
    return (
        jax.ShapeDtypeStruct((rows, y), F32),
        jax.ShapeDtypeStruct((rows, y), F32),
        jax.ShapeDtypeStruct((x, y), F32),
        jax.ShapeDtypeStruct((x, y), F32),
    )


def _rows(n):
    return -(-n // 8) * 8


def prep_call(soil_class, soil_table, cot, slab, scales):
    nf, nz, x, y = cot.shape
    nclass = soil_table.shape[0]
    nplanes = nf * nz

    def kernel(cls_ref, tab_ref, sc_ref, cot_ref, slab_ref, coef_ref, xf_ref, xl_ref, yf_ref, yl_ref):
        cls = cls_ref[...]
        coefs = []
        for k in range(NCOEF):
            cv = jnp.zeros(cls.shape, F32)
            for j in range(nclass):
                cv = jnp.where(cls == j, tab_ref[j, k], cv)
            coef_ref[k] = cv
            coefs.append(cv)
        vals = [cot_ref[f, z] for f in range(nf) for z in range(nz)] + coefs
        _pack_edges(vals, xf_ref, xl_ref, yf_ref, yl_ref)
        base = len(vals)
        for k in range(nplanes):
            v = slab_ref[k // nz, k % nz].astype(F32)
            xf_ref[base + k : base + k + 1, :] = v[0:1, :]
            xl_ref[base + k : base + k + 1, :] = v[x - 1 : x, :]
        _, lane = _iotas((1, y))
        row = jnp.zeros((1, y), F32)
        for k in range(nplanes):
            row = jnp.where(lane == k, sc_ref[k], row)
        xf_ref[base + nplanes : base + nplanes + 1, :] = row
        xl_ref[base + nplanes : base + nplanes + 1, :] = row

    rows = _rows(2 * nplanes + NCOEF + 1)
    return pl.pallas_call(
        kernel,
        out_shape=(jax.ShapeDtypeStruct((NCOEF, x, y), F32),)
        + _edge_shapes(rows, x, y)[:2]
        + _edge_shapes(8, x, y)[2:],
        in_specs=[
            pl.BlockSpec(memory_space=VMEM),
            pl.BlockSpec(memory_space=SMEM),
            pl.BlockSpec(memory_space=SMEM),
            pl.BlockSpec(memory_space=VMEM),
            pl.BlockSpec(memory_space=VMEM),
        ],
    )(soil_class, soil_table, scales, cot, slab)


def _state0_body(sc_ref, r_ref, s_ref, xm_ref, xp_ref, ym_ref, yp_ref, per):
    nz, x, y = s_ref.shape[1], s_ref.shape[2], s_ref.shape[3]
    nplanes = s_ref.shape[0] * nz
    _, lane = _iotas((x, y))
    ym = jnp.zeros((x, y), F32)
    yp = jnp.zeros((x, y), F32)
    for k in range(nplanes):
        p, i = k // per, k % per
        s_ref[k // nz, k % nz] = r_ref[p, i].astype(F32) * sc_ref[k]
        hx = r_ref[p, per].astype(F32)
        xm_ref[k : k + 1, :] = hx[i : i + 1, :] * sc_ref[nplanes + k]
        xp_ref[k : k + 1, :] = hx[per + i : per + i + 1, :] * sc_ref[2 * nplanes + k]
        hy = r_ref[p, per + 2].astype(F32)
        ym = jnp.where(lane == k, _roll(hy, k - i, 1) * sc_ref[3 * nplanes + k], ym)
        yp = jnp.where(lane == k, _roll(hy, k - (per + i), 1) * sc_ref[4 * nplanes + k], yp)
    ym_ref[...] = ym
    yp_ref[...] = yp


def state0_step_call(pieces, scales, nf, per, coef, c_halo, c_first):
    npiece, _, x, y = pieces.shape
    nplanes = npiece * per
    nz = nplanes // nf

    def kernel(sc_ref, r_ref, c_ref, cxm, cxp, cym, cyp, *refs):
        s0_ref, xm_ref, xp_ref, ym_ref, yp_ref = refs[:5]
        s1_ref, xf_ref, xl_ref, yf_ref, yl_ref = refs[5:10]
        scratch = refs[10:]
        sh_all = scratch[0:4]
        cs = scratch[4]
        _state0_body(sc_ref, r_ref, s0_ref, xm_ref, xp_ref, ym_ref, yp_ref, per)
        _expand_halo(xm_ref, xp_ref, ym_ref, yp_ref, 0, nf, nz, sh_all)
        _coef_table(c_ref, cxm, cxp, cym, cyp, c_first, cs)
        masks = _iotas((x, y))
        sh = [tuple(h.at[f] for h in sh_all) for f in range(nf)]
        _step_body(s0_ref, sh, cs, s1_ref, nz, masks)
        vals = [s1_ref[f, z] for f in range(nf) for z in range(nz)]
        _pack_edges(vals, xf_ref, xl_ref, yf_ref, yl_ref)

    state = jax.ShapeDtypeStruct((nf, nz, x, y), F32)
    return pl.pallas_call(
        kernel,
        out_shape=(state,) + _edge_shapes(nplanes, x, y) + (state,) + _edge_shapes(_rows(nplanes), x, y),
        in_specs=[pl.BlockSpec(memory_space=SMEM)] + [pl.BlockSpec(memory_space=VMEM)] * 6,
        scratch_shapes=_halo_scratch(nf, nz, x, y) + [pltpu.VMEM((5 * NCOEF, x, y), F32)],
    )(scales, pieces, coef, *c_halo)


def step_call(s, s_halo, coef, c_halo, c_first, with_edges):
    nf, nz, x, y = s.shape

    def kernel(*refs):
        s_ref, sxm, sxp, sym, syp, c_ref, cxm, cxp, cym, cyp = refs[:10]
        rest = refs[10:]
        if with_edges:
            o_ref, xf_ref, xl_ref, yf_ref, yl_ref = rest[:5]
            scratch = rest[5:]
        else:
            o_ref = rest[0]
            scratch = rest[1:]
        sh_all = scratch[0:4]
        cs = scratch[4]
        _expand_halo(sxm, sxp, sym, syp, 0, nf, nz, sh_all)
        _coef_table(c_ref, cxm, cxp, cym, cyp, c_first, cs)
        masks = _iotas((x, y))
        sh = [tuple(h.at[f] for h in sh_all) for f in range(nf)]
        _step_body(s_ref, sh, cs, o_ref, nz, masks)
        if with_edges:
            vals = [o_ref[f, z] for f in range(nf) for z in range(nz)]
            _pack_edges(vals, xf_ref, xl_ref, yf_ref, yl_ref)

    out_shape = (jax.ShapeDtypeStruct(s.shape, F32),)
    if with_edges:
        out_shape = out_shape + _edge_shapes(_rows(nf * nz), x, y)
    res = pl.pallas_call(
        kernel,
        out_shape=out_shape,
        scratch_shapes=_halo_scratch(nf, nz, x, y) + [pltpu.VMEM((5 * NCOEF, x, y), F32)],
    )(s, *s_halo, coef, *c_halo)
    return res if with_edges else res[0]


def adjoint_call(s, s_halo, a, a_halo, a_first, coef, c_halo, c_first, with_edges):
    nf, nz, x, y = s.shape

    def kernel(*refs):
        s_ref, sxm, sxp, sym, syp, a_ref, axm, axp, aym, ayp, c_ref, cxm, cxp, cym, cyp = refs[:15]
        rest = refs[15:]
        if with_edges:
            o_ref, xf_ref, xl_ref, yf_ref, yl_ref = rest[:5]
            scratch = rest[5:]
        else:
            o_ref = rest[0]
            scratch = rest[1:]
        sh_all = scratch[0:4]
        ah_all = scratch[4:8]
        cs = scratch[8]
        _expand_halo(sxm, sxp, sym, syp, 0, nf, nz, sh_all)
        _expand_halo(axm, axp, aym, ayp, a_first, nf, nz, ah_all)
        _coef_table(c_ref, cxm, cxp, cym, cyp, c_first, cs)
        masks = _iotas((x, y))
        sh = [tuple(h.at[f] for h in sh_all) for f in range(nf)]
        ah = [tuple(h.at[f] for h in ah_all) for f in range(nf)]
        _adjoint_body(s_ref, sh, a_ref, ah, cs, o_ref, nz, masks)
        if with_edges:
            vals = [o_ref[f, z] for f in range(nf) for z in range(nz)]
            _pack_edges(vals, xf_ref, xl_ref, yf_ref, yl_ref)

    out_shape = (jax.ShapeDtypeStruct(s.shape, F32),)
    if with_edges:
        out_shape = out_shape + _edge_shapes(_rows(nf * nz), x, y)
    res = pl.pallas_call(
        kernel,
        out_shape=out_shape,
        scratch_shapes=_halo_scratch(nf, nz, x, y)
        + _halo_scratch(nf, nz, x, y)
        + [pltpu.VMEM((5 * NCOEF, x, y), F32)],
    )(s, *s_halo, a, *a_halo, coef, *c_halo)
    return res if with_edges else res[0]


def _shift(v, axis, step):
    n = lax.axis_size(axis)
    if step > 0:
        pairs = [(i, i + 1) for i in range(n - 1)]
    else:
        pairs = [(i + 1, i) for i in range(n - 1)]
    return lax.ppermute(v, axis, pairs)


def exchange(xf, xl, yf, yl):
    return (
        _shift(xl, "gx", 1),
        _shift(xf, "gx", -1),
        _shift(yl, "gy", 1),
        _shift(yf, "gy", -1),
    )


def forward_call(holder, held, per):
    n, planes, x, y = held.shape

    def kernel(hold_ref, h_ref, o_ref):
        _, lane = _iotas((x, y))
        for g in range(n):
            h = hold_ref[g]
            for i in range(planes):
                o_ref[g, i] = h_ref[h, i]
            cols = jnp.zeros((x, y), F32)
            scl = jnp.zeros((x, y), F32)
            if g > 0:
                hl = hold_ref[g - 1]
                for i in range(per):
                    v = h_ref[hl, i].astype(F32)
                    cols = jnp.where(lane == i, _roll(v, i - (y - 1), 1), cols)
                scl = jnp.where(lane < per, h_ref[hl, per + 1].astype(F32), scl)
            if g < n - 1:
                hr = hold_ref[g + 1]
                for i in range(per):
                    v = h_ref[hr, i].astype(F32)
                    cols = jnp.where(lane == per + i, _roll(v, per + i, 1), cols)
                sv = _roll(h_ref[hr, per + 1].astype(F32), per, 1)
                scl = jnp.where((lane >= per) & (lane < 2 * per), sv, scl)
            o_ref[g, planes] = cols.astype(o_ref.dtype)
            o_ref[g, planes + 1] = scl.astype(o_ref.dtype)

    return pl.pallas_call(
        kernel,
        out_shape=jax.ShapeDtypeStruct((n, planes + 2, x, y), held.dtype),
        in_specs=[pl.BlockSpec(memory_space=SMEM), pl.BlockSpec(memory_space=VMEM)],
    )(holder, held)


def route_blocks(stored_slab, block_scales, holder, xm_all, xp_all, first):
    nf, nz, x, y = stored_slab.shape
    n = lax.axis_size("gy")
    nplanes = nf * nz
    per = nplanes // n
    bf = stored_slab.dtype
    slab = stored_slab.reshape(n, per, x, y)
    rows_m = xm_all[first : first + nplanes].astype(bf).reshape(n, per, y)
    rows_p = xp_all[first : first + nplanes].astype(bf).reshape(n, per, y)
    halo = jnp.concatenate([rows_m, rows_p], axis=1)[:, None]
    sc_m = xm_all[first + nplanes, :nplanes].astype(bf).reshape(n, 1, per)
    sc_p = xp_all[first + nplanes, :nplanes].astype(bf).reshape(n, 1, per)
    sc = jnp.concatenate([block_scales.reshape(n, 1, per), sc_m, sc_p], axis=1)
    sc = jnp.pad(sc, ((0, 0), (0, x - 3), (0, y - per)))[:, None]
    held = lax.all_to_all(jnp.concatenate([slab, halo, sc], axis=1), "gy", 0, 0, tiled=True)

    forward = forward_call(holder, held, per)
    return lax.all_to_all(forward, "gy", 0, 0, tiled=True)


def on_device(stored_slab, block_scales, holder, soil_class, soil_table, cotangent):
    nf, nz, x, y = stored_slab.shape
    nplanes = nf * nz

    coef, cxf, cxl, cyf, cyl = prep_call(
        soil_class, soil_table, cotangent, stored_slab, block_scales.reshape(-1).astype(F32)
    )
    c_halo = exchange(cxf, cxl, cyf, cyl)
    c_first = nplanes

    pieces = route_blocks(stored_slab, block_scales, holder, c_halo[0], c_halo[1], nplanes + NCOEF)
    per = nplanes // pieces.shape[0]
    scales = jnp.concatenate(
        [
            pieces[:, per + 1, 0:3, :per].transpose(1, 0, 2).reshape(3, nplanes),
            pieces[:, per + 3, 0, : 2 * per].reshape(-1, 2, per).transpose(1, 0, 2).reshape(2, nplanes),
        ]
    ).astype(F32).reshape(-1)
    res = state0_step_call(pieces, scales, nf, per, coef, c_halo, c_first)
    s0, s0_halo, s1, s1_edges = res[0], res[1:5], res[5], res[6:10]
    s1_halo = exchange(*s1_edges)

    a1, *a1_edges = adjoint_call(
        s1, s1_halo, cotangent, c_halo, 0, coef, c_halo, c_first, True
    )
    a1_halo = exchange(*a1_edges)
    s2 = step_call(s1, s1_halo, coef, c_halo, c_first, False)

    sens = adjoint_call(s0, s0_halo, a1, a1_halo, 0, coef, c_halo, c_first, False)
    return (s2, sens)


def solution(mesh):
    placed = (
        P(None, None, "gx", "gy"),
        P(None, None, "gx", "gy"),
        P(),
        P("gx", "gy"),
        P(),
        P(None, None, "gx", "gy"),
    )
    return jax.shard_map(
        on_device,
        mesh=mesh,
        in_specs=placed,
        out_specs=(P(None, None, "gx", "gy"), P(None, None, "gx", "gy")),
        check_vma=False,
    )
```

```python
import jax
import jax.numpy as jnp
from jax import lax
from jax.experimental import pallas as pl
from jax.experimental.pallas import tpu as pltpu
from jax.sharding import PartitionSpec as P

F32 = jnp.float32
NCOEF = 4
UNROLL = 8
VMEM = pltpu.MemorySpace.VMEM
SMEM = pltpu.MemorySpace.SMEM


def _roll(v, shift, axis):
    shift = shift % v.shape[axis]
    if shift == 0:
        return v
    return pltpu.roll(v, shift, axis)


def _iotas(shape):
    return lax.broadcasted_iota(jnp.int32, shape, 0), lax.broadcasted_iota(jnp.int32, shape, 1)


def _pack_edges(vals, xf_ref, xl_ref, yf_ref, yl_ref):
    x, y = vals[0].shape
    _, lane = _iotas((x, y))
    xf_ref[...] = jnp.zeros(xf_ref.shape, F32)
    xl_ref[...] = jnp.zeros(xl_ref.shape, F32)
    yf = jnp.zeros((x, y), F32)
    yl = jnp.zeros((x, y), F32)
    for k, v in enumerate(vals):
        xf_ref[k : k + 1, :] = v[0:1, :]
        xl_ref[k : k + 1, :] = v[x - 1 : x, :]
        yf = jnp.where(lane == k, _roll(v, k, 1), yf)
        yl = jnp.where(lane == k, _roll(v, k - (y - 1), 1), yl)
    yf_ref[...] = yf
    yl_ref[...] = yl


def _expand_halo(xm_ref, xp_ref, ym_ref, yp_ref, first, nf, nz, dst):
    hxm, hxp, hym, hyp = dst
    x, y = hxm.shape[2], hxm.shape[3]
    ymv = ym_ref[...]
    ypv = yp_ref[...]
    for f in range(nf):
        for z in range(nz):
            k = first + f * nz + z
            hxm[f, z] = jnp.broadcast_to(xm_ref[k : k + 1, :], (x, y))
            hxp[f, z] = jnp.broadcast_to(xp_ref[k : k + 1, :], (x, y))
            hym[f, z] = _roll(ymv, -k, 1)
            hyp[f, z] = _roll(ypv, (y - 1) - k, 1)


def _coef_table(c_ref, cxm_ref, cxp_ref, cym_ref, cyp_ref, first, cs):
    x, y = c_ref.shape[1], c_ref.shape[2]
    ymv = cym_ref[...]
    ypv = cyp_ref[...]
    masks = _iotas((x, y))
    for k in range(NCOEF):
        r = first + k
        cv = c_ref[k]
        cs[k] = cv
        halo = (
            jnp.broadcast_to(cxm_ref[r : r + 1, :], (x, y)),
            jnp.broadcast_to(cxp_ref[r : r + 1, :], (x, y)),
            _roll(ymv, -r, 1),
            _roll(ypv, (y - 1) - r, 1),
        )
        for d, v in enumerate(_neighbours(cv, 0, [h[None] for h in halo], masks)):
            cs[4 + 4 * d + k] = v


def _neighbours(v, z, h, masks):
    row, lane = masks
    x, y = v.shape
    hxm, hxp, hym, hyp = h
    return (
        jnp.where(row == 0, hxm[z], _roll(v, 1, 0)),
        jnp.where(row == x - 1, hxp[z], _roll(v, x - 1, 0)),
        jnp.where(lane == 0, hym[z], _roll(v, 1, 1)),
        jnp.where(lane == y - 1, hyp[z], _roll(v, y - 1, 1)),
    )


def _field_at(ref, f, z, nz):
    zm = jnp.maximum(z - 1, 0)
    zp = jnp.minimum(z + 1, nz - 1)
    vm = jnp.where(z > 0, 1.0, 0.0).astype(F32)
    vp = jnp.where(z < nz - 1, 1.0, 0.0).astype(F32)
    return ref[f, z], ref[f, zm] * vm, ref[f, zp] * vp, vm, vp


def _gains(b):
    return 1.5 + b, 1.5 + 0.5 * b


def _step_body(s_ref, sh, cs, o_ref, nz, masks):
    def body(z, carry):
        u, u_m, u_p, vm, vp = _field_at(s_ref, 0, z, nz)
        t, t_m, t_p, _, _ = _field_at(s_ref, 1, z, nz)
        c = [cs[k] for k in range(NCOEF)]
        g1, g2 = _gains(jnp.tanh(u))
        kw, dtv, lamb, kv = c[0] * g1, c[1] * g2, c[2] * g2, c[3] * g1
        a1 = jnp.zeros_like(u)
        a2 = jnp.zeros_like(u)
        for un, tn, valid in ((u_m, t_m, vm), (u_p, t_p, vp)):
            g1n, g2n = _gains(jnp.tanh(un))
            a1 = a1 + (g1 + valid * g1n) * (un - u)
            a2 = a2 + (g2 + valid * g2n) * (tn - t)
        f0 = c[0] * a1 + c[1] * a2
        f1 = c[2] * a2 + c[3] * a1
        uns = _neighbours(u, z, sh[0], masks)
        tns = _neighbours(t, z, sh[1], masks)
        for d in range(4):
            un, tn = uns[d], tns[d]
            g1n, g2n = _gains(jnp.tanh(un))
            cn = [cs[4 + 4 * d + k] for k in range(NCOEF)]
            du = un - u
            dt = tn - t
            f0 = f0 + (kw + cn[0] * g1n) * du + (dtv + cn[1] * g2n) * dt
            f1 = f1 + (lamb + cn[2] * g2n) * dt + (kv + cn[3] * g1n) * du
        o_ref[0, z] = u + 0.5 * f0
        o_ref[1, z] = t + 0.5 * f1
        return carry

    lax.fori_loop(0, nz, body, 0, unroll=UNROLL)


def _adjoint_body(s_ref, sh, a_ref, ah, cs, o_ref, nz, masks):
    def body(z, carry):
        u, u_m, u_p, vm, vp = _field_at(s_ref, 0, z, nz)
        t, t_m, t_p, _, _ = _field_at(s_ref, 1, z, nz)
        a0, a0_m, a0_p, _, _ = _field_at(a_ref, 0, z, nz)
        a1, a1_m, a1_p, _, _ = _field_at(a_ref, 1, z, nz)
        c = [cs[k] for k in range(NCOEF)]
        b = jnp.tanh(u)
        g1, g2 = _gains(b)
        kw, dtv, lamb, kv = c[0] * g1, c[1] * g2, c[2] * g2, c[3] * g1
        zero = jnp.zeros_like(u)
        p10, p11, p20, p21 = zero, zero, zero, zero
        gu0, gu1, gt0, gt1 = zero, zero, zero, zero
        for un, tn, a0n, a1n, valid in ((u_m, t_m, a0_m, a1_m, vm), (u_p, t_p, a0_p, a1_p, vp)):
            g1n, g2n = _gains(jnp.tanh(un))
            s1 = g1 + valid * g1n
            s2 = g2 + valid * g2n
            du, dt, da0, da1 = un - u, tn - t, a0n - a0, a1n - a1
            p10 = p10 + s1 * da0
            p11 = p11 + s1 * da1
            p20 = p20 + s2 * da0
            p21 = p21 + s2 * da1
            gu0 = gu0 + du * da0
            gu1 = gu1 + du * da1
            gt0 = gt0 + dt * da0
            gt1 = gt1 + dt * da1
        ju = c[0] * p10 + c[3] * p11
        jt = c[1] * p20 + c[2] * p21
        uns = _neighbours(u, z, sh[0], masks)
        tns = _neighbours(t, z, sh[1], masks)
        a0ns = _neighbours(a0, z, ah[0], masks)
        a1ns = _neighbours(a1, z, ah[1], masks)
        for d in range(4):
            un, tn, a0n, a1n = uns[d], tns[d], a0ns[d], a1ns[d]
            g1n, g2n = _gains(jnp.tanh(un))
            cn = [cs[4 + 4 * d + k] for k in range(NCOEF)]
            du, dt, da0, da1 = un - u, tn - t, a0n - a0, a1n - a1
            ju = ju + (kw + cn[0] * g1n) * da0 + (kv + cn[3] * g1n) * da1
            jt = jt + (dtv + cn[1] * g2n) * da0 + (lamb + cn[2] * g2n) * da1
            gu0 = gu0 + du * da0
            gu1 = gu1 + du * da1
            gt0 = gt0 + dt * da0
            gt1 = gt1 + dt * da1
        gsum = c[0] * gu0 + c[3] * gu1 + 0.5 * (c[1] * gt0 + c[2] * gt1)
        o_ref[0, z] = a0 + 0.5 * ju - 0.5 * (1.0 - b * b) * gsum
        o_ref[1, z] = a1 + 0.5 * jt
        return carry

    lax.fori_loop(0, nz, body, 0, unroll=UNROLL)


def _halo_scratch(nf, nz, x, y):
    return [pltpu.VMEM((nf, nz, x, y), F32) for _ in range(4)]


def _edge_shapes(rows, x, y):
    return (
        jax.ShapeDtypeStruct((rows, y), F32),
        jax.ShapeDtypeStruct((rows, y), F32),
        jax.ShapeDtypeStruct((x, y), F32),
        jax.ShapeDtypeStruct((x, y), F32),
    )


def _rows(n):
    return -(-n // 8) * 8


def prep_call(soil_class, soil_table, cot):
    nf, nz, x, y = cot.shape
    nclass = soil_table.shape[0]

    def kernel(cls_ref, tab_ref, cot_ref, coef_ref, xf_ref, xl_ref, yf_ref, yl_ref):
        cls = cls_ref[...]
        coefs = []
        for k in range(NCOEF):
            cv = jnp.zeros(cls.shape, F32)
            for j in range(nclass):
                cv = jnp.where(cls == j, tab_ref[j, k], cv)
            coef_ref[k] = cv
            coefs.append(cv)
        vals = [cot_ref[f, z] for f in range(nf) for z in range(nz)] + coefs
        _pack_edges(vals, xf_ref, xl_ref, yf_ref, yl_ref)

    rows = _rows(nf * nz + NCOEF)
    return pl.pallas_call(
        kernel,
        out_shape=(jax.ShapeDtypeStruct((NCOEF, x, y), F32),) + _edge_shapes(rows, x, y),
        in_specs=[
            pl.BlockSpec(memory_space=VMEM),
            pl.BlockSpec(memory_space=SMEM),
            pl.BlockSpec(memory_space=VMEM),
        ],
    )(soil_class, soil_table, cot)


def _state0_body(sc_ref, r_ref, s_ref, xm_ref, xp_ref, ym_ref, yp_ref, per):
    nz, x, y = s_ref.shape[1], s_ref.shape[2], s_ref.shape[3]
    nplanes = s_ref.shape[0] * nz
    _, lane = _iotas((x, y))
    ym = jnp.zeros((x, y), F32)
    yp = jnp.zeros((x, y), F32)
    for k in range(nplanes):
        p, i = k // per, k % per
        s_ref[k // nz, k % nz] = r_ref[p, i].astype(F32) * sc_ref[k]
        hx = r_ref[p, per].astype(F32)
        xm_ref[k : k + 1, :] = hx[i : i + 1, :] * sc_ref[nplanes + k]
        xp_ref[k : k + 1, :] = hx[per + i : per + i + 1, :] * sc_ref[2 * nplanes + k]
        hy = r_ref[p, per + 2].astype(F32)
        ym = jnp.where(lane == k, _roll(hy, k - i, 1) * sc_ref[3 * nplanes + k], ym)
        yp = jnp.where(lane == k, _roll(hy, k - (per + i), 1) * sc_ref[4 * nplanes + k], yp)
    ym_ref[...] = ym
    yp_ref[...] = yp


def state0_step_call(pieces, scales, nf, per, coef, c_halo, c_first):
    npiece, _, x, y = pieces.shape
    nplanes = npiece * per
    nz = nplanes // nf

    def kernel(sc_ref, r_ref, c_ref, cxm, cxp, cym, cyp, *refs):
        s0_ref, xm_ref, xp_ref, ym_ref, yp_ref = refs[:5]
        s1_ref, xf_ref, xl_ref, yf_ref, yl_ref = refs[5:10]
        scratch = refs[10:]
        sh_all = scratch[0:4]
        cs = scratch[4]
        _state0_body(sc_ref, r_ref, s0_ref, xm_ref, xp_ref, ym_ref, yp_ref, per)
        _expand_halo(xm_ref, xp_ref, ym_ref, yp_ref, 0, nf, nz, sh_all)
        _coef_table(c_ref, cxm, cxp, cym, cyp, c_first, cs)
        masks = _iotas((x, y))
        sh = [tuple(h.at[f] for h in sh_all) for f in range(nf)]
        _step_body(s0_ref, sh, cs, s1_ref, nz, masks)
        vals = [s1_ref[f, z] for f in range(nf) for z in range(nz)]
        _pack_edges(vals, xf_ref, xl_ref, yf_ref, yl_ref)

    state = jax.ShapeDtypeStruct((nf, nz, x, y), F32)
    return pl.pallas_call(
        kernel,
        out_shape=(state,) + _edge_shapes(nplanes, x, y) + (state,) + _edge_shapes(_rows(nplanes), x, y),
        in_specs=[pl.BlockSpec(memory_space=SMEM)] + [pl.BlockSpec(memory_space=VMEM)] * 6,
        scratch_shapes=_halo_scratch(nf, nz, x, y) + [pltpu.VMEM((5 * NCOEF, x, y), F32)],
    )(scales, pieces, coef, *c_halo)


def step_call(s, s_halo, coef, c_halo, c_first, with_edges):
    nf, nz, x, y = s.shape

    def kernel(*refs):
        s_ref, sxm, sxp, sym, syp, c_ref, cxm, cxp, cym, cyp = refs[:10]
        rest = refs[10:]
        if with_edges:
            o_ref, xf_ref, xl_ref, yf_ref, yl_ref = rest[:5]
            scratch = rest[5:]
        else:
            o_ref = rest[0]
            scratch = rest[1:]
        sh_all = scratch[0:4]
        cs = scratch[4]
        _expand_halo(sxm, sxp, sym, syp, 0, nf, nz, sh_all)
        _coef_table(c_ref, cxm, cxp, cym, cyp, c_first, cs)
        masks = _iotas((x, y))
        sh = [tuple(h.at[f] for h in sh_all) for f in range(nf)]
        _step_body(s_ref, sh, cs, o_ref, nz, masks)
        if with_edges:
            vals = [o_ref[f, z] for f in range(nf) for z in range(nz)]
            _pack_edges(vals, xf_ref, xl_ref, yf_ref, yl_ref)

    out_shape = (jax.ShapeDtypeStruct(s.shape, F32),)
    if with_edges:
        out_shape = out_shape + _edge_shapes(_rows(nf * nz), x, y)
    res = pl.pallas_call(
        kernel,
        out_shape=out_shape,
        scratch_shapes=_halo_scratch(nf, nz, x, y) + [pltpu.VMEM((5 * NCOEF, x, y), F32)],
    )(s, *s_halo, coef, *c_halo)
    return res if with_edges else res[0]


def adjoint_call(s, s_halo, a, a_halo, a_first, coef, c_halo, c_first, with_edges):
    nf, nz, x, y = s.shape

    def kernel(*refs):
        s_ref, sxm, sxp, sym, syp, a_ref, axm, axp, aym, ayp, c_ref, cxm, cxp, cym, cyp = refs[:15]
        rest = refs[15:]
        if with_edges:
            o_ref, xf_ref, xl_ref, yf_ref, yl_ref = rest[:5]
            scratch = rest[5:]
        else:
            o_ref = rest[0]
            scratch = rest[1:]
        sh_all = scratch[0:4]
        ah_all = scratch[4:8]
        cs = scratch[8]
        _expand_halo(sxm, sxp, sym, syp, 0, nf, nz, sh_all)
        _expand_halo(axm, axp, aym, ayp, a_first, nf, nz, ah_all)
        _coef_table(c_ref, cxm, cxp, cym, cyp, c_first, cs)
        masks = _iotas((x, y))
        sh = [tuple(h.at[f] for h in sh_all) for f in range(nf)]
        ah = [tuple(h.at[f] for h in ah_all) for f in range(nf)]
        _adjoint_body(s_ref, sh, a_ref, ah, cs, o_ref, nz, masks)
        if with_edges:
            vals = [o_ref[f, z] for f in range(nf) for z in range(nz)]
            _pack_edges(vals, xf_ref, xl_ref, yf_ref, yl_ref)

    out_shape = (jax.ShapeDtypeStruct(s.shape, F32),)
    if with_edges:
        out_shape = out_shape + _edge_shapes(_rows(nf * nz), x, y)
    res = pl.pallas_call(
        kernel,
        out_shape=out_shape,
        scratch_shapes=_halo_scratch(nf, nz, x, y)
        + _halo_scratch(nf, nz, x, y)
        + [pltpu.VMEM((5 * NCOEF, x, y), F32)],
    )(s, *s_halo, a, *a_halo, coef, *c_halo)
    return res if with_edges else res[0]


def _shift(v, axis, step):
    n = lax.axis_size(axis)
    if step > 0:
        pairs = [(i, i + 1) for i in range(n - 1)]
    else:
        pairs = [(i + 1, i) for i in range(n - 1)]
    return lax.ppermute(v, axis, pairs)


def exchange(xf, xl, yf, yl):
    return (
        _shift(xl, "gx", 1),
        _shift(xf, "gx", -1),
        _shift(yl, "gy", 1),
        _shift(yf, "gy", -1),
    )


def forward_call(holder, held, xm_rows, xp_rows, per):
    n, planes, x, y = held.shape

    def kernel(hold_ref, h_ref, m_ref, p_ref, o_ref):
        row, lane = _iotas((x, y))
        for g in range(n):
            h = hold_ref[g]
            for i in range(per):
                o_ref[g, i] = h_ref[h, i]
            hm = m_ref[h].astype(F32)
            hp = p_ref[h].astype(F32)
            o_ref[g, per] = jnp.where(row < per, hm, _roll(hp, per, 0)).astype(o_ref.dtype)
            own = h_ref[h, per].astype(F32)
            sc = jnp.where(row == 0, own, jnp.where(row == 1, _roll(hm, 1 - per, 0), _roll(hp, 2 - per, 0)))
            o_ref[g, per + 1] = jnp.where(row < 3, sc, 0.0).astype(o_ref.dtype)
            cols = jnp.zeros((x, y), F32)
            scl = jnp.zeros((x, y), F32)
            if g > 0:
                hl = hold_ref[g - 1]
                for i in range(per):
                    v = h_ref[hl, i].astype(F32)
                    cols = jnp.where(lane == i, _roll(v, i - (y - 1), 1), cols)
                scl = jnp.where(lane < per, h_ref[hl, per].astype(F32), scl)
            if g < n - 1:
                hr = hold_ref[g + 1]
                for i in range(per):
                    v = h_ref[hr, i].astype(F32)
                    cols = jnp.where(lane == per + i, _roll(v, per + i, 1), cols)
                sv = _roll(h_ref[hr, per].astype(F32), per, 1)
                scl = jnp.where((lane >= per) & (lane < 2 * per), sv, scl)
            o_ref[g, per + 2] = cols.astype(o_ref.dtype)
            o_ref[g, per + 3] = scl.astype(o_ref.dtype)

    return pl.pallas_call(
        kernel,
        out_shape=jax.ShapeDtypeStruct((n, per + 4, x, y), held.dtype),
        in_specs=[pl.BlockSpec(memory_space=SMEM)] + [pl.BlockSpec(memory_space=VMEM)] * 3,
    )(holder, held, xm_rows, xp_rows)


def route_blocks(stored_slab, block_scales, holder):
    nf, nz, x, y = stored_slab.shape
    n = lax.axis_size("gy")
    nplanes = nf * nz
    per = nplanes // n
    slab = stored_slab.reshape(n, per, x, y)
    sc = jnp.pad(block_scales.reshape(n, 1, 1, per), ((0, 0), (0, 0), (0, x - 1), (0, y - per)))
    held = lax.all_to_all(jnp.concatenate([slab, sc], axis=1), "gy", 0, 0, tiled=True)
    pad = ((0, 0), (0, x - per - 1), (0, 0))
    first = jnp.pad(jnp.concatenate([held[:, :per, 0, :], held[:, per:, 0, :]], axis=1), pad)
    last = jnp.pad(jnp.concatenate([held[:, :per, x - 1, :], held[:, per:, 0, :]], axis=1), pad)
    forward = forward_call(holder, held, _shift(last, "gx", 1), _shift(first, "gx", -1), per)
    return lax.all_to_all(forward, "gy", 0, 0, tiled=True)


def on_device(stored_slab, block_scales, holder, soil_class, soil_table, cotangent):
    nf, nz, x, y = stored_slab.shape
    nplanes = nf * nz

    pieces = route_blocks(stored_slab, block_scales, holder)

    coef, cxf, cxl, cyf, cyl = prep_call(soil_class, soil_table, cotangent)
    c_halo = exchange(cxf, cxl, cyf, cyl)
    c_first = nplanes
    per = nplanes // pieces.shape[0]
    scales = jnp.concatenate(
        [
            pieces[:, per + 1, 0:3, :per].transpose(1, 0, 2).reshape(3, nplanes),
            pieces[:, per + 3, 0, : 2 * per].reshape(-1, 2, per).transpose(1, 0, 2).reshape(2, nplanes),
        ]
    ).astype(F32).reshape(-1)
    res = state0_step_call(pieces, scales, nf, per, coef, c_halo, c_first)
    s0, s0_halo, s1, s1_edges = res[0], res[1:5], res[5], res[6:10]
    s1_halo = exchange(*s1_edges)

    a1, *a1_edges = adjoint_call(
        s1, s1_halo, cotangent, c_halo, 0, coef, c_halo, c_first, True
    )
    a1_halo = exchange(*a1_edges)
    s2 = step_call(s1, s1_halo, coef, c_halo, c_first, False)

    sens = adjoint_call(s0, s0_halo, a1, a1_halo, 0, coef, c_halo, c_first, False)
    return (s2, sens)


def solution(mesh):
    placed = (
        P(None, None, "gx", "gy"),
        P(None, None, "gx", "gy"),
        P(),
        P("gx", "gy"),
        P(),
        P(None, None, "gx", "gy"),
    )
    return jax.shard_map(
        on_device,
        mesh=mesh,
        in_specs=placed,
        out_specs=(P(None, None, "gx", "gy"), P(None, None, "gx", "gy")),
        check_vma=False,
    )
```

```python
import jax
import jax.numpy as jnp
from jax.sharding import Mesh
from jax import lax
from jax.experimental import pallas as pl
from jax.experimental.pallas import tpu as pltpu
from jax.sharding import PartitionSpec as P

F32 = jnp.float32
NCOEF = 4
UNROLL = 8
GY = ("ga", "gb")
VMEM = pltpu.MemorySpace.VMEM
SMEM = pltpu.MemorySpace.SMEM


def _roll(v, shift, axis):
    shift = shift % v.shape[axis]
    if shift == 0:
        return v
    return pltpu.roll(v, shift, axis)


def _iotas(shape):
    return lax.broadcasted_iota(jnp.int32, shape, 0), lax.broadcasted_iota(jnp.int32, shape, 1)


def _pack_edges(vals, xf_ref, xl_ref, yf_ref, yl_ref):
    x, y = vals[0].shape
    _, lane = _iotas((x, y))
    xf_ref[...] = jnp.zeros(xf_ref.shape, F32)
    xl_ref[...] = jnp.zeros(xl_ref.shape, F32)
    yf = jnp.zeros((x, y), F32)
    yl = jnp.zeros((x, y), F32)
    for k, v in enumerate(vals):
        xf_ref[k : k + 1, :] = v[0:1, :]
        xl_ref[k : k + 1, :] = v[x - 1 : x, :]
        yf = jnp.where(lane == k, _roll(v, k, 1), yf)
        yl = jnp.where(lane == k, _roll(v, k - (y - 1), 1), yl)
    yf_ref[...] = yf
    yl_ref[...] = yl


def _expand_halo(xm_ref, xp_ref, ym_ref, yp_ref, first, nf, nz, dst):
    hxm, hxp, hym, hyp = dst
    x, y = hxm.shape[2], hxm.shape[3]
    ymv = ym_ref[...]
    ypv = yp_ref[...]
    for f in range(nf):
        for z in range(nz):
            k = first + f * nz + z
            hxm[f, z] = jnp.broadcast_to(xm_ref[k : k + 1, :], (x, y))
            hxp[f, z] = jnp.broadcast_to(xp_ref[k : k + 1, :], (x, y))
            hym[f, z] = _roll(ymv, -k, 1)
            hyp[f, z] = _roll(ypv, (y - 1) - k, 1)


def _coef_table(c_ref, cxm_ref, cxp_ref, cym_ref, cyp_ref, first, cs):
    x, y = c_ref.shape[1], c_ref.shape[2]
    ymv = cym_ref[...]
    ypv = cyp_ref[...]
    masks = _iotas((x, y))
    for k in range(NCOEF):
        r = first + k
        cv = c_ref[k]
        cs[k] = cv
        halo = (
            jnp.broadcast_to(cxm_ref[r : r + 1, :], (x, y)),
            jnp.broadcast_to(cxp_ref[r : r + 1, :], (x, y)),
            _roll(ymv, -r, 1),
            _roll(ypv, (y - 1) - r, 1),
        )
        for d, v in enumerate(_neighbours(cv, 0, [h[None] for h in halo], masks)):
            cs[4 + 4 * d + k] = v


def _neighbours(v, z, h, masks):
    row, lane = masks
    x, y = v.shape
    hxm, hxp, hym, hyp = h
    return (
        jnp.where(row == 0, hxm[z], _roll(v, 1, 0)),
        jnp.where(row == x - 1, hxp[z], _roll(v, x - 1, 0)),
        jnp.where(lane == 0, hym[z], _roll(v, 1, 1)),
        jnp.where(lane == y - 1, hyp[z], _roll(v, y - 1, 1)),
    )


def _field_at(ref, f, z, nz):
    zm = jnp.maximum(z - 1, 0)
    zp = jnp.minimum(z + 1, nz - 1)
    vm = jnp.where(z > 0, 1.0, 0.0).astype(F32)
    vp = jnp.where(z < nz - 1, 1.0, 0.0).astype(F32)
    return ref[f, z], ref[f, zm] * vm, ref[f, zp] * vp, vm, vp


def _gains(b):
    return 1.5 + b, 1.5 + 0.5 * b


def _step_body(s_ref, sh, cs, o_ref, nz, masks):
    def body(z, carry):
        u, u_m, u_p, vm, vp = _field_at(s_ref, 0, z, nz)
        t, t_m, t_p, _, _ = _field_at(s_ref, 1, z, nz)
        c = [cs[k] for k in range(NCOEF)]
        g1, g2 = _gains(jnp.tanh(u))
        kw, dtv, lamb, kv = c[0] * g1, c[1] * g2, c[2] * g2, c[3] * g1
        a1 = jnp.zeros_like(u)
        a2 = jnp.zeros_like(u)
        for un, tn, valid in ((u_m, t_m, vm), (u_p, t_p, vp)):
            g1n, g2n = _gains(jnp.tanh(un))
            a1 = a1 + (g1 + valid * g1n) * (un - u)
            a2 = a2 + (g2 + valid * g2n) * (tn - t)
        f0 = c[0] * a1 + c[1] * a2
        f1 = c[2] * a2 + c[3] * a1
        uns = _neighbours(u, z, sh[0], masks)
        tns = _neighbours(t, z, sh[1], masks)
        for d in range(4):
            un, tn = uns[d], tns[d]
            g1n, g2n = _gains(jnp.tanh(un))
            cn = [cs[4 + 4 * d + k] for k in range(NCOEF)]
            du = un - u
            dt = tn - t
            f0 = f0 + (kw + cn[0] * g1n) * du + (dtv + cn[1] * g2n) * dt
            f1 = f1 + (lamb + cn[2] * g2n) * dt + (kv + cn[3] * g1n) * du
        o_ref[0, z] = u + 0.5 * f0
        o_ref[1, z] = t + 0.5 * f1
        return carry

    lax.fori_loop(0, nz, body, 0, unroll=UNROLL)


def _adjoint_body(s_ref, sh, a_ref, ah, cs, o_ref, nz, masks):
    def body(z, carry):
        u, u_m, u_p, vm, vp = _field_at(s_ref, 0, z, nz)
        t, t_m, t_p, _, _ = _field_at(s_ref, 1, z, nz)
        a0, a0_m, a0_p, _, _ = _field_at(a_ref, 0, z, nz)
        a1, a1_m, a1_p, _, _ = _field_at(a_ref, 1, z, nz)
        c = [cs[k] for k in range(NCOEF)]
        b = jnp.tanh(u)
        g1, g2 = _gains(b)
        kw, dtv, lamb, kv = c[0] * g1, c[1] * g2, c[2] * g2, c[3] * g1
        zero = jnp.zeros_like(u)
        p10, p11, p20, p21 = zero, zero, zero, zero
        gu0, gu1, gt0, gt1 = zero, zero, zero, zero
        for un, tn, a0n, a1n, valid in ((u_m, t_m, a0_m, a1_m, vm), (u_p, t_p, a0_p, a1_p, vp)):
            g1n, g2n = _gains(jnp.tanh(un))
            s1 = g1 + valid * g1n
            s2 = g2 + valid * g2n
            du, dt, da0, da1 = un - u, tn - t, a0n - a0, a1n - a1
            p10 = p10 + s1 * da0
            p11 = p11 + s1 * da1
            p20 = p20 + s2 * da0
            p21 = p21 + s2 * da1
            gu0 = gu0 + du * da0
            gu1 = gu1 + du * da1
            gt0 = gt0 + dt * da0
            gt1 = gt1 + dt * da1
        ju = c[0] * p10 + c[3] * p11
        jt = c[1] * p20 + c[2] * p21
        uns = _neighbours(u, z, sh[0], masks)
        tns = _neighbours(t, z, sh[1], masks)
        a0ns = _neighbours(a0, z, ah[0], masks)
        a1ns = _neighbours(a1, z, ah[1], masks)
        for d in range(4):
            un, tn, a0n, a1n = uns[d], tns[d], a0ns[d], a1ns[d]
            g1n, g2n = _gains(jnp.tanh(un))
            cn = [cs[4 + 4 * d + k] for k in range(NCOEF)]
            du, dt, da0, da1 = un - u, tn - t, a0n - a0, a1n - a1
            ju = ju + (kw + cn[0] * g1n) * da0 + (kv + cn[3] * g1n) * da1
            jt = jt + (dtv + cn[1] * g2n) * da0 + (lamb + cn[2] * g2n) * da1
            gu0 = gu0 + du * da0
            gu1 = gu1 + du * da1
            gt0 = gt0 + dt * da0
            gt1 = gt1 + dt * da1
        gsum = c[0] * gu0 + c[3] * gu1 + 0.5 * (c[1] * gt0 + c[2] * gt1)
        o_ref[0, z] = a0 + 0.5 * ju - 0.5 * (1.0 - b * b) * gsum
        o_ref[1, z] = a1 + 0.5 * jt
        return carry

    lax.fori_loop(0, nz, body, 0, unroll=UNROLL)


def _halo_scratch(nf, nz, x, y):
    return [pltpu.VMEM((nf, nz, x, y), F32) for _ in range(4)]


def _edge_shapes(rows, x, y):
    return (
        jax.ShapeDtypeStruct((rows, y), F32),
        jax.ShapeDtypeStruct((rows, y), F32),
        jax.ShapeDtypeStruct((x, y), F32),
        jax.ShapeDtypeStruct((x, y), F32),
    )


def _rows(n):
    return -(-n // 8) * 8


def prep_call(soil_class, soil_table, cot, slab, scales):
    nf, nz, x, y = cot.shape
    nclass = soil_table.shape[0]
    nplanes = nf * nz

    def kernel(cls_ref, tab_ref, sc_ref, cot_ref, slab_ref, coef_ref, xf_ref, xl_ref, yf_ref, yl_ref):
        cls = cls_ref[...]
        coefs = []
        for k in range(NCOEF):
            cv = jnp.zeros(cls.shape, F32)
            for j in range(nclass):
                cv = jnp.where(cls == j, tab_ref[j, k], cv)
            coef_ref[k] = cv
            coefs.append(cv)
        vals = [cot_ref[f, z] for f in range(nf) for z in range(nz)] + coefs
        _pack_edges(vals, xf_ref, xl_ref, yf_ref, yl_ref)
        base = len(vals)
        for k in range(nplanes):
            v = slab_ref[k // nz, k % nz].astype(F32)
            xf_ref[base + k : base + k + 1, :] = v[0:1, :]
            xl_ref[base + k : base + k + 1, :] = v[x - 1 : x, :]
        _, lane = _iotas((1, y))
        row = jnp.zeros((1, y), F32)
        for k in range(nplanes):
            row = jnp.where(lane == k, sc_ref[k], row)
        xf_ref[base + nplanes : base + nplanes + 1, :] = row
        xl_ref[base + nplanes : base + nplanes + 1, :] = row

    rows = _rows(2 * nplanes + NCOEF + 1)
    return pl.pallas_call(
        kernel,
        out_shape=(jax.ShapeDtypeStruct((NCOEF, x, y), F32),)
        + _edge_shapes(rows, x, y)[:2]
        + _edge_shapes(8, x, y)[2:],
        in_specs=[
            pl.BlockSpec(memory_space=VMEM),
            pl.BlockSpec(memory_space=SMEM),
            pl.BlockSpec(memory_space=SMEM),
            pl.BlockSpec(memory_space=VMEM),
            pl.BlockSpec(memory_space=VMEM),
        ],
    )(soil_class, soil_table, scales, cot, slab)


def _state0_body(sc_ref, r_ref, s_ref, xm_ref, xp_ref, ym_ref, yp_ref, per):
    nz, x, y = s_ref.shape[1], s_ref.shape[2], s_ref.shape[3]
    nplanes = s_ref.shape[0] * nz
    _, lane = _iotas((x, y))
    ym = jnp.zeros((x, y), F32)
    yp = jnp.zeros((x, y), F32)
    for k in range(nplanes):
        p, i = k // per, k % per
        s_ref[k // nz, k % nz] = r_ref[p, i].astype(F32) * sc_ref[k]
        hx = r_ref[p, per].astype(F32)
        xm_ref[k : k + 1, :] = hx[i : i + 1, :] * sc_ref[nplanes + k]
        xp_ref[k : k + 1, :] = hx[per + i : per + i + 1, :] * sc_ref[2 * nplanes + k]
        hy = r_ref[p, per + 2].astype(F32)
        ym = jnp.where(lane == k, _roll(hy, k - i, 1) * sc_ref[3 * nplanes + k], ym)
        yp = jnp.where(lane == k, _roll(hy, k - (per + i), 1) * sc_ref[4 * nplanes + k], yp)
    ym_ref[...] = ym
    yp_ref[...] = yp


def state0_step_call(pieces, scales, nf, per, coef, c_halo, c_first):
    npiece, _, x, y = pieces.shape
    nplanes = npiece * per
    nz = nplanes // nf

    def kernel(sc_ref, r_ref, c_ref, cxm, cxp, cym, cyp, *refs):
        s0_ref, xm_ref, xp_ref, ym_ref, yp_ref = refs[:5]
        s1_ref, xf_ref, xl_ref, yf_ref, yl_ref = refs[5:10]
        scratch = refs[10:]
        sh_all = scratch[0:4]
        cs = scratch[4]
        _state0_body(sc_ref, r_ref, s0_ref, xm_ref, xp_ref, ym_ref, yp_ref, per)
        _expand_halo(xm_ref, xp_ref, ym_ref, yp_ref, 0, nf, nz, sh_all)
        _coef_table(c_ref, cxm, cxp, cym, cyp, c_first, cs)
        masks = _iotas((x, y))
        sh = [tuple(h.at[f] for h in sh_all) for f in range(nf)]
        _step_body(s0_ref, sh, cs, s1_ref, nz, masks)
        vals = [s1_ref[f, z] for f in range(nf) for z in range(nz)]
        _pack_edges(vals, xf_ref, xl_ref, yf_ref, yl_ref)

    state = jax.ShapeDtypeStruct((nf, nz, x, y), F32)
    return pl.pallas_call(
        kernel,
        out_shape=(state,) + _edge_shapes(nplanes, x, y) + (state,) + _edge_shapes(_rows(nplanes), x, y),
        in_specs=[pl.BlockSpec(memory_space=SMEM)] + [pl.BlockSpec(memory_space=VMEM)] * 6,
        scratch_shapes=_halo_scratch(nf, nz, x, y) + [pltpu.VMEM((5 * NCOEF, x, y), F32)],
    )(scales, pieces, coef, *c_halo)


def step_call(s, s_halo, coef, c_halo, c_first, with_edges):
    nf, nz, x, y = s.shape

    def kernel(*refs):
        s_ref, sxm, sxp, sym, syp, c_ref, cxm, cxp, cym, cyp = refs[:10]
        rest = refs[10:]
        if with_edges:
            o_ref, xf_ref, xl_ref, yf_ref, yl_ref = rest[:5]
            scratch = rest[5:]
        else:
            o_ref = rest[0]
            scratch = rest[1:]
        sh_all = scratch[0:4]
        cs = scratch[4]
        _expand_halo(sxm, sxp, sym, syp, 0, nf, nz, sh_all)
        _coef_table(c_ref, cxm, cxp, cym, cyp, c_first, cs)
        masks = _iotas((x, y))
        sh = [tuple(h.at[f] for h in sh_all) for f in range(nf)]
        _step_body(s_ref, sh, cs, o_ref, nz, masks)
        if with_edges:
            vals = [o_ref[f, z] for f in range(nf) for z in range(nz)]
            _pack_edges(vals, xf_ref, xl_ref, yf_ref, yl_ref)

    out_shape = (jax.ShapeDtypeStruct(s.shape, F32),)
    if with_edges:
        out_shape = out_shape + _edge_shapes(_rows(nf * nz), x, y)
    res = pl.pallas_call(
        kernel,
        out_shape=out_shape,
        scratch_shapes=_halo_scratch(nf, nz, x, y) + [pltpu.VMEM((5 * NCOEF, x, y), F32)],
    )(s, *s_halo, coef, *c_halo)
    return res if with_edges else res[0]


def adjoint_call(s, s_halo, a, a_halo, a_first, coef, c_halo, c_first, with_edges):
    nf, nz, x, y = s.shape

    def kernel(*refs):
        s_ref, sxm, sxp, sym, syp, a_ref, axm, axp, aym, ayp, c_ref, cxm, cxp, cym, cyp = refs[:15]
        rest = refs[15:]
        if with_edges:
            o_ref, xf_ref, xl_ref, yf_ref, yl_ref = rest[:5]
            scratch = rest[5:]
        else:
            o_ref = rest[0]
            scratch = rest[1:]
        sh_all = scratch[0:4]
        ah_all = scratch[4:8]
        cs = scratch[8]
        _expand_halo(sxm, sxp, sym, syp, 0, nf, nz, sh_all)
        _expand_halo(axm, axp, aym, ayp, a_first, nf, nz, ah_all)
        _coef_table(c_ref, cxm, cxp, cym, cyp, c_first, cs)
        masks = _iotas((x, y))
        sh = [tuple(h.at[f] for h in sh_all) for f in range(nf)]
        ah = [tuple(h.at[f] for h in ah_all) for f in range(nf)]
        _adjoint_body(s_ref, sh, a_ref, ah, cs, o_ref, nz, masks)
        if with_edges:
            vals = [o_ref[f, z] for f in range(nf) for z in range(nz)]
            _pack_edges(vals, xf_ref, xl_ref, yf_ref, yl_ref)

    out_shape = (jax.ShapeDtypeStruct(s.shape, F32),)
    if with_edges:
        out_shape = out_shape + _edge_shapes(_rows(nf * nz), x, y)
    res = pl.pallas_call(
        kernel,
        out_shape=out_shape,
        scratch_shapes=_halo_scratch(nf, nz, x, y)
        + _halo_scratch(nf, nz, x, y)
        + [pltpu.VMEM((5 * NCOEF, x, y), F32)],
    )(s, *s_halo, a, *a_halo, coef, *c_halo)
    return res if with_edges else res[0]


def _shift(v, axis, step):
    n = lax.axis_size(axis)
    if step > 0:
        pairs = [(i, i + 1) for i in range(n - 1)]
    else:
        pairs = [(i + 1, i) for i in range(n - 1)]
    return lax.ppermute(v, axis, pairs)


def exchange(xf, xl, yf, yl):
    return (
        _shift(xl, "gx", 1),
        _shift(xf, "gx", -1),
        _shift(yl, GY, 1),
        _shift(yf, GY, -1),
    )


def forward_call(holder, held, per):
    n, planes, x, y = held.shape

    def kernel(hold_ref, h_ref, o_ref):
        _, lane = _iotas((x, y))
        for g in range(n):
            h = hold_ref[g]
            for i in range(planes):
                o_ref[g, i] = h_ref[h, i]
            cols = jnp.zeros((x, y), F32)
            scl = jnp.zeros((x, y), F32)
            if g > 0:
                hl = hold_ref[g - 1]
                for i in range(per):
                    v = h_ref[hl, i].astype(F32)
                    cols = jnp.where(lane == i, _roll(v, i - (y - 1), 1), cols)
                scl = jnp.where(lane < per, h_ref[hl, per + 1].astype(F32), scl)
            if g < n - 1:
                hr = hold_ref[g + 1]
                for i in range(per):
                    v = h_ref[hr, i].astype(F32)
                    cols = jnp.where(lane == per + i, _roll(v, per + i, 1), cols)
                sv = _roll(h_ref[hr, per + 1].astype(F32), per, 1)
                scl = jnp.where((lane >= per) & (lane < 2 * per), sv, scl)
            o_ref[g, planes] = cols.astype(o_ref.dtype)
            o_ref[g, planes + 1] = scl.astype(o_ref.dtype)

    return pl.pallas_call(
        kernel,
        out_shape=jax.ShapeDtypeStruct((n, planes + 2, x, y), held.dtype),
        in_specs=[pl.BlockSpec(memory_space=SMEM), pl.BlockSpec(memory_space=VMEM)],
    )(holder, held)


def _all_to_all(v):
    na, nb = lax.axis_size("ga"), lax.axis_size("gb")
    rest = v.shape[1:]
    v = v.reshape((na, nb) + rest)
    v = lax.all_to_all(v, "gb", 1, 1, tiled=True)
    v = lax.all_to_all(v, "ga", 0, 0, tiled=True)
    return v.reshape((na * nb,) + rest)


def route_blocks(stored_slab, block_scales, holder, xm_all, xp_all, first):
    nf, nz, x, y = stored_slab.shape
    n = lax.axis_size(GY)
    nplanes = nf * nz
    per = nplanes // n
    bf = stored_slab.dtype
    slab = stored_slab.reshape(n, per, x, y)
    rows_m = xm_all[first : first + nplanes].astype(bf).reshape(n, per, y)
    rows_p = xp_all[first : first + nplanes].astype(bf).reshape(n, per, y)
    halo = jnp.concatenate([rows_m, rows_p], axis=1)[:, None]
    sc_m = xm_all[first + nplanes, :nplanes].astype(bf).reshape(n, 1, per)
    sc_p = xp_all[first + nplanes, :nplanes].astype(bf).reshape(n, 1, per)
    sc = jnp.concatenate([block_scales.reshape(n, 1, per), sc_m, sc_p], axis=1)
    sc = jnp.pad(sc, ((0, 0), (0, x - 3), (0, y - per)))[:, None]
    held = _all_to_all(jnp.concatenate([slab, halo, sc], axis=1))

    forward = forward_call(holder, held, per)
    return _all_to_all(forward)


def on_device(stored_slab, block_scales, holder, soil_class, soil_table, cotangent):
    nf, nz, x, y = stored_slab.shape
    nplanes = nf * nz

    coef, cxf, cxl, cyf, cyl = prep_call(
        soil_class, soil_table, cotangent, stored_slab, block_scales.reshape(-1).astype(F32)
    )
    c_halo = exchange(cxf, cxl, cyf, cyl)
    c_first = nplanes

    pieces = route_blocks(stored_slab, block_scales, holder, c_halo[0], c_halo[1], nplanes + NCOEF)
    per = nplanes // pieces.shape[0]
    scales = jnp.concatenate(
        [
            pieces[:, per + 1, 0:3, :per].transpose(1, 0, 2).reshape(3, nplanes),
            pieces[:, per + 3, 0, : 2 * per].reshape(-1, 2, per).transpose(1, 0, 2).reshape(2, nplanes),
        ]
    ).astype(F32).reshape(-1)
    res = state0_step_call(pieces, scales, nf, per, coef, c_halo, c_first)
    s0, s0_halo, s1, s1_edges = res[0], res[1:5], res[5], res[6:10]
    s1_halo = exchange(*s1_edges)

    a1, *a1_edges = adjoint_call(
        s1, s1_halo, cotangent, c_halo, 0, coef, c_halo, c_first, True
    )
    a1_halo = exchange(*a1_edges)
    s2 = step_call(s1, s1_halo, coef, c_halo, c_first, False)

    sens = adjoint_call(s0, s0_halo, a1, a1_halo, 0, coef, c_halo, c_first, False)
    return (s2, sens)


def solution(mesh):
    ngx, ngy = mesh.shape["gx"], mesh.shape["gy"]
    nb = 4 if ngy % 4 == 0 else 1
    split = Mesh(mesh.devices.reshape(ngx, ngy // nb, nb), ("gx",) + GY)
    placed = (
        P(None, None, "gx", GY),
        P(None, None, "gx", GY),
        P(),
        P("gx", GY),
        P(),
        P(None, None, "gx", GY),
    )
    return jax.shard_map(
        on_device,
        mesh=split,
        in_specs=placed,
        out_specs=(P(None, None, "gx", GY), P(None, None, "gx", GY)),
        check_vma=False,
    )
```

```python
import jax
import jax.numpy as jnp
from jax import lax
from jax.experimental import pallas as pl
from jax.experimental.pallas import tpu as pltpu
from jax.sharding import PartitionSpec as P

F32 = jnp.float32
NCOEF = 4
UNROLL = 32
VMEM = pltpu.MemorySpace.VMEM
SMEM = pltpu.MemorySpace.SMEM


def _roll(v, shift, axis):
    shift = shift % v.shape[axis]
    if shift == 0:
        return v
    return pltpu.roll(v, shift, axis)


def _iotas(shape):
    return lax.broadcasted_iota(jnp.int32, shape, 0), lax.broadcasted_iota(jnp.int32, shape, 1)


def _pack_edges(vals, xf_ref, xl_ref, yf_ref, yl_ref):
    x, y = vals[0].shape
    _, lane = _iotas((x, y))
    xf_ref[...] = jnp.zeros(xf_ref.shape, F32)
    xl_ref[...] = jnp.zeros(xl_ref.shape, F32)
    yf = jnp.zeros((x, y), F32)
    yl = jnp.zeros((x, y), F32)
    for k, v in enumerate(vals):
        xf_ref[k : k + 1, :] = v[0:1, :]
        xl_ref[k : k + 1, :] = v[x - 1 : x, :]
        yf = jnp.where(lane == k, _roll(v, k, 1), yf)
        yl = jnp.where(lane == k, _roll(v, k - (y - 1), 1), yl)
    yf_ref[...] = yf
    yl_ref[...] = yl


def _expand_halo(xm_ref, xp_ref, ym_ref, yp_ref, first, nf, nz, dst):
    hxm, hxp, hym, hyp = dst
    x, y = hxm.shape[2], hxm.shape[3]
    ymv = ym_ref[...]
    ypv = yp_ref[...]
    for f in range(nf):
        for z in range(nz):
            k = first + f * nz + z
            hxm[f, z] = jnp.broadcast_to(xm_ref[k : k + 1, :], (x, y))
            hxp[f, z] = jnp.broadcast_to(xp_ref[k : k + 1, :], (x, y))
            hym[f, z] = _roll(ymv, -k, 1)
            hyp[f, z] = _roll(ypv, (y - 1) - k, 1)


def _coef_table(c_ref, cxm_ref, cxp_ref, cym_ref, cyp_ref, first, cs):
    x, y = c_ref.shape[1], c_ref.shape[2]
    ymv = cym_ref[...]
    ypv = cyp_ref[...]
    masks = _iotas((x, y))
    for k in range(NCOEF):
        r = first + k
        cv = c_ref[k]
        cs[k] = cv
        halo = (
            jnp.broadcast_to(cxm_ref[r : r + 1, :], (x, y)),
            jnp.broadcast_to(cxp_ref[r : r + 1, :], (x, y)),
            _roll(ymv, -r, 1),
            _roll(ypv, (y - 1) - r, 1),
        )
        for d, v in enumerate(_neighbours(cv, 0, [h[None] for h in halo], masks)):
            cs[4 + 4 * d + k] = v


def _neighbours(v, z, h, masks):
    row, lane = masks
    x, y = v.shape
    hxm, hxp, hym, hyp = h
    return (
        jnp.where(row == 0, hxm[z], _roll(v, 1, 0)),
        jnp.where(row == x - 1, hxp[z], _roll(v, x - 1, 0)),
        jnp.where(lane == 0, hym[z], _roll(v, 1, 1)),
        jnp.where(lane == y - 1, hyp[z], _roll(v, y - 1, 1)),
    )


def _field_at(ref, f, z, nz):
    zm = jnp.maximum(z - 1, 0)
    zp = jnp.minimum(z + 1, nz - 1)
    vm = jnp.where(z > 0, 1.0, 0.0).astype(F32)
    vp = jnp.where(z < nz - 1, 1.0, 0.0).astype(F32)
    return ref[f, z], ref[f, zm] * vm, ref[f, zp] * vp, vm, vp


def _gains(b):
    return 1.5 + b, 1.5 + 0.5 * b


def _step_body(s_ref, sh, cs, o_ref, nz, masks):
    def body(z, carry):
        u, u_m, u_p, vm, vp = _field_at(s_ref, 0, z, nz)
        t, t_m, t_p, _, _ = _field_at(s_ref, 1, z, nz)
        c = [cs[k] for k in range(NCOEF)]
        g1, g2 = _gains(jnp.tanh(u))
        kw, dtv, lamb, kv = c[0] * g1, c[1] * g2, c[2] * g2, c[3] * g1
        a1 = jnp.zeros_like(u)
        a2 = jnp.zeros_like(u)
        for un, tn, valid in ((u_m, t_m, vm), (u_p, t_p, vp)):
            g1n, g2n = _gains(jnp.tanh(un))
            a1 = a1 + (g1 + valid * g1n) * (un - u)
            a2 = a2 + (g2 + valid * g2n) * (tn - t)
        f0 = c[0] * a1 + c[1] * a2
        f1 = c[2] * a2 + c[3] * a1
        uns = _neighbours(u, z, sh[0], masks)
        tns = _neighbours(t, z, sh[1], masks)
        for d in range(4):
            un, tn = uns[d], tns[d]
            g1n, g2n = _gains(jnp.tanh(un))
            cn = [cs[4 + 4 * d + k] for k in range(NCOEF)]
            du = un - u
            dt = tn - t
            f0 = f0 + (kw + cn[0] * g1n) * du + (dtv + cn[1] * g2n) * dt
            f1 = f1 + (lamb + cn[2] * g2n) * dt + (kv + cn[3] * g1n) * du
        o_ref[0, z] = u + 0.5 * f0
        o_ref[1, z] = t + 0.5 * f1
        return carry

    lax.fori_loop(0, nz, body, 0, unroll=UNROLL)


def _adjoint_body(s_ref, sh, a_ref, ah, cs, o_ref, nz, masks):
    def body(z, carry):
        u, u_m, u_p, vm, vp = _field_at(s_ref, 0, z, nz)
        t, t_m, t_p, _, _ = _field_at(s_ref, 1, z, nz)
        a0, a0_m, a0_p, _, _ = _field_at(a_ref, 0, z, nz)
        a1, a1_m, a1_p, _, _ = _field_at(a_ref, 1, z, nz)
        c = [cs[k] for k in range(NCOEF)]
        b = jnp.tanh(u)
        g1, g2 = _gains(b)
        kw, dtv, lamb, kv = c[0] * g1, c[1] * g2, c[2] * g2, c[3] * g1
        zero = jnp.zeros_like(u)
        p10, p11, p20, p21 = zero, zero, zero, zero
        gu0, gu1, gt0, gt1 = zero, zero, zero, zero
        for un, tn, a0n, a1n, valid in ((u_m, t_m, a0_m, a1_m, vm), (u_p, t_p, a0_p, a1_p, vp)):
            g1n, g2n = _gains(jnp.tanh(un))
            s1 = g1 + valid * g1n
            s2 = g2 + valid * g2n
            du, dt, da0, da1 = un - u, tn - t, a0n - a0, a1n - a1
            p10 = p10 + s1 * da0
            p11 = p11 + s1 * da1
            p20 = p20 + s2 * da0
            p21 = p21 + s2 * da1
            gu0 = gu0 + du * da0
            gu1 = gu1 + du * da1
            gt0 = gt0 + dt * da0
            gt1 = gt1 + dt * da1
        ju = c[0] * p10 + c[3] * p11
        jt = c[1] * p20 + c[2] * p21
        uns = _neighbours(u, z, sh[0], masks)
        tns = _neighbours(t, z, sh[1], masks)
        a0ns = _neighbours(a0, z, ah[0], masks)
        a1ns = _neighbours(a1, z, ah[1], masks)
        for d in range(4):
            un, tn, a0n, a1n = uns[d], tns[d], a0ns[d], a1ns[d]
            g1n, g2n = _gains(jnp.tanh(un))
            cn = [cs[4 + 4 * d + k] for k in range(NCOEF)]
            du, dt, da0, da1 = un - u, tn - t, a0n - a0, a1n - a1
            ju = ju + (kw + cn[0] * g1n) * da0 + (kv + cn[3] * g1n) * da1
            jt = jt + (dtv + cn[1] * g2n) * da0 + (lamb + cn[2] * g2n) * da1
            gu0 = gu0 + du * da0
            gu1 = gu1 + du * da1
            gt0 = gt0 + dt * da0
            gt1 = gt1 + dt * da1
        gsum = c[0] * gu0 + c[3] * gu1 + 0.5 * (c[1] * gt0 + c[2] * gt1)
        o_ref[0, z] = a0 + 0.5 * ju - 0.5 * (1.0 - b * b) * gsum
        o_ref[1, z] = a1 + 0.5 * jt
        return carry

    lax.fori_loop(0, nz, body, 0, unroll=UNROLL)


def _halo_scratch(nf, nz, x, y):
    return [pltpu.VMEM((nf, nz, x, y), F32) for _ in range(4)]


def _edge_shapes(rows, x, y):
    return (
        jax.ShapeDtypeStruct((rows, y), F32),
        jax.ShapeDtypeStruct((rows, y), F32),
        jax.ShapeDtypeStruct((x, y), F32),
        jax.ShapeDtypeStruct((x, y), F32),
    )


def _rows(n):
    return -(-n // 8) * 8


def prep_call(soil_class, soil_table, cot, slab, scales):
    nf, nz, x, y = cot.shape
    nclass = soil_table.shape[0]
    nplanes = nf * nz

    def kernel(cls_ref, tab_ref, sc_ref, cot_ref, slab_ref, coef_ref, xf_ref, xl_ref, yf_ref, yl_ref):
        cls = cls_ref[...]
        coefs = []
        for k in range(NCOEF):
            cv = jnp.zeros(cls.shape, F32)
            for j in range(nclass):
                cv = jnp.where(cls == j, tab_ref[j, k], cv)
            coef_ref[k] = cv
            coefs.append(cv)
        vals = [cot_ref[f, z] for f in range(nf) for z in range(nz)] + coefs
        _pack_edges(vals, xf_ref, xl_ref, yf_ref, yl_ref)
        base = len(vals)
        for k in range(nplanes):
            v = slab_ref[k // nz, k % nz].astype(F32)
            xf_ref[base + k : base + k + 1, :] = v[0:1, :]
            xl_ref[base + k : base + k + 1, :] = v[x - 1 : x, :]
        _, lane = _iotas((1, y))
        row = jnp.zeros((1, y), F32)
        for k in range(nplanes):
            row = jnp.where(lane == k, sc_ref[k], row)
        xf_ref[base + nplanes : base + nplanes + 1, :] = row
        xl_ref[base + nplanes : base + nplanes + 1, :] = row

    rows = _rows(2 * nplanes + NCOEF + 1)
    return pl.pallas_call(
        kernel,
        out_shape=(jax.ShapeDtypeStruct((NCOEF, x, y), F32),)
        + _edge_shapes(rows, x, y)[:2]
        + _edge_shapes(8, x, y)[2:],
        in_specs=[
            pl.BlockSpec(memory_space=VMEM),
            pl.BlockSpec(memory_space=SMEM),
            pl.BlockSpec(memory_space=SMEM),
            pl.BlockSpec(memory_space=VMEM),
            pl.BlockSpec(memory_space=VMEM),
        ],
    )(soil_class, soil_table, scales, cot, slab)


def _state0_body(sc_ref, r_ref, s_ref, xm_ref, xp_ref, ym_ref, yp_ref, per):
    nz, x, y = s_ref.shape[1], s_ref.shape[2], s_ref.shape[3]
    nplanes = s_ref.shape[0] * nz
    _, lane = _iotas((x, y))
    ym = jnp.zeros((x, y), F32)
    yp = jnp.zeros((x, y), F32)
    for k in range(nplanes):
        p, i = k // per, k % per
        s_ref[k // nz, k % nz] = r_ref[p, i].astype(F32) * sc_ref[k]
        hx = r_ref[p, per].astype(F32)
        xm_ref[k : k + 1, :] = hx[i : i + 1, :] * sc_ref[nplanes + k]
        xp_ref[k : k + 1, :] = hx[per + i : per + i + 1, :] * sc_ref[2 * nplanes + k]
        hy = r_ref[p, per + 2].astype(F32)
        ym = jnp.where(lane == k, _roll(hy, k - i, 1) * sc_ref[3 * nplanes + k], ym)
        yp = jnp.where(lane == k, _roll(hy, k - (per + i), 1) * sc_ref[4 * nplanes + k], yp)
    ym_ref[...] = ym
    yp_ref[...] = yp


def state0_step_call(pieces, scales, nf, per, coef, c_halo, c_first):
    npiece, _, x, y = pieces.shape
    nplanes = npiece * per
    nz = nplanes // nf

    def kernel(sc_ref, r_ref, c_ref, cxm, cxp, cym, cyp, *refs):
        s0_ref, xm_ref, xp_ref, ym_ref, yp_ref = refs[:5]
        s1_ref, xf_ref, xl_ref, yf_ref, yl_ref = refs[5:10]
        scratch = refs[10:]
        sh_all = scratch[0:4]
        cs = scratch[4]
        _state0_body(sc_ref, r_ref, s0_ref, xm_ref, xp_ref, ym_ref, yp_ref, per)
        _expand_halo(xm_ref, xp_ref, ym_ref, yp_ref, 0, nf, nz, sh_all)
        _coef_table(c_ref, cxm, cxp, cym, cyp, c_first, cs)
        masks = _iotas((x, y))
        sh = [tuple(h.at[f] for h in sh_all) for f in range(nf)]
        _step_body(s0_ref, sh, cs, s1_ref, nz, masks)
        vals = [s1_ref[f, z] for f in range(nf) for z in range(nz)]
        _pack_edges(vals, xf_ref, xl_ref, yf_ref, yl_ref)

    state = jax.ShapeDtypeStruct((nf, nz, x, y), F32)
    return pl.pallas_call(
        kernel,
        out_shape=(state,) + _edge_shapes(nplanes, x, y) + (state,) + _edge_shapes(_rows(nplanes), x, y),
        in_specs=[pl.BlockSpec(memory_space=SMEM)] + [pl.BlockSpec(memory_space=VMEM)] * 6,
        scratch_shapes=_halo_scratch(nf, nz, x, y) + [pltpu.VMEM((5 * NCOEF, x, y), F32)],
    )(scales, pieces, coef, *c_halo)


def step_call(s, s_halo, coef, c_halo, c_first, with_edges):
    nf, nz, x, y = s.shape

    def kernel(*refs):
        s_ref, sxm, sxp, sym, syp, c_ref, cxm, cxp, cym, cyp = refs[:10]
        rest = refs[10:]
        if with_edges:
            o_ref, xf_ref, xl_ref, yf_ref, yl_ref = rest[:5]
            scratch = rest[5:]
        else:
            o_ref = rest[0]
            scratch = rest[1:]
        sh_all = scratch[0:4]
        cs = scratch[4]
        _expand_halo(sxm, sxp, sym, syp, 0, nf, nz, sh_all)
        _coef_table(c_ref, cxm, cxp, cym, cyp, c_first, cs)
        masks = _iotas((x, y))
        sh = [tuple(h.at[f] for h in sh_all) for f in range(nf)]
        _step_body(s_ref, sh, cs, o_ref, nz, masks)
        if with_edges:
            vals = [o_ref[f, z] for f in range(nf) for z in range(nz)]
            _pack_edges(vals, xf_ref, xl_ref, yf_ref, yl_ref)

    out_shape = (jax.ShapeDtypeStruct(s.shape, F32),)
    if with_edges:
        out_shape = out_shape + _edge_shapes(_rows(nf * nz), x, y)
    res = pl.pallas_call(
        kernel,
        out_shape=out_shape,
        scratch_shapes=_halo_scratch(nf, nz, x, y) + [pltpu.VMEM((5 * NCOEF, x, y), F32)],
    )(s, *s_halo, coef, *c_halo)
    return res if with_edges else res[0]


def adjoint_call(s, s_halo, a, a_halo, a_first, coef, c_halo, c_first, with_edges):
    nf, nz, x, y = s.shape

    def kernel(*refs):
        s_ref, sxm, sxp, sym, syp, a_ref, axm, axp, aym, ayp, c_ref, cxm, cxp, cym, cyp = refs[:15]
        rest = refs[15:]
        if with_edges:
            o_ref, xf_ref, xl_ref, yf_ref, yl_ref = rest[:5]
            scratch = rest[5:]
        else:
            o_ref = rest[0]
            scratch = rest[1:]
        sh_all = scratch[0:4]
        ah_all = scratch[4:8]
        cs = scratch[8]
        _expand_halo(sxm, sxp, sym, syp, 0, nf, nz, sh_all)
        _expand_halo(axm, axp, aym, ayp, a_first, nf, nz, ah_all)
        _coef_table(c_ref, cxm, cxp, cym, cyp, c_first, cs)
        masks = _iotas((x, y))
        sh = [tuple(h.at[f] for h in sh_all) for f in range(nf)]
        ah = [tuple(h.at[f] for h in ah_all) for f in range(nf)]
        _adjoint_body(s_ref, sh, a_ref, ah, cs, o_ref, nz, masks)
        if with_edges:
            vals = [o_ref[f, z] for f in range(nf) for z in range(nz)]
            _pack_edges(vals, xf_ref, xl_ref, yf_ref, yl_ref)

    out_shape = (jax.ShapeDtypeStruct(s.shape, F32),)
    if with_edges:
        out_shape = out_shape + _edge_shapes(_rows(nf * nz), x, y)
    res = pl.pallas_call(
        kernel,
        out_shape=out_shape,
        scratch_shapes=_halo_scratch(nf, nz, x, y)
        + _halo_scratch(nf, nz, x, y)
        + [pltpu.VMEM((5 * NCOEF, x, y), F32)],
    )(s, *s_halo, a, *a_halo, coef, *c_halo)
    return res if with_edges else res[0]


def _shift(v, axis, step):
    n = lax.axis_size(axis)
    if step > 0:
        pairs = [(i, i + 1) for i in range(n - 1)]
    else:
        pairs = [(i + 1, i) for i in range(n - 1)]
    return lax.ppermute(v, axis, pairs)


def exchange(xf, xl, yf, yl):
    return (
        _shift(xl, "gx", 1),
        _shift(xf, "gx", -1),
        _shift(yl, "gy", 1),
        _shift(yf, "gy", -1),
    )


def forward_call(holder, held, per):
    n, planes, x, y = held.shape

    def kernel(hold_ref, h_ref, o_ref):
        _, lane = _iotas((x, y))
        for g in range(n):
            h = hold_ref[g]
            for i in range(planes):
                o_ref[g, i] = h_ref[h, i]
            cols = jnp.zeros((x, y), F32)
            scl = jnp.zeros((x, y), F32)
            if g > 0:
                hl = hold_ref[g - 1]
                for i in range(per):
                    v = h_ref[hl, i].astype(F32)
                    cols = jnp.where(lane == i, _roll(v, i - (y - 1), 1), cols)
                scl = jnp.where(lane < per, h_ref[hl, per + 1].astype(F32), scl)
            if g < n - 1:
                hr = hold_ref[g + 1]
                for i in range(per):
                    v = h_ref[hr, i].astype(F32)
                    cols = jnp.where(lane == per + i, _roll(v, per + i, 1), cols)
                sv = _roll(h_ref[hr, per + 1].astype(F32), per, 1)
                scl = jnp.where((lane >= per) & (lane < 2 * per), sv, scl)
            o_ref[g, planes] = cols.astype(o_ref.dtype)
            o_ref[g, planes + 1] = scl.astype(o_ref.dtype)

    return pl.pallas_call(
        kernel,
        out_shape=jax.ShapeDtypeStruct((n, planes + 2, x, y), held.dtype),
        in_specs=[pl.BlockSpec(memory_space=SMEM), pl.BlockSpec(memory_space=VMEM)],
    )(holder, held)


def route_blocks(stored_slab, block_scales, holder, xm_all, xp_all, first):
    nf, nz, x, y = stored_slab.shape
    n = lax.axis_size("gy")
    nplanes = nf * nz
    per = nplanes // n
    bf = stored_slab.dtype
    slab = stored_slab.reshape(n, per, x, y)
    rows_m = xm_all[first : first + nplanes].astype(bf).reshape(n, per, y)
    rows_p = xp_all[first : first + nplanes].astype(bf).reshape(n, per, y)
    halo = jnp.concatenate([rows_m, rows_p], axis=1)[:, None]
    sc_m = xm_all[first + nplanes, :nplanes].astype(bf).reshape(n, 1, per)
    sc_p = xp_all[first + nplanes, :nplanes].astype(bf).reshape(n, 1, per)
    sc = jnp.concatenate([block_scales.reshape(n, 1, per), sc_m, sc_p], axis=1)
    sc = jnp.pad(sc, ((0, 0), (0, x - 3), (0, y - per)))[:, None]
    held = lax.all_to_all(jnp.concatenate([slab, halo, sc], axis=1), "gy", 0, 0, tiled=True)

    forward = forward_call(holder, held, per)
    return lax.all_to_all(forward, "gy", 0, 0, tiled=True)


def on_device(stored_slab, block_scales, holder, soil_class, soil_table, cotangent):
    nf, nz, x, y = stored_slab.shape
    nplanes = nf * nz

    coef, cxf, cxl, cyf, cyl = prep_call(
        soil_class, soil_table, cotangent, stored_slab, block_scales.reshape(-1).astype(F32)
    )
    c_halo = exchange(cxf, cxl, cyf, cyl)
    c_first = nplanes

    pieces = route_blocks(stored_slab, block_scales, holder, c_halo[0], c_halo[1], nplanes + NCOEF)
    per = nplanes // pieces.shape[0]
    scales = jnp.concatenate(
        [
            pieces[:, per + 1, 0:3, :per].transpose(1, 0, 2).reshape(3, nplanes),
            pieces[:, per + 3, 0, : 2 * per].reshape(-1, 2, per).transpose(1, 0, 2).reshape(2, nplanes),
        ]
    ).astype(F32).reshape(-1)
    res = state0_step_call(pieces, scales, nf, per, coef, c_halo, c_first)
    s0, s0_halo, s1, s1_edges = res[0], res[1:5], res[5], res[6:10]
    s1_halo = exchange(*s1_edges)

    a1, *a1_edges = adjoint_call(
        s1, s1_halo, cotangent, c_halo, 0, coef, c_halo, c_first, True
    )
    a1_halo = exchange(*a1_edges)
    s2 = step_call(s1, s1_halo, coef, c_halo, c_first, False)

    sens = adjoint_call(s0, s0_halo, a1, a1_halo, 0, coef, c_halo, c_first, False)
    return (s2, sens)


def solution(mesh):
    placed = (
        P(None, None, "gx", "gy"),
        P(None, None, "gx", "gy"),
        P(),
        P("gx", "gy"),
        P(),
        P(None, None, "gx", "gy"),
    )
    return jax.shard_map(
        on_device,
        mesh=mesh,
        in_specs=placed,
        out_specs=(P(None, None, "gx", "gy"), P(None, None, "gx", "gy")),
        check_vma=False,
    )
```

```python
import jax
import jax.numpy as jnp
from jax import lax
from jax.experimental import pallas as pl
from jax.experimental.pallas import tpu as pltpu
from jax.sharding import PartitionSpec as P

F32 = jnp.float32
NCOEF = 4
UNROLL = 32
VMEM = pltpu.MemorySpace.VMEM
SMEM = pltpu.MemorySpace.SMEM


def _roll(v, shift, axis):
    shift = shift % v.shape[axis]
    if shift == 0:
        return v
    return pltpu.roll(v, shift, axis)


def _iotas(shape):
    return lax.broadcasted_iota(jnp.int32, shape, 0), lax.broadcasted_iota(jnp.int32, shape, 1)


def _pack_edges(vals, xf_ref, xl_ref, yf_ref, yl_ref):
    x, y = vals[0].shape
    _, lane = _iotas((x, y))
    xf_ref[...] = jnp.zeros(xf_ref.shape, F32)
    xl_ref[...] = jnp.zeros(xl_ref.shape, F32)
    yf = jnp.zeros((x, y), F32)
    yl = jnp.zeros((x, y), F32)
    for k, v in enumerate(vals):
        xf_ref[k : k + 1, :] = v[0:1, :]
        xl_ref[k : k + 1, :] = v[x - 1 : x, :]
        yf = jnp.where(lane == k, _roll(v, k, 1), yf)
        yl = jnp.where(lane == k, _roll(v, k - (y - 1), 1), yl)
    yf_ref[...] = yf
    yl_ref[...] = yl


def _expand_halo(xm_ref, xp_ref, ym_ref, yp_ref, first, nf, nz, dst):
    hxm, hxp, hym, hyp = dst
    x, y = hxm.shape[2], hxm.shape[3]
    ymv = ym_ref[...]
    ypv = yp_ref[...]
    for f in range(nf):
        for z in range(nz):
            k = first + f * nz + z
            hxm[f, z] = jnp.broadcast_to(xm_ref[k : k + 1, :], (x, y))
            hxp[f, z] = jnp.broadcast_to(xp_ref[k : k + 1, :], (x, y))
            hym[f, z] = _roll(ymv, -k, 1)
            hyp[f, z] = _roll(ypv, (y - 1) - k, 1)


def _coef_table(c_ref, cxm_ref, cxp_ref, cym_ref, cyp_ref, first, cs):
    x, y = c_ref.shape[1], c_ref.shape[2]
    ymv = cym_ref[...]
    ypv = cyp_ref[...]
    masks = _iotas((x, y))
    for k in range(NCOEF):
        r = first + k
        cv = c_ref[k]
        cs[k] = cv
        halo = (
            jnp.broadcast_to(cxm_ref[r : r + 1, :], (x, y)),
            jnp.broadcast_to(cxp_ref[r : r + 1, :], (x, y)),
            _roll(ymv, -r, 1),
            _roll(ypv, (y - 1) - r, 1),
        )
        for d, v in enumerate(_neighbours(cv, 0, [h[None] for h in halo], masks)):
            cs[4 + 4 * d + k] = v


def _neighbours(v, z, h, masks):
    row, lane = masks
    x, y = v.shape
    hxm, hxp, hym, hyp = h
    return (
        jnp.where(row == 0, hxm[z], _roll(v, 1, 0)),
        jnp.where(row == x - 1, hxp[z], _roll(v, x - 1, 0)),
        jnp.where(lane == 0, hym[z], _roll(v, 1, 1)),
        jnp.where(lane == y - 1, hyp[z], _roll(v, y - 1, 1)),
    )


def _field_at(ref, f, z, nz):
    zm = jnp.maximum(z - 1, 0)
    zp = jnp.minimum(z + 1, nz - 1)
    vm = jnp.where(z > 0, 1.0, 0.0).astype(F32)
    vp = jnp.where(z < nz - 1, 1.0, 0.0).astype(F32)
    return ref[f, z], ref[f, zm] * vm, ref[f, zp] * vp, vm, vp


def _gains(b):
    return 1.5 + b, 1.5 + 0.5 * b


def _step_body(s_ref, sh, cs, o_ref, nz, masks):
    def body(z, carry):
        u, u_m, u_p, vm, vp = _field_at(s_ref, 0, z, nz)
        t, t_m, t_p, _, _ = _field_at(s_ref, 1, z, nz)
        c = [cs[k] for k in range(NCOEF)]
        g1, g2 = _gains(jnp.tanh(u))
        kw, dtv, lamb, kv = c[0] * g1, c[1] * g2, c[2] * g2, c[3] * g1
        a1 = jnp.zeros_like(u)
        a2 = jnp.zeros_like(u)
        for un, tn, valid in ((u_m, t_m, vm), (u_p, t_p, vp)):
            g1n, g2n = _gains(jnp.tanh(un))
            a1 = a1 + (g1 + valid * g1n) * (un - u)
            a2 = a2 + (g2 + valid * g2n) * (tn - t)
        f0 = c[0] * a1 + c[1] * a2
        f1 = c[2] * a2 + c[3] * a1
        uns = _neighbours(u, z, sh[0], masks)
        tns = _neighbours(t, z, sh[1], masks)
        for d in range(4):
            un, tn = uns[d], tns[d]
            g1n, g2n = _gains(jnp.tanh(un))
            cn = [cs[4 + 4 * d + k] for k in range(NCOEF)]
            du = un - u
            dt = tn - t
            f0 = f0 + (kw + cn[0] * g1n) * du + (dtv + cn[1] * g2n) * dt
            f1 = f1 + (lamb + cn[2] * g2n) * dt + (kv + cn[3] * g1n) * du
        o_ref[0, z] = u + 0.5 * f0
        o_ref[1, z] = t + 0.5 * f1
        return carry

    lax.fori_loop(0, nz, body, 0, unroll=UNROLL)


def _adjoint_body(s_ref, sh, a_ref, ah, cs, o_ref, nz, masks):
    def body(z, carry):
        u, u_m, u_p, vm, vp = _field_at(s_ref, 0, z, nz)
        t, t_m, t_p, _, _ = _field_at(s_ref, 1, z, nz)
        a0, a0_m, a0_p, _, _ = _field_at(a_ref, 0, z, nz)
        a1, a1_m, a1_p, _, _ = _field_at(a_ref, 1, z, nz)
        c = [cs[k] for k in range(NCOEF)]
        b = jnp.tanh(u)
        g1, g2 = _gains(b)
        kw, dtv, lamb, kv = c[0] * g1, c[1] * g2, c[2] * g2, c[3] * g1
        zero = jnp.zeros_like(u)
        p10, p11, p20, p21 = zero, zero, zero, zero
        gu0, gu1, gt0, gt1 = zero, zero, zero, zero
        for un, tn, a0n, a1n, valid in ((u_m, t_m, a0_m, a1_m, vm), (u_p, t_p, a0_p, a1_p, vp)):
            g1n, g2n = _gains(jnp.tanh(un))
            s1 = g1 + valid * g1n
            s2 = g2 + valid * g2n
            du, dt, da0, da1 = un - u, tn - t, a0n - a0, a1n - a1
            p10 = p10 + s1 * da0
            p11 = p11 + s1 * da1
            p20 = p20 + s2 * da0
            p21 = p21 + s2 * da1
            gu0 = gu0 + du * da0
            gu1 = gu1 + du * da1
            gt0 = gt0 + dt * da0
            gt1 = gt1 + dt * da1
        ju = c[0] * p10 + c[3] * p11
        jt = c[1] * p20 + c[2] * p21
        uns = _neighbours(u, z, sh[0], masks)
        tns = _neighbours(t, z, sh[1], masks)
        a0ns = _neighbours(a0, z, ah[0], masks)
        a1ns = _neighbours(a1, z, ah[1], masks)
        for d in range(4):
            un, tn, a0n, a1n = uns[d], tns[d], a0ns[d], a1ns[d]
            g1n, g2n = _gains(jnp.tanh(un))
            cn = [cs[4 + 4 * d + k] for k in range(NCOEF)]
            du, dt, da0, da1 = un - u, tn - t, a0n - a0, a1n - a1
            ju = ju + (kw + cn[0] * g1n) * da0 + (kv + cn[3] * g1n) * da1
            jt = jt + (dtv + cn[1] * g2n) * da0 + (lamb + cn[2] * g2n) * da1
            gu0 = gu0 + du * da0
            gu1 = gu1 + du * da1
            gt0 = gt0 + dt * da0
            gt1 = gt1 + dt * da1
        gsum = c[0] * gu0 + c[3] * gu1 + 0.5 * (c[1] * gt0 + c[2] * gt1)
        o_ref[0, z] = a0 + 0.5 * ju - 0.5 * (1.0 - b * b) * gsum
        o_ref[1, z] = a1 + 0.5 * jt
        return carry

    lax.fori_loop(0, nz, body, 0, unroll=UNROLL)


def _halo_scratch(nf, nz, x, y):
    return [pltpu.VMEM((nf, nz, x, y), F32) for _ in range(4)]


def _edge_shapes(rows, x, y):
    return (
        jax.ShapeDtypeStruct((rows, y), F32),
        jax.ShapeDtypeStruct((rows, y), F32),
        jax.ShapeDtypeStruct((x, y), F32),
        jax.ShapeDtypeStruct((x, y), F32),
    )


def _rows(n):
    return -(-n // 8) * 8


def prep_call(soil_class, soil_table, cot, slab, scales):
    nf, nz, x, y = cot.shape
    nclass = soil_table.shape[0]
    table = soil_table.T
    nplanes = nf * nz

    def kernel(cls_ref, tab_ref, sc_ref, cot_ref, slab_ref, coef_ref, xf_ref, xl_ref, yf_ref, yl_ref):
        cls = cls_ref[...]
        coefs = []
        for k in range(NCOEF):
            cv = jnp.zeros(cls.shape, F32)
            for j in range(nclass):
                cv = jnp.where(cls == j, tab_ref[k, j], cv)
            coef_ref[k] = cv
            coefs.append(cv)
        vals = [cot_ref[f, z] for f in range(nf) for z in range(nz)] + coefs
        _pack_edges(vals, xf_ref, xl_ref, yf_ref, yl_ref)
        base = len(vals)
        for k in range(nplanes):
            v = slab_ref[k // nz, k % nz].astype(F32)
            xf_ref[base + k : base + k + 1, :] = v[0:1, :]
            xl_ref[base + k : base + k + 1, :] = v[x - 1 : x, :]
        _, lane = _iotas((1, y))
        row = jnp.zeros((1, y), F32)
        for k in range(nplanes):
            row = jnp.where(lane == k, sc_ref[k], row)
        xf_ref[base + nplanes : base + nplanes + 1, :] = row
        xl_ref[base + nplanes : base + nplanes + 1, :] = row

    rows = _rows(2 * nplanes + NCOEF + 1)
    return pl.pallas_call(
        kernel,
        out_shape=(jax.ShapeDtypeStruct((NCOEF, x, y), F32),)
        + _edge_shapes(rows, x, y)[:2]
        + _edge_shapes(8, x, y)[2:],
        in_specs=[
            pl.BlockSpec(memory_space=VMEM),
            pl.BlockSpec(memory_space=SMEM),
            pl.BlockSpec(memory_space=SMEM),
            pl.BlockSpec(memory_space=VMEM),
            pl.BlockSpec(memory_space=VMEM),
        ],
    )(soil_class, table, scales, cot, slab)


def _state0_body(sc_ref, r_ref, s_ref, xm_ref, xp_ref, ym_ref, yp_ref, per):
    nz, x, y = s_ref.shape[1], s_ref.shape[2], s_ref.shape[3]
    nplanes = s_ref.shape[0] * nz
    _, lane = _iotas((x, y))
    ym = jnp.zeros((x, y), F32)
    yp = jnp.zeros((x, y), F32)
    for k in range(nplanes):
        p, i = k // per, k % per
        s_ref[k // nz, k % nz] = r_ref[p, i].astype(F32) * sc_ref[k]
        hx = r_ref[p, per].astype(F32)
        xm_ref[k : k + 1, :] = hx[i : i + 1, :] * sc_ref[nplanes + k]
        xp_ref[k : k + 1, :] = hx[per + i : per + i + 1, :] * sc_ref[2 * nplanes + k]
        hy = r_ref[p, per + 2].astype(F32)
        ym = jnp.where(lane == k, _roll(hy, k - i, 1) * sc_ref[3 * nplanes + k], ym)
        yp = jnp.where(lane == k, _roll(hy, k - (per + i), 1) * sc_ref[4 * nplanes + k], yp)
    ym_ref[...] = ym
    yp_ref[...] = yp


def state0_step_call(pieces, scales, nf, per, coef, c_halo, c_first):
    npiece, _, x, y = pieces.shape
    nplanes = npiece * per
    nz = nplanes // nf

    def kernel(sc_ref, r_ref, c_ref, cxm, cxp, cym, cyp, *refs):
        s0_ref, xm_ref, xp_ref, ym_ref, yp_ref = refs[:5]
        s1_ref, xf_ref, xl_ref, yf_ref, yl_ref = refs[5:10]
        scratch = refs[10:]
        sh_all = scratch[0:4]
        cs = scratch[4]
        _state0_body(sc_ref, r_ref, s0_ref, xm_ref, xp_ref, ym_ref, yp_ref, per)
        _expand_halo(xm_ref, xp_ref, ym_ref, yp_ref, 0, nf, nz, sh_all)
        _coef_table(c_ref, cxm, cxp, cym, cyp, c_first, cs)
        masks = _iotas((x, y))
        sh = [tuple(h.at[f] for h in sh_all) for f in range(nf)]
        _step_body(s0_ref, sh, cs, s1_ref, nz, masks)
        vals = [s1_ref[f, z] for f in range(nf) for z in range(nz)]
        _pack_edges(vals, xf_ref, xl_ref, yf_ref, yl_ref)

    state = jax.ShapeDtypeStruct((nf, nz, x, y), F32)
    return pl.pallas_call(
        kernel,
        out_shape=(state,) + _edge_shapes(nplanes, x, y) + (state,) + _edge_shapes(_rows(nplanes), x, y),
        in_specs=[pl.BlockSpec(memory_space=SMEM)] + [pl.BlockSpec(memory_space=VMEM)] * 6,
        scratch_shapes=_halo_scratch(nf, nz, x, y) + [pltpu.VMEM((5 * NCOEF, x, y), F32)],
    )(scales, pieces, coef, *c_halo)


def step_call(s, s_halo, coef, c_halo, c_first, with_edges):
    nf, nz, x, y = s.shape

    def kernel(*refs):
        s_ref, sxm, sxp, sym, syp, c_ref, cxm, cxp, cym, cyp = refs[:10]
        rest = refs[10:]
        if with_edges:
            o_ref, xf_ref, xl_ref, yf_ref, yl_ref = rest[:5]
            scratch = rest[5:]
        else:
            o_ref = rest[0]
            scratch = rest[1:]
        sh_all = scratch[0:4]
        cs = scratch[4]
        _expand_halo(sxm, sxp, sym, syp, 0, nf, nz, sh_all)
        _coef_table(c_ref, cxm, cxp, cym, cyp, c_first, cs)
        masks = _iotas((x, y))
        sh = [tuple(h.at[f] for h in sh_all) for f in range(nf)]
        _step_body(s_ref, sh, cs, o_ref, nz, masks)
        if with_edges:
            vals = [o_ref[f, z] for f in range(nf) for z in range(nz)]
            _pack_edges(vals, xf_ref, xl_ref, yf_ref, yl_ref)

    out_shape = (jax.ShapeDtypeStruct(s.shape, F32),)
    if with_edges:
        out_shape = out_shape + _edge_shapes(_rows(nf * nz), x, y)
    res = pl.pallas_call(
        kernel,
        out_shape=out_shape,
        scratch_shapes=_halo_scratch(nf, nz, x, y) + [pltpu.VMEM((5 * NCOEF, x, y), F32)],
    )(s, *s_halo, coef, *c_halo)
    return res if with_edges else res[0]


def adjoint_call(s, s_halo, a, a_halo, a_first, coef, c_halo, c_first, with_edges):
    nf, nz, x, y = s.shape

    def kernel(*refs):
        s_ref, sxm, sxp, sym, syp, a_ref, axm, axp, aym, ayp, c_ref, cxm, cxp, cym, cyp = refs[:15]
        rest = refs[15:]
        if with_edges:
            o_ref, xf_ref, xl_ref, yf_ref, yl_ref = rest[:5]
            scratch = rest[5:]
        else:
            o_ref = rest[0]
            scratch = rest[1:]
        sh_all = scratch[0:4]
        ah_all = scratch[4:8]
        cs = scratch[8]
        _expand_halo(sxm, sxp, sym, syp, 0, nf, nz, sh_all)
        _expand_halo(axm, axp, aym, ayp, a_first, nf, nz, ah_all)
        _coef_table(c_ref, cxm, cxp, cym, cyp, c_first, cs)
        masks = _iotas((x, y))
        sh = [tuple(h.at[f] for h in sh_all) for f in range(nf)]
        ah = [tuple(h.at[f] for h in ah_all) for f in range(nf)]
        _adjoint_body(s_ref, sh, a_ref, ah, cs, o_ref, nz, masks)
        if with_edges:
            vals = [o_ref[f, z] for f in range(nf) for z in range(nz)]
            _pack_edges(vals, xf_ref, xl_ref, yf_ref, yl_ref)

    out_shape = (jax.ShapeDtypeStruct(s.shape, F32),)
    if with_edges:
        out_shape = out_shape + _edge_shapes(_rows(nf * nz), x, y)
    res = pl.pallas_call(
        kernel,
        out_shape=out_shape,
        scratch_shapes=_halo_scratch(nf, nz, x, y)
        + _halo_scratch(nf, nz, x, y)
        + [pltpu.VMEM((5 * NCOEF, x, y), F32)],
    )(s, *s_halo, a, *a_halo, coef, *c_halo)
    return res if with_edges else res[0]


def _shift(v, axis, step):
    n = lax.axis_size(axis)
    if step > 0:
        pairs = [(i, i + 1) for i in range(n - 1)]
    else:
        pairs = [(i + 1, i) for i in range(n - 1)]
    return lax.ppermute(v, axis, pairs)


def exchange(xf, xl, yf, yl):
    return (
        _shift(xl, "gx", 1),
        _shift(xf, "gx", -1),
        _shift(yl, "gy", 1),
        _shift(yf, "gy", -1),
    )


def forward_call(holder, held, per):
    n, planes, x, y = held.shape

    def kernel(hold_ref, h_ref, o_ref):
        _, lane = _iotas((x, y))
        for g in range(n):
            h = hold_ref[g]
            for i in range(planes):
                o_ref[g, i] = h_ref[h, i]
            cols = jnp.zeros((x, y), F32)
            scl = jnp.zeros((x, y), F32)
            if g > 0:
                hl = hold_ref[g - 1]
                for i in range(per):
                    v = h_ref[hl, i].astype(F32)
                    cols = jnp.where(lane == i, _roll(v, i - (y - 1), 1), cols)
                scl = jnp.where(lane < per, h_ref[hl, per + 1].astype(F32), scl)
            if g < n - 1:
                hr = hold_ref[g + 1]
                for i in range(per):
                    v = h_ref[hr, i].astype(F32)
                    cols = jnp.where(lane == per + i, _roll(v, per + i, 1), cols)
                sv = _roll(h_ref[hr, per + 1].astype(F32), per, 1)
                scl = jnp.where((lane >= per) & (lane < 2 * per), sv, scl)
            o_ref[g, planes] = cols.astype(o_ref.dtype)
            o_ref[g, planes + 1] = scl.astype(o_ref.dtype)

    return pl.pallas_call(
        kernel,
        out_shape=jax.ShapeDtypeStruct((n, planes + 2, x, y), held.dtype),
        in_specs=[pl.BlockSpec(memory_space=SMEM), pl.BlockSpec(memory_space=VMEM)],
    )(holder, held)


def route_blocks(stored_slab, block_scales, holder, xm_all, xp_all, first):
    nf, nz, x, y = stored_slab.shape
    n = lax.axis_size("gy")
    nplanes = nf * nz
    per = nplanes // n
    bf = stored_slab.dtype
    slab = stored_slab.reshape(n, per, x, y)
    rows_m = xm_all[first : first + nplanes].astype(bf).reshape(n, per, y)
    rows_p = xp_all[first : first + nplanes].astype(bf).reshape(n, per, y)
    halo = jnp.concatenate([rows_m, rows_p], axis=1)[:, None]
    sc_m = xm_all[first + nplanes, :nplanes].astype(bf).reshape(n, 1, per)
    sc_p = xp_all[first + nplanes, :nplanes].astype(bf).reshape(n, 1, per)
    sc = jnp.concatenate([block_scales.reshape(n, 1, per), sc_m, sc_p], axis=1)
    sc = jnp.pad(sc, ((0, 0), (0, x - 3), (0, y - per)))[:, None]
    held = lax.all_to_all(jnp.concatenate([slab, halo, sc], axis=1), "gy", 0, 0, tiled=True)

    forward = forward_call(holder, held, per)
    return lax.all_to_all(forward, "gy", 0, 0, tiled=True)


def on_device(stored_slab, block_scales, holder, soil_class, soil_table, cotangent):
    nf, nz, x, y = stored_slab.shape
    nplanes = nf * nz

    coef, cxf, cxl, cyf, cyl = prep_call(
        soil_class, soil_table, cotangent, stored_slab, block_scales.reshape(-1).astype(F32)
    )
    c_halo = exchange(cxf, cxl, cyf, cyl)
    c_first = nplanes

    pieces = route_blocks(stored_slab, block_scales, holder, c_halo[0], c_halo[1], nplanes + NCOEF)
    per = nplanes // pieces.shape[0]
    scales = jnp.concatenate(
        [
            pieces[:, per + 1, 0:3, :per].transpose(1, 0, 2).reshape(3, nplanes),
            pieces[:, per + 3, 0, : 2 * per].reshape(-1, 2, per).transpose(1, 0, 2).reshape(2, nplanes),
        ]
    ).astype(F32).reshape(-1)
    res = state0_step_call(pieces, scales, nf, per, coef, c_halo, c_first)
    s0, s0_halo, s1, s1_edges = res[0], res[1:5], res[5], res[6:10]
    s1_halo = exchange(*s1_edges)

    a1, *a1_edges = adjoint_call(
        s1, s1_halo, cotangent, c_halo, 0, coef, c_halo, c_first, True
    )
    a1_halo = exchange(*a1_edges)
    s2 = step_call(s1, s1_halo, coef, c_halo, c_first, False)

    sens = adjoint_call(s0, s0_halo, a1, a1_halo, 0, coef, c_halo, c_first, False)
    return (s2, sens)


def solution(mesh):
    placed = (
        P(None, None, "gx", "gy"),
        P(None, None, "gx", "gy"),
        P(),
        P("gx", "gy"),
        P(),
        P(None, None, "gx", "gy"),
    )
    return jax.shard_map(
        on_device,
        mesh=mesh,
        in_specs=placed,
        out_specs=(P(None, None, "gx", "gy"), P(None, None, "gx", "gy")),
        check_vma=False,
    )
```

```python
import jax
import jax.numpy as jnp
from jax import lax
from jax.experimental import pallas as pl
from jax.experimental.pallas import tpu as pltpu
from jax.sharding import PartitionSpec as P

F32 = jnp.float32
NCOEF = 4
UNROLL = 32
VMEM = pltpu.MemorySpace.VMEM
SMEM = pltpu.MemorySpace.SMEM


def _roll(v, shift, axis):
    shift = shift % v.shape[axis]
    if shift == 0:
        return v
    return pltpu.roll(v, shift, axis)


def _iotas(shape):
    return lax.broadcasted_iota(jnp.int32, shape, 0), lax.broadcasted_iota(jnp.int32, shape, 1)


def _pack_edges(vals, xf_ref, xl_ref, yf_ref, yl_ref):
    x, y = vals[0].shape
    _, lane = _iotas((x, y))
    xf_ref[...] = jnp.zeros(xf_ref.shape, F32)
    xl_ref[...] = jnp.zeros(xl_ref.shape, F32)
    yf = jnp.zeros((x, y), F32)
    yl = jnp.zeros((x, y), F32)
    for k, v in enumerate(vals):
        xf_ref[k : k + 1, :] = v[0:1, :]
        xl_ref[k : k + 1, :] = v[x - 1 : x, :]
        yf = jnp.where(lane == k, _roll(v, k, 1), yf)
        yl = jnp.where(lane == k, _roll(v, k - (y - 1), 1), yl)
    yf_ref[...] = yf
    yl_ref[...] = yl


def _expand_halo(xm_ref, xp_ref, ym_ref, yp_ref, first, nf, nz, dst):
    hxm, hxp, hym, hyp = dst
    x, y = hxm.shape[2], hxm.shape[3]
    ymv = ym_ref[...]
    ypv = yp_ref[...]
    for f in range(nf):
        for z in range(nz):
            k = first + f * nz + z
            hxm[f, z] = jnp.broadcast_to(xm_ref[k : k + 1, :], (x, y))
            hxp[f, z] = jnp.broadcast_to(xp_ref[k : k + 1, :], (x, y))
            hym[f, z] = _roll(ymv, -k, 1)
            hyp[f, z] = _roll(ypv, (y - 1) - k, 1)


def _coef_table(c_ref, cxm_ref, cxp_ref, cym_ref, cyp_ref, first, cs):
    x, y = c_ref.shape[1], c_ref.shape[2]
    ymv = cym_ref[...]
    ypv = cyp_ref[...]
    masks = _iotas((x, y))
    for k in range(NCOEF):
        r = first + k
        cv = c_ref[k]
        cs[k] = cv
        halo = (
            jnp.broadcast_to(cxm_ref[r : r + 1, :], (x, y)),
            jnp.broadcast_to(cxp_ref[r : r + 1, :], (x, y)),
            _roll(ymv, -r, 1),
            _roll(ypv, (y - 1) - r, 1),
        )
        for d, v in enumerate(_neighbours(cv, 0, [h[None] for h in halo], masks)):
            cs[4 + 4 * d + k] = v


def _neighbours(v, z, h, masks):
    row, lane = masks
    x, y = v.shape
    hxm, hxp, hym, hyp = h
    return (
        jnp.where(row == 0, hxm[z], _roll(v, 1, 0)),
        jnp.where(row == x - 1, hxp[z], _roll(v, x - 1, 0)),
        jnp.where(lane == 0, hym[z], _roll(v, 1, 1)),
        jnp.where(lane == y - 1, hyp[z], _roll(v, y - 1, 1)),
    )


def _field_at(ref, f, z, nz):
    zm = jnp.maximum(z - 1, 0)
    zp = jnp.minimum(z + 1, nz - 1)
    vm = jnp.where(z > 0, 1.0, 0.0).astype(F32)
    vp = jnp.where(z < nz - 1, 1.0, 0.0).astype(F32)
    return ref[f, z], ref[f, zm] * vm, ref[f, zp] * vp, vm, vp


def _gains(b):
    return 1.5 + b, 1.5 + 0.5 * b


def _step_body(s_ref, sh, cs, o_ref, nz, masks):
    def body(z, carry):
        u, u_m, u_p, vm, vp = _field_at(s_ref, 0, z, nz)
        t, t_m, t_p, _, _ = _field_at(s_ref, 1, z, nz)
        c = [cs[k] for k in range(NCOEF)]
        g1, g2 = _gains(jnp.tanh(u))
        kw, dtv, lamb, kv = c[0] * g1, c[1] * g2, c[2] * g2, c[3] * g1
        a1 = jnp.zeros_like(u)
        a2 = jnp.zeros_like(u)
        for un, tn, valid in ((u_m, t_m, vm), (u_p, t_p, vp)):
            g1n, g2n = _gains(jnp.tanh(un))
            a1 = a1 + (g1 + valid * g1n) * (un - u)
            a2 = a2 + (g2 + valid * g2n) * (tn - t)
        f0 = c[0] * a1 + c[1] * a2
        f1 = c[2] * a2 + c[3] * a1
        uns = _neighbours(u, z, sh[0], masks)
        tns = _neighbours(t, z, sh[1], masks)
        for d in range(4):
            un, tn = uns[d], tns[d]
            g1n, g2n = _gains(jnp.tanh(un))
            cn = [cs[4 + 4 * d + k] for k in range(NCOEF)]
            du = un - u
            dt = tn - t
            f0 = f0 + (kw + cn[0] * g1n) * du + (dtv + cn[1] * g2n) * dt
            f1 = f1 + (lamb + cn[2] * g2n) * dt + (kv + cn[3] * g1n) * du
        o_ref[0, z] = u + 0.5 * f0
        o_ref[1, z] = t + 0.5 * f1
        return carry

    lax.fori_loop(0, nz, body, 0, unroll=UNROLL)


def _adjoint_body(s_ref, sh, a_ref, ah, cs, o_ref, nz, masks):
    def body(z, carry):
        u, u_m, u_p, vm, vp = _field_at(s_ref, 0, z, nz)
        t, t_m, t_p, _, _ = _field_at(s_ref, 1, z, nz)
        a0, a0_m, a0_p, _, _ = _field_at(a_ref, 0, z, nz)
        a1, a1_m, a1_p, _, _ = _field_at(a_ref, 1, z, nz)
        c = [cs[k] for k in range(NCOEF)]
        b = jnp.tanh(u)
        g1, g2 = _gains(b)
        kw, dtv, lamb, kv = c[0] * g1, c[1] * g2, c[2] * g2, c[3] * g1
        zero = jnp.zeros_like(u)
        p10, p11, p20, p21 = zero, zero, zero, zero
        gu0, gu1, gt0, gt1 = zero, zero, zero, zero
        for un, tn, a0n, a1n, valid in ((u_m, t_m, a0_m, a1_m, vm), (u_p, t_p, a0_p, a1_p, vp)):
            g1n, g2n = _gains(jnp.tanh(un))
            s1 = g1 + valid * g1n
            s2 = g2 + valid * g2n
            du, dt, da0, da1 = un - u, tn - t, a0n - a0, a1n - a1
            p10 = p10 + s1 * da0
            p11 = p11 + s1 * da1
            p20 = p20 + s2 * da0
            p21 = p21 + s2 * da1
            gu0 = gu0 + du * da0
            gu1 = gu1 + du * da1
            gt0 = gt0 + dt * da0
            gt1 = gt1 + dt * da1
        ju = c[0] * p10 + c[3] * p11
        jt = c[1] * p20 + c[2] * p21
        uns = _neighbours(u, z, sh[0], masks)
        tns = _neighbours(t, z, sh[1], masks)
        a0ns = _neighbours(a0, z, ah[0], masks)
        a1ns = _neighbours(a1, z, ah[1], masks)
        for d in range(4):
            un, tn, a0n, a1n = uns[d], tns[d], a0ns[d], a1ns[d]
            g1n, g2n = _gains(jnp.tanh(un))
            cn = [cs[4 + 4 * d + k] for k in range(NCOEF)]
            du, dt, da0, da1 = un - u, tn - t, a0n - a0, a1n - a1
            ju = ju + (kw + cn[0] * g1n) * da0 + (kv + cn[3] * g1n) * da1
            jt = jt + (dtv + cn[1] * g2n) * da0 + (lamb + cn[2] * g2n) * da1
            gu0 = gu0 + du * da0
            gu1 = gu1 + du * da1
            gt0 = gt0 + dt * da0
            gt1 = gt1 + dt * da1
        gsum = c[0] * gu0 + c[3] * gu1 + 0.5 * (c[1] * gt0 + c[2] * gt1)
        o_ref[0, z] = a0 + 0.5 * ju - 0.5 * (1.0 - b * b) * gsum
        o_ref[1, z] = a1 + 0.5 * jt
        return carry

    lax.fori_loop(0, nz, body, 0, unroll=UNROLL)


def _halo_scratch(nf, nz, x, y):
    return [pltpu.VMEM((nf, nz, x, y), F32) for _ in range(4)]


def _edge_shapes(rows, x, y):
    return (
        jax.ShapeDtypeStruct((rows, y), F32),
        jax.ShapeDtypeStruct((rows, y), F32),
        jax.ShapeDtypeStruct((x, y), F32),
        jax.ShapeDtypeStruct((x, y), F32),
    )


def _rows(n):
    return -(-n // 8) * 8


def prep_call(soil_class, soil_table, cot, slab, scales):
    nf, nz, x, y = cot.shape
    nclass = soil_table.shape[0]
    table = soil_table.T
    nplanes = nf * nz

    def kernel(cls_ref, tab_ref, sc_ref, cot_ref, slab_ref, coef_ref, xf_ref, xl_ref, yf_ref, yl_ref):
        cls = cls_ref[...]
        coefs = []
        for k in range(NCOEF):
            cv = jnp.zeros(cls.shape, F32)
            for j in range(nclass):
                cv = jnp.where(cls == j, tab_ref[k, j], cv)
            coef_ref[k] = cv
            coefs.append(cv)
        vals = [cot_ref[f, z] for f in range(nf) for z in range(nz)] + coefs
        _pack_edges(vals, xf_ref, xl_ref, yf_ref, yl_ref)
        base = len(vals)
        for k in range(nplanes):
            v = slab_ref[k // nz, k % nz].astype(F32)
            xf_ref[base + k : base + k + 1, :] = v[0:1, :]
            xl_ref[base + k : base + k + 1, :] = v[x - 1 : x, :]
        _, lane = _iotas((1, y))
        row = jnp.zeros((1, y), F32)
        scv = sc_ref[...].astype(F32)
        for k in range(nplanes):
            v = jnp.broadcast_to(scv[k // nz : k // nz + 1, k % nz : k % nz + 1], (1, y))
            row = jnp.where(lane == k, v, row)
        xf_ref[base + nplanes : base + nplanes + 1, :] = row
        xl_ref[base + nplanes : base + nplanes + 1, :] = row

    rows = _rows(2 * nplanes + NCOEF + 1)
    return pl.pallas_call(
        kernel,
        out_shape=(jax.ShapeDtypeStruct((NCOEF, x, y), F32),)
        + _edge_shapes(rows, x, y)[:2]
        + _edge_shapes(8, x, y)[2:],
        in_specs=[
            pl.BlockSpec(memory_space=VMEM),
            pl.BlockSpec(memory_space=SMEM),
            pl.BlockSpec(memory_space=VMEM),
            pl.BlockSpec(memory_space=VMEM),
            pl.BlockSpec(memory_space=VMEM),
        ],
    )(soil_class, table, scales, cot, slab)


def _state0_body(sc_ref, r_ref, s_ref, xm_ref, xp_ref, ym_ref, yp_ref, per):
    nz, x, y = s_ref.shape[1], s_ref.shape[2], s_ref.shape[3]
    nplanes = s_ref.shape[0] * nz
    _, lane = _iotas((x, y))
    ym = jnp.zeros((x, y), F32)
    yp = jnp.zeros((x, y), F32)
    for k in range(nplanes):
        p, i = k // per, k % per
        s_ref[k // nz, k % nz] = r_ref[p, i].astype(F32) * sc_ref[k]
        hx = r_ref[p, per].astype(F32)
        xm_ref[k : k + 1, :] = hx[i : i + 1, :] * sc_ref[nplanes + k]
        xp_ref[k : k + 1, :] = hx[per + i : per + i + 1, :] * sc_ref[2 * nplanes + k]
        hy = r_ref[p, per + 2].astype(F32)
        ym = jnp.where(lane == k, _roll(hy, k - i, 1) * sc_ref[3 * nplanes + k], ym)
        yp = jnp.where(lane == k, _roll(hy, k - (per + i), 1) * sc_ref[4 * nplanes + k], yp)
    ym_ref[...] = ym
    yp_ref[...] = yp


def state0_step_call(pieces, scales, nf, per, coef, c_halo, c_first):
    npiece, _, x, y = pieces.shape
    nplanes = npiece * per
    nz = nplanes // nf

    def kernel(sc_ref, r_ref, c_ref, cxm, cxp, cym, cyp, *refs):
        s0_ref, xm_ref, xp_ref, ym_ref, yp_ref = refs[:5]
        s1_ref, xf_ref, xl_ref, yf_ref, yl_ref = refs[5:10]
        scratch = refs[10:]
        sh_all = scratch[0:4]
        cs = scratch[4]
        _state0_body(sc_ref, r_ref, s0_ref, xm_ref, xp_ref, ym_ref, yp_ref, per)
        _expand_halo(xm_ref, xp_ref, ym_ref, yp_ref, 0, nf, nz, sh_all)
        _coef_table(c_ref, cxm, cxp, cym, cyp, c_first, cs)
        masks = _iotas((x, y))
        sh = [tuple(h.at[f] for h in sh_all) for f in range(nf)]
        _step_body(s0_ref, sh, cs, s1_ref, nz, masks)
        vals = [s1_ref[f, z] for f in range(nf) for z in range(nz)]
        _pack_edges(vals, xf_ref, xl_ref, yf_ref, yl_ref)

    state = jax.ShapeDtypeStruct((nf, nz, x, y), F32)
    return pl.pallas_call(
        kernel,
        out_shape=(state,) + _edge_shapes(nplanes, x, y) + (state,) + _edge_shapes(_rows(nplanes), x, y),
        in_specs=[pl.BlockSpec(memory_space=SMEM)] + [pl.BlockSpec(memory_space=VMEM)] * 6,
        scratch_shapes=_halo_scratch(nf, nz, x, y) + [pltpu.VMEM((5 * NCOEF, x, y), F32)],
    )(scales, pieces, coef, *c_halo)


def step_call(s, s_halo, coef, c_halo, c_first, with_edges):
    nf, nz, x, y = s.shape

    def kernel(*refs):
        s_ref, sxm, sxp, sym, syp, c_ref, cxm, cxp, cym, cyp = refs[:10]
        rest = refs[10:]
        if with_edges:
            o_ref, xf_ref, xl_ref, yf_ref, yl_ref = rest[:5]
            scratch = rest[5:]
        else:
            o_ref = rest[0]
            scratch = rest[1:]
        sh_all = scratch[0:4]
        cs = scratch[4]
        _expand_halo(sxm, sxp, sym, syp, 0, nf, nz, sh_all)
        _coef_table(c_ref, cxm, cxp, cym, cyp, c_first, cs)
        masks = _iotas((x, y))
        sh = [tuple(h.at[f] for h in sh_all) for f in range(nf)]
        _step_body(s_ref, sh, cs, o_ref, nz, masks)
        if with_edges:
            vals = [o_ref[f, z] for f in range(nf) for z in range(nz)]
            _pack_edges(vals, xf_ref, xl_ref, yf_ref, yl_ref)

    out_shape = (jax.ShapeDtypeStruct(s.shape, F32),)
    if with_edges:
        out_shape = out_shape + _edge_shapes(_rows(nf * nz), x, y)
    res = pl.pallas_call(
        kernel,
        out_shape=out_shape,
        scratch_shapes=_halo_scratch(nf, nz, x, y) + [pltpu.VMEM((5 * NCOEF, x, y), F32)],
    )(s, *s_halo, coef, *c_halo)
    return res if with_edges else res[0]


def adjoint_call(s, s_halo, a, a_halo, a_first, coef, c_halo, c_first, with_edges):
    nf, nz, x, y = s.shape

    def kernel(*refs):
        s_ref, sxm, sxp, sym, syp, a_ref, axm, axp, aym, ayp, c_ref, cxm, cxp, cym, cyp = refs[:15]
        rest = refs[15:]
        if with_edges:
            o_ref, xf_ref, xl_ref, yf_ref, yl_ref = rest[:5]
            scratch = rest[5:]
        else:
            o_ref = rest[0]
            scratch = rest[1:]
        sh_all = scratch[0:4]
        ah_all = scratch[4:8]
        cs = scratch[8]
        _expand_halo(sxm, sxp, sym, syp, 0, nf, nz, sh_all)
        _expand_halo(axm, axp, aym, ayp, a_first, nf, nz, ah_all)
        _coef_table(c_ref, cxm, cxp, cym, cyp, c_first, cs)
        masks = _iotas((x, y))
        sh = [tuple(h.at[f] for h in sh_all) for f in range(nf)]
        ah = [tuple(h.at[f] for h in ah_all) for f in range(nf)]
        _adjoint_body(s_ref, sh, a_ref, ah, cs, o_ref, nz, masks)
        if with_edges:
            vals = [o_ref[f, z] for f in range(nf) for z in range(nz)]
            _pack_edges(vals, xf_ref, xl_ref, yf_ref, yl_ref)

    out_shape = (jax.ShapeDtypeStruct(s.shape, F32),)
    if with_edges:
        out_shape = out_shape + _edge_shapes(_rows(nf * nz), x, y)
    res = pl.pallas_call(
        kernel,
        out_shape=out_shape,
        scratch_shapes=_halo_scratch(nf, nz, x, y)
        + _halo_scratch(nf, nz, x, y)
        + [pltpu.VMEM((5 * NCOEF, x, y), F32)],
    )(s, *s_halo, a, *a_halo, coef, *c_halo)
    return res if with_edges else res[0]


def _shift(v, axis, step):
    n = lax.axis_size(axis)
    if step > 0:
        pairs = [(i, i + 1) for i in range(n - 1)]
    else:
        pairs = [(i + 1, i) for i in range(n - 1)]
    return lax.ppermute(v, axis, pairs)


def exchange(xf, xl, yf, yl):
    return (
        _shift(xl, "gx", 1),
        _shift(xf, "gx", -1),
        _shift(yl, "gy", 1),
        _shift(yf, "gy", -1),
    )


def forward_call(holder, held, per):
    n, planes, x, y = held.shape

    def kernel(hold_ref, h_ref, o_ref):
        _, lane = _iotas((x, y))
        for g in range(n):
            h = hold_ref[g]
            for i in range(planes):
                o_ref[g, i] = h_ref[h, i]
            cols = jnp.zeros((x, y), F32)
            scl = jnp.zeros((x, y), F32)
            if g > 0:
                hl = hold_ref[g - 1]
                for i in range(per):
                    v = h_ref[hl, i].astype(F32)
                    cols = jnp.where(lane == i, _roll(v, i - (y - 1), 1), cols)
                scl = jnp.where(lane < per, h_ref[hl, per + 1].astype(F32), scl)
            if g < n - 1:
                hr = hold_ref[g + 1]
                for i in range(per):
                    v = h_ref[hr, i].astype(F32)
                    cols = jnp.where(lane == per + i, _roll(v, per + i, 1), cols)
                sv = _roll(h_ref[hr, per + 1].astype(F32), per, 1)
                scl = jnp.where((lane >= per) & (lane < 2 * per), sv, scl)
            o_ref[g, planes] = cols.astype(o_ref.dtype)
            o_ref[g, planes + 1] = scl.astype(o_ref.dtype)

    return pl.pallas_call(
        kernel,
        out_shape=jax.ShapeDtypeStruct((n, planes + 2, x, y), held.dtype),
        in_specs=[pl.BlockSpec(memory_space=SMEM), pl.BlockSpec(memory_space=VMEM)],
    )(holder, held)


def route_blocks(stored_slab, block_scales, holder, xm_all, xp_all, first):
    nf, nz, x, y = stored_slab.shape
    n = lax.axis_size("gy")
    nplanes = nf * nz
    per = nplanes // n
    bf = stored_slab.dtype
    slab = stored_slab.reshape(n, per, x, y)
    rows_m = xm_all[first : first + nplanes].astype(bf).reshape(n, per, y)
    rows_p = xp_all[first : first + nplanes].astype(bf).reshape(n, per, y)
    halo = jnp.concatenate([rows_m, rows_p], axis=1)[:, None]
    sc_m = xm_all[first + nplanes, :nplanes].astype(bf).reshape(n, 1, per)
    sc_p = xp_all[first + nplanes, :nplanes].astype(bf).reshape(n, 1, per)
    sc = jnp.concatenate([block_scales.reshape(n, 1, per), sc_m, sc_p], axis=1)
    sc = jnp.pad(sc, ((0, 0), (0, x - 3), (0, y - per)))[:, None]
    held = lax.all_to_all(jnp.concatenate([slab, halo, sc], axis=1), "gy", 0, 0, tiled=True)

    forward = forward_call(holder, held, per)
    return lax.all_to_all(forward, "gy", 0, 0, tiled=True)


def on_device(stored_slab, block_scales, holder, soil_class, soil_table, cotangent):
    nf, nz, x, y = stored_slab.shape
    nplanes = nf * nz

    coef, cxf, cxl, cyf, cyl = prep_call(
        soil_class, soil_table, cotangent, stored_slab, block_scales.reshape(nf, nz)
    )
    c_halo = exchange(cxf, cxl, cyf, cyl)
    c_first = nplanes

    pieces = route_blocks(stored_slab, block_scales, holder, c_halo[0], c_halo[1], nplanes + NCOEF)
    per = nplanes // pieces.shape[0]
    scales = jnp.concatenate(
        [
            pieces[:, per + 1, 0:3, :per].transpose(1, 0, 2).reshape(3, nplanes),
            pieces[:, per + 3, 0, : 2 * per].reshape(-1, 2, per).transpose(1, 0, 2).reshape(2, nplanes),
        ]
    ).astype(F32).reshape(-1)
    res = state0_step_call(pieces, scales, nf, per, coef, c_halo, c_first)
    s0, s0_halo, s1, s1_edges = res[0], res[1:5], res[5], res[6:10]
    s1_halo = exchange(*s1_edges)

    a1, *a1_edges = adjoint_call(
        s1, s1_halo, cotangent, c_halo, 0, coef, c_halo, c_first, True
    )
    a1_halo = exchange(*a1_edges)
    s2 = step_call(s1, s1_halo, coef, c_halo, c_first, False)

    sens = adjoint_call(s0, s0_halo, a1, a1_halo, 0, coef, c_halo, c_first, False)
    return (s2, sens)


def solution(mesh):
    placed = (
        P(None, None, "gx", "gy"),
        P(None, None, "gx", "gy"),
        P(),
        P("gx", "gy"),
        P(),
        P(None, None, "gx", "gy"),
    )
    return jax.shard_map(
        on_device,
        mesh=mesh,
        in_specs=placed,
        out_specs=(P(None, None, "gx", "gy"), P(None, None, "gx", "gy")),
        check_vma=False,
    )
```

```python
import jax
import jax.numpy as jnp
from jax import lax
from jax.experimental import pallas as pl
from jax.experimental.pallas import tpu as pltpu
from jax.sharding import PartitionSpec as P

F32 = jnp.float32
NCOEF = 4
UNROLL = 32
VMEM = pltpu.MemorySpace.VMEM
SMEM = pltpu.MemorySpace.SMEM


def _roll(v, shift, axis):
    shift = shift % v.shape[axis]
    if shift == 0:
        return v
    return pltpu.roll(v, shift, axis)


def _iotas(shape):
    return lax.broadcasted_iota(jnp.int32, shape, 0), lax.broadcasted_iota(jnp.int32, shape, 1)


def _pack_edges(vals, xf_ref, xl_ref, yf_ref, yl_ref):
    x, y = vals[0].shape
    _, lane = _iotas((x, y))
    xf_ref[...] = jnp.zeros(xf_ref.shape, F32)
    xl_ref[...] = jnp.zeros(xl_ref.shape, F32)
    yf = jnp.zeros((x, y), F32)
    yl = jnp.zeros((x, y), F32)
    for k, v in enumerate(vals):
        xf_ref[k : k + 1, :] = v[0:1, :]
        xl_ref[k : k + 1, :] = v[x - 1 : x, :]
        yf = jnp.where(lane == k, _roll(v, k, 1), yf)
        yl = jnp.where(lane == k, _roll(v, k - (y - 1), 1), yl)
    yf_ref[...] = yf
    yl_ref[...] = yl


def _expand_halo(xm_ref, xp_ref, ym_ref, yp_ref, first, nf, nz, dst):
    hxm, hxp, hym, hyp = dst
    x, y = hxm.shape[2], hxm.shape[3]
    ymv = ym_ref[...]
    ypv = yp_ref[...]
    for f in range(nf):
        for z in range(nz):
            k = first + f * nz + z
            hxm[f, z] = jnp.broadcast_to(xm_ref[k : k + 1, :], (x, y))
            hxp[f, z] = jnp.broadcast_to(xp_ref[k : k + 1, :], (x, y))
            hym[f, z] = _roll(ymv, -k, 1)
            hyp[f, z] = _roll(ypv, (y - 1) - k, 1)


def _coef_table(c_ref, cxm_ref, cxp_ref, cym_ref, cyp_ref, first, cs):
    x, y = c_ref.shape[1], c_ref.shape[2]
    ymv = cym_ref[...]
    ypv = cyp_ref[...]
    masks = _iotas((x, y))
    for k in range(NCOEF):
        r = first + k
        cv = c_ref[k]
        cs[k] = cv
        halo = (
            jnp.broadcast_to(cxm_ref[r : r + 1, :], (x, y)),
            jnp.broadcast_to(cxp_ref[r : r + 1, :], (x, y)),
            _roll(ymv, -r, 1),
            _roll(ypv, (y - 1) - r, 1),
        )
        for d, v in enumerate(_neighbours(cv, 0, [h[None] for h in halo], masks)):
            cs[4 + 4 * d + k] = v


def _neighbours(v, z, h, masks):
    row, lane = masks
    x, y = v.shape
    hxm, hxp, hym, hyp = h
    return (
        jnp.where(row == 0, hxm[z], _roll(v, 1, 0)),
        jnp.where(row == x - 1, hxp[z], _roll(v, x - 1, 0)),
        jnp.where(lane == 0, hym[z], _roll(v, 1, 1)),
        jnp.where(lane == y - 1, hyp[z], _roll(v, y - 1, 1)),
    )


def _field_at(ref, f, z, nz):
    zm = jnp.maximum(z - 1, 0)
    zp = jnp.minimum(z + 1, nz - 1)
    vm = jnp.where(z > 0, 1.0, 0.0).astype(F32)
    vp = jnp.where(z < nz - 1, 1.0, 0.0).astype(F32)
    return ref[f, z], ref[f, zm] * vm, ref[f, zp] * vp, vm, vp


def _gains(b):
    return 1.5 + b, 1.5 + 0.5 * b


def _step_body(s_ref, sh, cs, o_ref, nz, masks):
    def body(z, carry):
        u, u_m, u_p, vm, vp = _field_at(s_ref, 0, z, nz)
        t, t_m, t_p, _, _ = _field_at(s_ref, 1, z, nz)
        c = [cs[k] for k in range(NCOEF)]
        g1, g2 = _gains(jnp.tanh(u))
        kw, dtv, lamb, kv = c[0] * g1, c[1] * g2, c[2] * g2, c[3] * g1
        a1 = jnp.zeros_like(u)
        a2 = jnp.zeros_like(u)
        for un, tn, valid in ((u_m, t_m, vm), (u_p, t_p, vp)):
            g1n, g2n = _gains(jnp.tanh(un))
            a1 = a1 + (g1 + valid * g1n) * (un - u)
            a2 = a2 + (g2 + valid * g2n) * (tn - t)
        f0 = c[0] * a1 + c[1] * a2
        f1 = c[2] * a2 + c[3] * a1
        uns = _neighbours(u, z, sh[0], masks)
        tns = _neighbours(t, z, sh[1], masks)
        for d in range(4):
            un, tn = uns[d], tns[d]
            g1n, g2n = _gains(jnp.tanh(un))
            cn = [cs[4 + 4 * d + k] for k in range(NCOEF)]
            du = un - u
            dt = tn - t
            f0 = f0 + (kw + cn[0] * g1n) * du + (dtv + cn[1] * g2n) * dt
            f1 = f1 + (lamb + cn[2] * g2n) * dt + (kv + cn[3] * g1n) * du
        o_ref[0, z] = u + 0.5 * f0
        o_ref[1, z] = t + 0.5 * f1
        return carry

    lax.fori_loop(0, nz, body, 0, unroll=UNROLL)


def _adjoint_body(s_ref, sh, a_ref, ah, cs, o_ref, nz, masks):
    def body(z, carry):
        u, u_m, u_p, vm, vp = _field_at(s_ref, 0, z, nz)
        t, t_m, t_p, _, _ = _field_at(s_ref, 1, z, nz)
        a0, a0_m, a0_p, _, _ = _field_at(a_ref, 0, z, nz)
        a1, a1_m, a1_p, _, _ = _field_at(a_ref, 1, z, nz)
        c = [cs[k] for k in range(NCOEF)]
        b = jnp.tanh(u)
        g1, g2 = _gains(b)
        kw, dtv, lamb, kv = c[0] * g1, c[1] * g2, c[2] * g2, c[3] * g1
        zero = jnp.zeros_like(u)
        p10, p11, p20, p21 = zero, zero, zero, zero
        gu0, gu1, gt0, gt1 = zero, zero, zero, zero
        for un, tn, a0n, a1n, valid in ((u_m, t_m, a0_m, a1_m, vm), (u_p, t_p, a0_p, a1_p, vp)):
            g1n, g2n = _gains(jnp.tanh(un))
            s1 = g1 + valid * g1n
            s2 = g2 + valid * g2n
            du, dt, da0, da1 = un - u, tn - t, a0n - a0, a1n - a1
            p10 = p10 + s1 * da0
            p11 = p11 + s1 * da1
            p20 = p20 + s2 * da0
            p21 = p21 + s2 * da1
            gu0 = gu0 + du * da0
            gu1 = gu1 + du * da1
            gt0 = gt0 + dt * da0
            gt1 = gt1 + dt * da1
        ju = c[0] * p10 + c[3] * p11
        jt = c[1] * p20 + c[2] * p21
        uns = _neighbours(u, z, sh[0], masks)
        tns = _neighbours(t, z, sh[1], masks)
        a0ns = _neighbours(a0, z, ah[0], masks)
        a1ns = _neighbours(a1, z, ah[1], masks)
        for d in range(4):
            un, tn, a0n, a1n = uns[d], tns[d], a0ns[d], a1ns[d]
            g1n, g2n = _gains(jnp.tanh(un))
            cn = [cs[4 + 4 * d + k] for k in range(NCOEF)]
            du, dt, da0, da1 = un - u, tn - t, a0n - a0, a1n - a1
            ju = ju + (kw + cn[0] * g1n) * da0 + (kv + cn[3] * g1n) * da1
            jt = jt + (dtv + cn[1] * g2n) * da0 + (lamb + cn[2] * g2n) * da1
            gu0 = gu0 + du * da0
            gu1 = gu1 + du * da1
            gt0 = gt0 + dt * da0
            gt1 = gt1 + dt * da1
        gsum = c[0] * gu0 + c[3] * gu1 + 0.5 * (c[1] * gt0 + c[2] * gt1)
        o_ref[0, z] = a0 + 0.5 * ju - 0.5 * (1.0 - b * b) * gsum
        o_ref[1, z] = a1 + 0.5 * jt
        return carry

    lax.fori_loop(0, nz, body, 0, unroll=UNROLL)


def _halo_scratch(nf, nz, x, y):
    return [pltpu.VMEM((nf, nz, x, y), F32) for _ in range(4)]


def _edge_shapes(rows, x, y):
    return (
        jax.ShapeDtypeStruct((rows, y), F32),
        jax.ShapeDtypeStruct((rows, y), F32),
        jax.ShapeDtypeStruct((x, y), F32),
        jax.ShapeDtypeStruct((x, y), F32),
    )


def _rows(n):
    return -(-n // 8) * 8


def prep_call(soil_class, soil_table, cot, slab, scales):
    nf, nz, x, y = cot.shape
    nclass = soil_table.shape[0]
    table = soil_table.T
    nplanes = nf * nz

    def kernel(cls_ref, tab_ref, sc_ref, cot_ref, slab_ref, coef_ref, xf_ref, xl_ref, yf_ref, yl_ref):
        cls = cls_ref[...]
        coefs = []
        for k in range(NCOEF):
            cv = jnp.zeros(cls.shape, F32)
            for j in range(nclass):
                cv = jnp.where(cls == j, tab_ref[k, j], cv)
            coef_ref[k] = cv
            coefs.append(cv)
        vals = [cot_ref[f, z] for f in range(nf) for z in range(nz)] + coefs
        _pack_edges(vals, xf_ref, xl_ref, yf_ref, yl_ref)
        base = len(vals)
        for k in range(nplanes):
            v = slab_ref[k // nz, k % nz].astype(F32)
            xf_ref[base + k : base + k + 1, :] = v[0:1, :]
            xl_ref[base + k : base + k + 1, :] = v[x - 1 : x, :]
        _, lane = _iotas((1, y))
        row = jnp.zeros((1, y), F32)
        scv = sc_ref[...].astype(F32)
        for k in range(nplanes):
            v = jnp.broadcast_to(scv[k // nz : k // nz + 1, k % nz : k % nz + 1], (1, y))
            row = jnp.where(lane == k, v, row)
        xf_ref[base + nplanes : base + nplanes + 1, :] = row
        xl_ref[base + nplanes : base + nplanes + 1, :] = row

    rows = _rows(2 * nplanes + NCOEF + 1)
    return pl.pallas_call(
        kernel,
        out_shape=(jax.ShapeDtypeStruct((NCOEF, x, y), F32),)
        + _edge_shapes(rows, x, y)[:2]
        + _edge_shapes(8, x, y)[2:],
        in_specs=[
            pl.BlockSpec(memory_space=VMEM),
            pl.BlockSpec(memory_space=SMEM),
            pl.BlockSpec(memory_space=VMEM),
            pl.BlockSpec(memory_space=VMEM),
            pl.BlockSpec(memory_space=VMEM),
        ],
    )(soil_class, table, scales, cot, slab)


def _state0_body(sc_ref, r_ref, s_ref, xm_ref, xp_ref, ym_ref, yp_ref, per):
    nz, x, y = s_ref.shape[1], s_ref.shape[2], s_ref.shape[3]
    nplanes = s_ref.shape[0] * nz
    _, lane = _iotas((x, y))
    ym = jnp.zeros((x, y), F32)
    yp = jnp.zeros((x, y), F32)
    for k in range(nplanes):
        p, i = k // per, k % per
        sp = r_ref[p, per + 1].astype(F32)
        sq = r_ref[p, per + 3].astype(F32)
        own = jnp.broadcast_to(sp[0:1, i : i + 1], (x, y))
        s_ref[k // nz, k % nz] = r_ref[p, i].astype(F32) * own
        hx = r_ref[p, per].astype(F32)
        xm_ref[k : k + 1, :] = hx[i : i + 1, :] * jnp.broadcast_to(sp[1:2, i : i + 1], (1, y))
        xp_ref[k : k + 1, :] = hx[per + i : per + i + 1, :] * jnp.broadcast_to(sp[2:3, i : i + 1], (1, y))
        hy = r_ref[p, per + 2].astype(F32)
        sm = jnp.broadcast_to(sq[0:1, i : i + 1], (x, y))
        spp = jnp.broadcast_to(sq[0:1, per + i : per + i + 1], (x, y))
        ym = jnp.where(lane == k, _roll(hy, k - i, 1) * sm, ym)
        yp = jnp.where(lane == k, _roll(hy, k - (per + i), 1) * spp, yp)
    ym_ref[...] = ym
    yp_ref[...] = yp


def state0_step_call(pieces, scales, nf, per, coef, c_halo, c_first):
    npiece, _, x, y = pieces.shape
    nplanes = npiece * per
    nz = nplanes // nf

    def kernel(r_ref, c_ref, cxm, cxp, cym, cyp, *refs):
        s0_ref, xm_ref, xp_ref, ym_ref, yp_ref = refs[:5]
        s1_ref, xf_ref, xl_ref, yf_ref, yl_ref = refs[5:10]
        scratch = refs[10:]
        sh_all = scratch[0:4]
        cs = scratch[4]
        _state0_body(None, r_ref, s0_ref, xm_ref, xp_ref, ym_ref, yp_ref, per)
        _expand_halo(xm_ref, xp_ref, ym_ref, yp_ref, 0, nf, nz, sh_all)
        _coef_table(c_ref, cxm, cxp, cym, cyp, c_first, cs)
        masks = _iotas((x, y))
        sh = [tuple(h.at[f] for h in sh_all) for f in range(nf)]
        _step_body(s0_ref, sh, cs, s1_ref, nz, masks)
        vals = [s1_ref[f, z] for f in range(nf) for z in range(nz)]
        _pack_edges(vals, xf_ref, xl_ref, yf_ref, yl_ref)

    state = jax.ShapeDtypeStruct((nf, nz, x, y), F32)
    return pl.pallas_call(
        kernel,
        out_shape=(state,) + _edge_shapes(nplanes, x, y) + (state,) + _edge_shapes(_rows(nplanes), x, y),
        in_specs=[pl.BlockSpec(memory_space=VMEM)] * 6,
        scratch_shapes=_halo_scratch(nf, nz, x, y) + [pltpu.VMEM((5 * NCOEF, x, y), F32)],
    )(pieces, coef, *c_halo)


def step_call(s, s_halo, coef, c_halo, c_first, with_edges):
    nf, nz, x, y = s.shape

    def kernel(*refs):
        s_ref, sxm, sxp, sym, syp, c_ref, cxm, cxp, cym, cyp = refs[:10]
        rest = refs[10:]
        if with_edges:
            o_ref, xf_ref, xl_ref, yf_ref, yl_ref = rest[:5]
            scratch = rest[5:]
        else:
            o_ref = rest[0]
            scratch = rest[1:]
        sh_all = scratch[0:4]
        cs = scratch[4]
        _expand_halo(sxm, sxp, sym, syp, 0, nf, nz, sh_all)
        _coef_table(c_ref, cxm, cxp, cym, cyp, c_first, cs)
        masks = _iotas((x, y))
        sh = [tuple(h.at[f] for h in sh_all) for f in range(nf)]
        _step_body(s_ref, sh, cs, o_ref, nz, masks)
        if with_edges:
            vals = [o_ref[f, z] for f in range(nf) for z in range(nz)]
            _pack_edges(vals, xf_ref, xl_ref, yf_ref, yl_ref)

    out_shape = (jax.ShapeDtypeStruct(s.shape, F32),)
    if with_edges:
        out_shape = out_shape + _edge_shapes(_rows(nf * nz), x, y)
    res = pl.pallas_call(
        kernel,
        out_shape=out_shape,
        scratch_shapes=_halo_scratch(nf, nz, x, y) + [pltpu.VMEM((5 * NCOEF, x, y), F32)],
    )(s, *s_halo, coef, *c_halo)
    return res if with_edges else res[0]


def adjoint_call(s, s_halo, a, a_halo, a_first, coef, c_halo, c_first, with_edges):
    nf, nz, x, y = s.shape

    def kernel(*refs):
        s_ref, sxm, sxp, sym, syp, a_ref, axm, axp, aym, ayp, c_ref, cxm, cxp, cym, cyp = refs[:15]
        rest = refs[15:]
        if with_edges:
            o_ref, xf_ref, xl_ref, yf_ref, yl_ref = rest[:5]
            scratch = rest[5:]
        else:
            o_ref = rest[0]
            scratch = rest[1:]
        sh_all = scratch[0:4]
        ah_all = scratch[4:8]
        cs = scratch[8]
        _expand_halo(sxm, sxp, sym, syp, 0, nf, nz, sh_all)
        _expand_halo(axm, axp, aym, ayp, a_first, nf, nz, ah_all)
        _coef_table(c_ref, cxm, cxp, cym, cyp, c_first, cs)
        masks = _iotas((x, y))
        sh = [tuple(h.at[f] for h in sh_all) for f in range(nf)]
        ah = [tuple(h.at[f] for h in ah_all) for f in range(nf)]
        _adjoint_body(s_ref, sh, a_ref, ah, cs, o_ref, nz, masks)
        if with_edges:
            vals = [o_ref[f, z] for f in range(nf) for z in range(nz)]
            _pack_edges(vals, xf_ref, xl_ref, yf_ref, yl_ref)

    out_shape = (jax.ShapeDtypeStruct(s.shape, F32),)
    if with_edges:
        out_shape = out_shape + _edge_shapes(_rows(nf * nz), x, y)
    res = pl.pallas_call(
        kernel,
        out_shape=out_shape,
        scratch_shapes=_halo_scratch(nf, nz, x, y)
        + _halo_scratch(nf, nz, x, y)
        + [pltpu.VMEM((5 * NCOEF, x, y), F32)],
    )(s, *s_halo, a, *a_halo, coef, *c_halo)
    return res if with_edges else res[0]


def _shift(v, axis, step):
    n = lax.axis_size(axis)
    if step > 0:
        pairs = [(i, i + 1) for i in range(n - 1)]
    else:
        pairs = [(i + 1, i) for i in range(n - 1)]
    return lax.ppermute(v, axis, pairs)


def exchange(xf, xl, yf, yl):
    return (
        _shift(xl, "gx", 1),
        _shift(xf, "gx", -1),
        _shift(yl, "gy", 1),
        _shift(yf, "gy", -1),
    )


def forward_call(holder, held, per):
    n, planes, x, y = held.shape

    def kernel(hold_ref, h_ref, o_ref):
        _, lane = _iotas((x, y))
        for g in range(n):
            h = hold_ref[g]
            for i in range(planes):
                o_ref[g, i] = h_ref[h, i]
            cols = jnp.zeros((x, y), F32)
            scl = jnp.zeros((x, y), F32)
            if g > 0:
                hl = hold_ref[g - 1]
                for i in range(per):
                    v = h_ref[hl, i].astype(F32)
                    cols = jnp.where(lane == i, _roll(v, i - (y - 1), 1), cols)
                scl = jnp.where(lane < per, h_ref[hl, per + 1].astype(F32), scl)
            if g < n - 1:
                hr = hold_ref[g + 1]
                for i in range(per):
                    v = h_ref[hr, i].astype(F32)
                    cols = jnp.where(lane == per + i, _roll(v, per + i, 1), cols)
                sv = _roll(h_ref[hr, per + 1].astype(F32), per, 1)
                scl = jnp.where((lane >= per) & (lane < 2 * per), sv, scl)
            o_ref[g, planes] = cols.astype(o_ref.dtype)
            o_ref[g, planes + 1] = scl.astype(o_ref.dtype)

    return pl.pallas_call(
        kernel,
        out_shape=jax.ShapeDtypeStruct((n, planes + 2, x, y), held.dtype),
        in_specs=[pl.BlockSpec(memory_space=SMEM), pl.BlockSpec(memory_space=VMEM)],
    )(holder, held)


def route_blocks(stored_slab, block_scales, holder, xm_all, xp_all, first):
    nf, nz, x, y = stored_slab.shape
    n = lax.axis_size("gy")
    nplanes = nf * nz
    per = nplanes // n
    bf = stored_slab.dtype
    slab = stored_slab.reshape(n, per, x, y)
    rows_m = xm_all[first : first + nplanes].astype(bf).reshape(n, per, y)
    rows_p = xp_all[first : first + nplanes].astype(bf).reshape(n, per, y)
    halo = jnp.concatenate([rows_m, rows_p], axis=1)[:, None]
    sc_m = xm_all[first + nplanes, :nplanes].astype(bf).reshape(n, 1, per)
    sc_p = xp_all[first + nplanes, :nplanes].astype(bf).reshape(n, 1, per)
    sc = jnp.concatenate([block_scales.reshape(n, 1, per), sc_m, sc_p], axis=1)
    sc = jnp.pad(sc, ((0, 0), (0, x - 3), (0, y - per)))[:, None]
    held = lax.all_to_all(jnp.concatenate([slab, halo, sc], axis=1), "gy", 0, 0, tiled=True)

    forward = forward_call(holder, held, per)
    return lax.all_to_all(forward, "gy", 0, 0, tiled=True)


def on_device(stored_slab, block_scales, holder, soil_class, soil_table, cotangent):
    nf, nz, x, y = stored_slab.shape
    nplanes = nf * nz

    coef, cxf, cxl, cyf, cyl = prep_call(
        soil_class, soil_table, cotangent, stored_slab, block_scales.reshape(nf, nz)
    )
    c_halo = exchange(cxf, cxl, cyf, cyl)
    c_first = nplanes

    pieces = route_blocks(stored_slab, block_scales, holder, c_halo[0], c_halo[1], nplanes + NCOEF)
    per = nplanes // pieces.shape[0]
    scales = jnp.concatenate(
        [
            pieces[:, per + 1, 0:3, :per].transpose(1, 0, 2).reshape(3, nplanes),
            pieces[:, per + 3, 0, : 2 * per].reshape(-1, 2, per).transpose(1, 0, 2).reshape(2, nplanes),
        ]
    ).astype(F32).reshape(-1)
    res = state0_step_call(pieces, scales, nf, per, coef, c_halo, c_first)
    s0, s0_halo, s1, s1_edges = res[0], res[1:5], res[5], res[6:10]
    s1_halo = exchange(*s1_edges)

    a1, *a1_edges = adjoint_call(
        s1, s1_halo, cotangent, c_halo, 0, coef, c_halo, c_first, True
    )
    a1_halo = exchange(*a1_edges)
    s2 = step_call(s1, s1_halo, coef, c_halo, c_first, False)

    sens = adjoint_call(s0, s0_halo, a1, a1_halo, 0, coef, c_halo, c_first, False)
    return (s2, sens)


def solution(mesh):
    placed = (
        P(None, None, "gx", "gy"),
        P(None, None, "gx", "gy"),
        P(),
        P("gx", "gy"),
        P(),
        P(None, None, "gx", "gy"),
    )
    return jax.shard_map(
        on_device,
        mesh=mesh,
        in_specs=placed,
        out_specs=(P(None, None, "gx", "gy"), P(None, None, "gx", "gy")),
        check_vma=False,
    )
```
